256 devices in a mesh: req: 16 (over z, core), head: 16 (over x, y).
Axes of the slice: x: 4, y: 4, z: 8, core: 2. Of those that a mesh axis runs over, the one named last changes fastest.
Arguments:
- tree_heads: bfloat16 [4096, 16384], P(('req', 'head')), may hold values from -6 to 6
- tree_gates: bfloat16 [4096, 16384], P(('req', 'head')), may hold values from -6 to 6
- tree_steps: bfloat16 [4096, 256], P(('req', 'head')), may hold values from -6 to 6
- tree_groups: bfloat16 [4096, 4096], P(('req', 'head')), may hold values from -6 to 6
- new_tree: int32 [128, 32, 32], P('req'), may hold values from 0 to 1, as said below
- kernel_heads: bfloat16 [4, 16384], P(None, 'head'), may hold values from -3 to 3
- shift_heads: float32 [16384], P('head'), may hold values from -3 to 3
- kernel_groups: bfloat16 [4, 4096], replicated, may hold values from -3 to 3
- shift_groups: float32 [4096], replicated, may hold values from -3 to 3
- log_rates: float32 [256], P('head'), may hold values from 0 to 2.77
- step_bias: float32 [256], P('head'), may hold values from -6 to -2
- skip_gain: float32 [256], P('head'), may hold values from 0.5 to 1.5
- norm_gain: float32 [16384], P('head'), may hold values from 0.5 to 1.5
- old_state: bfloat16 [128, 256, 64, 256], P('req', 'head'), may hold values from -0.59765625 to 0.59765625
- old_heads: bfloat16 [128, 32, 16384], P('req', None, 'head'), may hold values from -3 to 3
- old_keys: bfloat16 [128, 32, 2048], P('req'), may hold values from -3 to 3
- old_steps: float32 [128, 32, 256], P('req', None, 'head'), may hold values from 0.002 to 0.2
- prior_heads: bfloat16 [128, 32, 16384], P('req', None, 'head'), may hold values from -6 to 6
- prior_groups: bfloat16 [128, 32, 4096], P('req', 'head'), may hold values from -6 to 6
- old_tree: int32 [128, 32, 32], P('req'), may hold values from 0 to 1, as said below
- accepted: int32 [128], P('req'), may hold values from 2 to 31, as said below
- new_owner: int32 [128], replicated, may hold values from 0 to 127, as said below
Outputs:
- mixed: bfloat16 [4096, 16384], P('req', 'head')
The draws below stay inside these ranges and needn't reach their ends.
Inputs may be any that keep to these rules, and one draw needn't show every extreme that they name: `old_tree`: entry (t, j) is 1 when node j is node t or one of its ancestors, else 0; node 0 is the root, every parent has a lower number than its child, node 1 is the child of node 0 and node 2 the child of node 1, and every node numbered 2 or more has depth two or more. `new_tree`: ancestor masks of the same kind as old_tree. The accepted node has depth two or more in old_tree. A permutation of the slots. Slot i lives on device i // 8 of req before and on device new_owner[i] // 8 after; no old device hands more than 2 requests to one new device, and in every draw some pairs of devices carry exactly 2.
All inputs are finite; a program needn't handle non-finite values.
Results may differ from the reference program's by a relative error of at most 0.0052.
Values may be sent and summed in bfloat16 or wider, within the bound.
No kernel may reach another device: no remote copies, remote signals or barrier semaphores. Data moves between devices by JAX's collectives and lax.ppermute only.
A program may use at most 128 MiB of HBM per device.

```python
import math
import jax
import jax.numpy as jnp
from jax import lax

HEADS = 256
HEAD_DIM = 64
STATE = 256
GROUPS = 8
NODES = 32
R_DEV = 8
REQS = 128
DINNER = 16384


def tree_ancestry(key, count):

    def one_tree(subkey):
        node_ids = jnp.arange(NODES, dtype=jnp.int32)
        backward = jax.random.randint(subkey, (NODES,), 0, 3, dtype=jnp.int32)
        reach_back = jnp.maximum(jnp.minimum(node_ids - 1, 3), 1)
        parents = node_ids - 1 - jnp.where(node_ids >= 3, backward % reach_back, 0)
        identity_rows = (node_ids[:, None] == node_ids[None, :]).astype(jnp.int32)

        def grow(node_at, lineage):
            above_row = lineage[jnp.maximum(parents[node_at], 0)]
            row_now = identity_rows[node_at] + jnp.where(node_at > 0, above_row, 0)
            return lineage.at[node_at].set(row_now)
        return lax.fori_loop(0, NODES, grow, jnp.zeros((NODES, NODES), jnp.int32))
    return jax.vmap(one_tree)(jax.random.split(key, count))


def draw_new_tree(key, part):
    return tree_ancestry(jax.random.fold_in(key, 23), REQS)


def draw_old_tree(key, part):
    return tree_ancestry(jax.random.fold_in(key, 11), REQS)


def draw_accepted(key, part):
    return jax.random.randint(jax.random.fold_in(key, 5), (REQS,), 2, NODES, dtype=jnp.int32)


def draw_new_owner(key, part):
    group_count = REQS // R_DEV
    keys_four = jax.random.split(jax.random.fold_in(key, 37), 4)
    shuffle_dev = jax.random.permutation(keys_four[0], group_count).astype(jnp.int32)
    shift_dev = jax.random.permutation(keys_four[1], group_count).astype(jnp.int32)
    offset_pool = jax.random.permutation(keys_four[2], group_count).astype(jnp.int32)
    offsets = offset_pool[jnp.arange(R_DEV, dtype=jnp.int32) // 2 % group_count]
    local_order = jax.vmap(lambda subkey: jax.random.permutation(subkey, R_DEV).astype(jnp.int32))(jax.random.split(keys_four[3], group_count))
    target_dev = shuffle_dev[(shift_dev[:, None] + offsets[local_order]) % group_count]
    return (target_dev * R_DEV + local_order).reshape(-1).astype(jnp.int32)


def level_of(own_key, extent, pieces, least, high):
    gain = 1.0
    for dim, blocks in pieces:
        steps = jax.random.uniform(jax.random.fold_in(jax.random.fold_in(own_key, 6), dim), (blocks,), jnp.float32, least / len(pieces), high / len(pieces))
        gain = gain * jnp.repeat(jnp.exp(steps), extent[dim] // blocks).reshape((-1,) + (1,) * (len(extent) - 1 - dim))
    return gain


def bell_draw(stream_key, extent, deviation, bound, cuts=(), kind=jnp.bfloat16):
    array = deviation * jax.random.normal(stream_key, extent, jnp.float32)
    if cuts:
        array = array * level_of(stream_key, extent, cuts, -0.22, 0.18)
    return jnp.clip(array, -bound, bound).astype(kind)


def setup_inputs(seed: int = 0) -> dict:
    key_list = jax.random.split(jax.random.key(seed), 23)
    return {
        "tree_heads": bell_draw(key_list[0], (REQS * NODES, DINNER), 1.0, 6.0, ((0, 256),)),
        "tree_gates": bell_draw(key_list[1], (REQS * NODES, DINNER), 1.0, 6.0, ((0, 256),)),
        "tree_steps": bell_draw(key_list[2], (REQS * NODES, HEADS), 1.0, 6.0, ((0, 256),)),
        "tree_groups": bell_draw(key_list[3], (REQS * NODES, 2 * GROUPS * STATE), 1.0, 6.0, ((0, 256),)),
        "new_tree": draw_new_tree(jax.random.fold_in(key_list[22], 71), 0),
        "kernel_heads": bell_draw(key_list[5], (4, DINNER), 4 ** -0.5, 3.0, ((1, 16),)),
        "shift_heads": bell_draw(key_list[6], (DINNER,), 0.5, 3.0, ((0, 16),), jnp.float32),
        "kernel_groups": bell_draw(key_list[7], (4, 2 * GROUPS * STATE), 4 ** -0.5, 3.0),
        "shift_groups": bell_draw(key_list[8], (2 * GROUPS * STATE,), 0.5, 3.0, (), jnp.float32),
        "log_rates": jnp.clip(2.77 * jax.random.uniform(key_list[9], (HEADS,), jnp.float32) ** level_of(key_list[9], (HEADS,), ((0, 16),), -0.2, 0.2), 0.0, 2.77),
        "step_bias": jnp.clip(-6.0 + 4.0 * jax.random.uniform(key_list[10], (HEADS,), jnp.float32) ** level_of(key_list[10], (HEADS,), ((0, 16),), -0.2, 0.2), -6.0, -2.0),
        "skip_gain": jnp.clip(0.5 + 1.0 * jax.random.uniform(key_list[11], (HEADS,), jnp.float32) ** level_of(key_list[11], (HEADS,), ((0, 16),), -0.2, 0.2), 0.5, 1.5),
        "norm_gain": jnp.clip(1.0 + 0.1 * jax.random.normal(key_list[12], (DINNER,), jnp.float32), 0.5, 1.5),
        "old_state": bell_draw(key_list[13], (REQS, HEADS, HEAD_DIM, STATE), 0.1, 0.59765625, ((0, 16), (1, 16))),
        "old_heads": bell_draw(key_list[14], (REQS, NODES, DINNER), 0.5, 3.0, ((0, 16), (2, 16))),
        "old_keys": bell_draw(key_list[15], (REQS, NODES, GROUPS * STATE), 0.5, 3.0, ((0, 16),)),
        "old_steps": jnp.clip(jnp.exp(math.log(0.2) - 4.6051702 * jax.random.uniform(key_list[16], (REQS, NODES, HEADS), jnp.float32) ** level_of(key_list[16], (REQS, NODES, HEADS), ((0, 16), (2, 16)), -0.2, 0.2)), 0.002, 0.2),
        "prior_heads": bell_draw(key_list[17], (REQS, NODES, DINNER), 1.0, 6.0, ((0, 16), (2, 16))),
        "prior_groups": bell_draw(key_list[18], (REQS, NODES, 2 * GROUPS * STATE), 1.0, 6.0, ((0, 16), (1, 16))),
        "old_tree": draw_old_tree(jax.random.fold_in(key_list[22], 71), 0),
        "accepted": draw_accepted(jax.random.fold_in(key_list[22], 71), 0),
        "new_owner": draw_new_owner(jax.random.fold_in(key_list[22], 71), 0),
    }


EPSILON = 1e-05

def tree_conv(tree_rows, tail_rows, ancestry, weight, offset_bias):
    node_depth = lax.optimization_barrier(jnp.sum(ancestry, axis=-1)) - 1
    places = jnp.arange(3, dtype=jnp.int32)
    summed = weight[3].astype(jnp.float32) * tree_rows.astype(jnp.float32) + offset_bias
    for upward in range(1, 4):
        picked = jnp.where((ancestry == 1) & (node_depth[None, :] == node_depth[:, None] - upward), 1.0, 0.0).astype(jnp.float32)
        older_rows = jnp.where(places[None, :] == node_depth[:, None] - upward + 3, 1.0, 0.0).astype(jnp.float32)
        shifted = jnp.dot(picked, tree_rows.astype(jnp.float32), preferred_element_type=jnp.float32)
        shifted = shifted + jnp.dot(older_rows, tail_rows.astype(jnp.float32), preferred_element_type=jnp.float32)
        summed = summed + weight[3 - upward].astype(jnp.float32) * shifted
    return jax.nn.silu(summed).astype(jnp.bfloat16)

def reference(tree_heads, tree_gates, tree_steps, tree_groups, new_tree, kernel_heads, shift_heads, kernel_groups, shift_groups, log_rates, step_bias, skip_gain, norm_gain, old_state, old_heads, old_keys, old_steps, prior_heads, prior_groups, old_tree, accepted, new_owner):
    new_slots = jnp.arange(REQS, dtype=jnp.int32)
    source = jnp.zeros((REQS,), jnp.int32).at[new_owner].set(new_slots)
    decay_rates = -jnp.exp(log_rates)
    per_group = HEADS // GROUPS
    key_width = GROUPS * STATE
    places = jnp.arange(3, dtype=jnp.int32)
    highest = lax.Precision.HIGHEST

    def one_request(request):
        anchor = source[request]
        prior_tree = old_tree[anchor]
        chosen = accepted[anchor]
        old_depth = lax.optimization_barrier(jnp.sum(prior_tree, axis=-1)) - 1
        lineage = prior_tree[chosen] == 1
        chosen_depth = old_depth[chosen]
        tail_pick = jnp.where(lineage[None, :] & (old_depth[None, :] == chosen_depth - 2 + places[:, None]), 1.0, 0.0).astype(jnp.float32)
        tail_heads = jnp.dot(tail_pick, prior_heads[anchor].astype(jnp.float32), preferred_element_type=jnp.float32).astype(jnp.bfloat16)
        tail_groups = jnp.dot(tail_pick, prior_groups[anchor].astype(jnp.float32), preferred_element_type=jnp.float32).astype(jnp.bfloat16)
        prior_steps = old_steps[anchor]
        old_sums = jnp.dot(prior_tree.astype(jnp.float32), prior_steps * decay_rates[None, :], precision=highest)
        chosen_sum = old_sums[chosen]
        kept_weight = jnp.where(lineage[:, None], jnp.exp(jnp.where(lineage[:, None], chosen_sum[None, :] - old_sums, 0.0)), 0.0) * prior_steps
        weighted = (kept_weight[:, :, None] * old_heads[anchor].reshape(NODES, HEADS, HEAD_DIM).astype(jnp.float32)).astype(jnp.bfloat16).reshape(NODES, GROUPS, per_group, HEAD_DIM)
        key_rows = old_keys[anchor].reshape(NODES, GROUPS, STATE).astype(jnp.float32)
        update = jnp.einsum('jgqp,jgn->gqpn', weighted.astype(jnp.float32), key_rows, precision=highest)
        carry_state = (jnp.exp(chosen_sum).reshape(GROUPS, per_group, 1, 1) * old_state[anchor].reshape(GROUPS, per_group, HEAD_DIM, STATE).astype(jnp.float32) + update).astype(jnp.bfloat16)
        row_start = request * NODES
        head_rows = lax.dynamic_slice_in_dim(tree_heads, row_start, NODES, 0)
        gate_rows = lax.dynamic_slice_in_dim(tree_gates, row_start, NODES, 0)
        step_rows = lax.dynamic_slice_in_dim(tree_steps, row_start, NODES, 0)
        group_rows = lax.dynamic_slice_in_dim(tree_groups, row_start, NODES, 0)
        current_tree = new_tree[request]
        conv_heads = tree_conv(head_rows, tail_heads, current_tree, kernel_heads, shift_heads)
        conv_groups = tree_conv(group_rows, tail_groups, current_tree, kernel_groups, shift_groups)
        key_cols = conv_groups[:, :key_width].reshape(NODES, GROUPS, STATE).astype(jnp.float32)
        queries = conv_groups[:, key_width:].reshape(NODES, GROUPS, STATE).astype(jnp.float32)
        step_sizes = jax.nn.softplus(step_rows.astype(jnp.float32) + step_bias[None, :])
        decay_sum = jnp.dot(current_tree.astype(jnp.float32), step_sizes * decay_rates[None, :], precision=highest)
        intersection = jnp.einsum('tgn,jgn->tjg', queries, key_cols)
        lineage_new = (current_tree == 1)[:, :, None]
        decay_gap = decay_sum[:, None, :] - decay_sum[None, :, :]
        decays = jnp.where(lineage_new, jnp.exp(jnp.where(lineage_new, decay_gap, 0.0)), 0.0)
        mixing = (decays.reshape(NODES, NODES, GROUPS, per_group) * intersection[:, :, :, None] * step_sizes.reshape(1, NODES, GROUPS, per_group)).astype(jnp.bfloat16)
        values = conv_heads.reshape(NODES, GROUPS, per_group, HEAD_DIM).astype(jnp.float32)
        inner_part = jnp.einsum('tjgq,jgqp->tgqp', mixing.astype(jnp.float32), values)
        carried = jnp.einsum('tgn,gqpn->tgqp', queries, carry_state.astype(jnp.float32))
        output = inner_part + jnp.exp(decay_sum).reshape(NODES, GROUPS, per_group, 1) * carried + skip_gain.reshape(1, GROUPS, per_group, 1) * values
        gated_out = output * jax.nn.silu(gate_rows.astype(jnp.float32)).reshape(NODES, GROUPS, per_group, HEAD_DIM)
        group_power = lax.optimization_barrier(jnp.sum(gated_out * gated_out, axis=(2, 3)))
        scale_factor = lax.rsqrt(group_power / (per_group * HEAD_DIM) + EPSILON)
        normed = gated_out * scale_factor[:, :, None, None] * norm_gain.reshape(1, GROUPS, per_group, HEAD_DIM)
        return normed.reshape(NODES, HEADS * HEAD_DIM).astype(jnp.bfloat16)
    all_mixed = lax.map(one_request, new_slots)
    return all_mixed.reshape(REQS * NODES, HEADS * HEAD_DIM)
```

```python
import jax
import jax.numpy as jnp
from jax import lax
from jax.sharding import PartitionSpec as P

HEADS = 256
HEAD_DIM = 64
STATE = 256
GROUPS = 8
NODES = 32
MOST = 2


EPSILON = 1e-05


def tree_conv(tree_rows, tail_rows, ancestry, weight, offset_bias):
    node_depth = jnp.sum(ancestry, axis=-1) - 1
    places = jnp.arange(3, dtype=jnp.int32)
    summed = weight[3].astype(jnp.float32) * tree_rows.astype(jnp.float32) + offset_bias
    for upward in range(1, 4):
        picked = (
            (ancestry == 1) & (node_depth[:, None, :] == node_depth[:, :, None] - upward)
        ).astype(jnp.bfloat16)
        older_rows = (places[None, None, :] == node_depth[:, :, None] - upward + 3).astype(
            jnp.bfloat16
        )
        shifted = jnp.einsum("btj,bjc->btc", picked, tree_rows, preferred_element_type=jnp.float32)
        shifted = shifted + jnp.einsum(
            "bti,bic->btc", older_rows, tail_rows, preferred_element_type=jnp.float32
        )
        summed = summed + weight[3 - upward].astype(jnp.float32) * shifted
    return jax.nn.silu(summed).astype(jnp.bfloat16)


def place_slots(payload, positions, count):
    wanted = jnp.arange(count, dtype=jnp.int32)
    owners = jnp.arange(positions.shape[0], dtype=jnp.int32)
    hits = positions[None, :] == wanted[:, None]
    chosen = jnp.sum(jnp.where(hits, owners[None, :], 0), axis=1)
    filled = jnp.any(hits, axis=1).reshape((count,) + (1,) * (payload.ndim - 1))
    taken = jnp.take(payload, chosen, axis=0)
    return jnp.where(filled, taken, jnp.zeros_like(taken))


def own_columns(rows, span_groups, dest_count, per_dest):
    lead = rows.shape[:-1]
    split = rows.reshape(lead + (2, GROUPS, STATE))
    moved = jnp.moveaxis(split, -2, 0)
    picks = (jnp.arange(dest_count, dtype=jnp.int32) // per_dest)[:, None] * span_groups + jnp.arange(
        span_groups, dtype=jnp.int32
    )[None, :]
    taken = jnp.take(moved, picks.reshape(-1), axis=0).reshape((dest_count, span_groups) + lead + (2, STATE))
    return jnp.moveaxis(taken, 1, -2).reshape((dest_count,) + lead + (2 * span_groups * STATE,))


def shards(
    tree_heads,
    tree_gates,
    tree_steps,
    tree_groups,
    new_tree,
    kernel_heads,
    shift_heads,
    kernel_groups,
    shift_groups,
    log_rates,
    step_bias,
    skip_gain,
    norm_gain,
    old_state,
    old_heads,
    old_keys,
    old_steps,
    prior_heads,
    prior_groups,
    old_tree,
    accepted,
    new_owner,
):
    req_count = lax.axis_size("req")
    head_count = lax.axis_size("head")
    req_index = lax.axis_index("req")
    head_index = lax.axis_index("head")
    reqs_dev = new_tree.shape[0]
    local_heads = log_rates.shape[0]
    local_nodes = prior_groups.shape[1]
    per_group = HEADS // GROUPS
    span_heads = min(local_heads, per_group)
    span_groups = local_heads // span_heads
    per_dest = per_group // span_heads
    first_group = head_index * local_heads // per_group
    slot_count = req_count * MOST
    own_width = span_groups * STATE
    highest = lax.Precision.HIGHEST
    owner_table = new_owner.reshape(req_count, reqs_dev)
    target_dev = owner_table // reqs_dev
    local_ids = jnp.arange(reqs_dev, dtype=jnp.int32)
    before = local_ids[None, :, None] > local_ids[None, None, :]
    same_dest = target_dev[:, :, None] == target_dev[:, None, :]
    arrival = jnp.sum((same_dest & before).astype(jnp.int32), axis=-1)
    send_table = target_dev * MOST + arrival
    send_pos = lax.dynamic_index_in_dim(send_table, req_index, 0, keepdims=False)
    wanted_slot = req_index * reqs_dev + local_ids
    all_ids = jnp.arange(new_owner.shape[0], dtype=jnp.int32)
    match = new_owner[None, :] == wanted_slot[:, None]
    anchor = jnp.sum(jnp.where(match, all_ids[None, :], 0), axis=1)
    recv_pos = anchor // reqs_dev * MOST + jnp.take(arrival.reshape(-1), anchor)

    def to_new(payload):
        placed = place_slots(payload, send_pos, slot_count)
        moved = lax.all_to_all(placed, "req", split_axis=0, concat_axis=0, tiled=True)
        return jnp.take(moved, recv_pos, axis=0)

    def to_old(payload):
        placed = place_slots(payload, recv_pos, slot_count)
        moved = lax.all_to_all(placed, "req", split_axis=0, concat_axis=0, tiled=True)
        return jnp.take(moved, send_pos, axis=0)

    decay_rates = -jnp.exp(log_rates)
    node_ids = jnp.arange(NODES, dtype=jnp.int32)
    chosen_hot = node_ids[None, :] == accepted[:, None]
    chosen_row = jnp.sum(jnp.where(chosen_hot[:, :, None], old_tree, 0), axis=1)
    old_depth = jnp.sum(old_tree, axis=-1) - 1
    chosen_depth = jnp.sum(jnp.where(chosen_hot, old_depth, 0), axis=1)
    places = jnp.arange(3, dtype=jnp.int32)
    lineage = chosen_row == 1
    tail_pick = (
        lineage[:, None, :]
        & (old_depth[:, None, :] == chosen_depth[:, None, None] - 2 + places[None, :, None])
    ).astype(jnp.bfloat16)
    tail_heads = jnp.einsum(
        "bij,bjc->bic", tail_pick, prior_heads, preferred_element_type=jnp.float32
    ).astype(jnp.bfloat16)
    prior_own = lax.all_to_all(
        own_columns(prior_groups, span_groups, head_count, per_dest),
        "head",
        split_axis=0,
        concat_axis=0,
        tiled=True,
    )
    prior_own = jnp.moveaxis(
        prior_own.reshape(head_count, reqs_dev, local_nodes, 2 * own_width), 0, 1
    ).reshape(reqs_dev, NODES, 2 * own_width)
    tail_groups = jnp.einsum(
        "bij,bjc->bic", tail_pick, prior_own, preferred_element_type=jnp.float32
    ).astype(jnp.bfloat16)
    old_sums = jnp.einsum(
        "btj,bjh->bth", old_tree.astype(jnp.float32), old_steps * decay_rates, precision=highest
    )
    chosen_sum = jnp.sum(jnp.where(chosen_hot[:, :, None], old_sums, 0.0), axis=1)
    kept_weight = (
        jnp.where(
            lineage[:, :, None],
            jnp.exp(jnp.where(lineage[:, :, None], chosen_sum[:, None, :] - old_sums, 0.0)),
            0.0,
        )
        * old_steps
    )
    weighted = (
        (
            kept_weight[..., None]
            * old_heads.reshape(reqs_dev, NODES, local_heads, HEAD_DIM).astype(jnp.float32)
        )
        .astype(jnp.bfloat16)
        .reshape(reqs_dev, NODES, span_groups, span_heads, HEAD_DIM)
    )
    key_slice = lax.dynamic_slice_in_dim(
        old_keys, first_group * STATE, span_groups * STATE, 2
    ).reshape(reqs_dev, NODES, span_groups, STATE)
    update = jnp.einsum(
        "bjgqp,bjgn->bgqpn", weighted, key_slice, preferred_element_type=jnp.float32
    )
    carry_state = (
        jnp.exp(chosen_sum).reshape(reqs_dev, span_groups, span_heads, 1, 1)
        * old_state.reshape(reqs_dev, span_groups, span_heads, HEAD_DIM, STATE).astype(jnp.float32)
        + update
    ).astype(jnp.bfloat16)
    head_rows, gate_rows, step_rows = (
        lax.all_to_all(tree_heads, "head", split_axis=1, concat_axis=0, tiled=True),
        lax.all_to_all(tree_gates, "head", split_axis=1, concat_axis=0, tiled=True),
        lax.all_to_all(tree_steps, "head", split_axis=1, concat_axis=0, tiled=True),
    )
    group_rows = lax.all_to_all(
        own_columns(tree_groups, span_groups, head_count, per_dest),
        "head",
        split_axis=0,
        concat_axis=0,
        tiled=True,
    )
    head_rows = head_rows.reshape(reqs_dev, NODES, -1)
    gate_rows = gate_rows.reshape(reqs_dev, NODES, span_groups, span_heads, HEAD_DIM)
    step_rows = step_rows.reshape(reqs_dev, NODES, local_heads)
    group_rows = group_rows.reshape(reqs_dev, NODES, -1)
    head_width = tail_heads.shape[-1]
    tails_new = to_new(jnp.concatenate([tail_heads, tail_groups], axis=-1))
    conv_heads = tree_conv(
        head_rows, tails_new[..., :head_width], new_tree, kernel_heads, shift_heads
    )
    kernel_own = own_columns(kernel_groups, span_groups, head_count, per_dest)[head_index]
    shift_own = own_columns(shift_groups, span_groups, head_count, per_dest)[head_index]
    conv_groups = tree_conv(
        group_rows, tails_new[..., head_width:], new_tree, kernel_own, shift_own
    )
    own_keys = conv_groups[..., :own_width]
    own_queries = conv_groups[..., own_width:]
    query_four = own_queries.reshape(reqs_dev, NODES, span_groups, STATE)
    query_old = to_old(query_four)
    carried_old = jnp.einsum(
        "btgn,bgqpn->btgqp", query_old, carry_state, preferred_element_type=jnp.float32
    )
    carried = to_new(carried_old)
    key_four = own_keys.reshape(reqs_dev, NODES, span_groups, STATE)
    step_sizes = jax.nn.softplus(step_rows.astype(jnp.float32) + step_bias)
    decay_sum = jnp.einsum(
        "btj,bjh->bth", new_tree.astype(jnp.float32), step_sizes * decay_rates, precision=highest
    )
    intersection = jnp.einsum(
        "btgn,bjgn->btjg", query_four, key_four, preferred_element_type=jnp.float32
    )
    lineage_new = (new_tree == 1)[:, :, :, None]
    decay_gap = decay_sum[:, :, None, :] - decay_sum[:, None, :, :]
    decays = jnp.where(lineage_new, jnp.exp(jnp.where(lineage_new, decay_gap, 0.0)), 0.0)
    mixing = (
        decays.reshape(reqs_dev, NODES, NODES, span_groups, span_heads)
        * intersection[..., None]
        * step_sizes.reshape(reqs_dev, 1, NODES, span_groups, span_heads)
    ).astype(jnp.bfloat16)
    values = conv_heads.reshape(reqs_dev, NODES, span_groups, span_heads, HEAD_DIM)
    inner_part = jnp.einsum(
        "btjgq,bjgqp->btgqp", mixing, values, preferred_element_type=jnp.float32
    )
    output = (
        inner_part
        + jnp.exp(decay_sum).reshape(reqs_dev, NODES, span_groups, span_heads, 1) * carried
        + skip_gain.reshape(1, 1, span_groups, span_heads, 1) * values.astype(jnp.float32)
    )
    gated_out = output * jax.nn.silu(gate_rows.astype(jnp.float32))
    group_power = jnp.sum(gated_out * gated_out, axis=(3, 4))
    if per_dest == 2:
        partner = [(d, d ^ 1) for d in range(head_count)]
        power_own = group_power + lax.ppermute(group_power, "head", partner)
    else:
        zero_index = jnp.zeros((), jnp.int32)
        power_full = lax.dynamic_update_slice(
            jnp.zeros((reqs_dev, NODES, GROUPS), jnp.float32),
            group_power,
            (zero_index, zero_index, first_group),
        )
        power_total = lax.psum(power_full, "head")
        power_own = lax.dynamic_slice_in_dim(power_total, first_group, span_groups, 2)
    scale_factor = lax.rsqrt(power_own / (per_group * HEAD_DIM) + EPSILON)
    normed = (
        gated_out
        * scale_factor[..., None, None]
        * norm_gain.reshape(1, 1, span_groups, span_heads, HEAD_DIM)
    )
    return normed.reshape(reqs_dev * NODES, local_heads * HEAD_DIM).astype(jnp.bfloat16)


def solution(mesh):
    placed = (
        P(("req", "head"), None),
        P(("req", "head"), None),
        P(("req", "head"), None),
        P(("req", "head"), None),
        P("req", None, None),
        P(None, "head"),
        P("head"),
        P(),
        P(),
        P("head"),
        P("head"),
        P("head"),
        P("head"),
        P("req", "head", None, None),
        P("req", None, "head"),
        P("req", None, None),
        P("req", None, "head"),
        P("req", None, "head"),
        P("req", "head", None),
        P("req", None, None),
        P("req"),
        P(),
    )
    return jax.shard_map(
        shards, mesh=mesh, in_specs=placed, out_specs=P("req", "head"), check_vma=False
    )
```

```python
import jax
import jax.numpy as jnp
from jax import lax
from jax.sharding import PartitionSpec as P

HEADS = 256
HEAD_DIM = 64
STATE = 256
GROUPS = 8
NODES = 32
MOST = 2


EPSILON = 1e-05


def tree_conv(tree_rows, tail_rows, ancestry, weight, offset_bias):
    node_depth = jnp.sum(ancestry, axis=-1) - 1
    places = jnp.arange(3, dtype=jnp.int32)
    summed = weight[3].astype(jnp.float32) * tree_rows.astype(jnp.float32) + offset_bias
    for upward in range(1, 4):
        picked = (
            (ancestry == 1) & (node_depth[:, None, :] == node_depth[:, :, None] - upward)
        ).astype(jnp.bfloat16)
        older_rows = (places[None, None, :] == node_depth[:, :, None] - upward + 3).astype(
            jnp.bfloat16
        )
        shifted = jnp.einsum("btj,bjc->btc", picked, tree_rows, preferred_element_type=jnp.float32)
        shifted = shifted + jnp.einsum(
            "bti,bic->btc", older_rows, tail_rows, preferred_element_type=jnp.float32
        )
        summed = summed + weight[3 - upward].astype(jnp.float32) * shifted
    return jax.nn.silu(summed).astype(jnp.bfloat16)


def place_slots(payload, positions, count):
    wanted = jnp.arange(count, dtype=jnp.int32)
    owners = jnp.arange(positions.shape[0], dtype=jnp.int32)
    hits = positions[None, :] == wanted[:, None]
    chosen = jnp.sum(jnp.where(hits, owners[None, :], 0), axis=1)
    filled = jnp.any(hits, axis=1).reshape((count,) + (1,) * (payload.ndim - 1))
    taken = jnp.take(payload, chosen, axis=0)
    return jnp.where(filled, taken, jnp.zeros_like(taken))


def own_columns(rows, span_groups, dest_count, per_dest):
    lead = rows.shape[:-1]
    split = rows.reshape(lead + (2, GROUPS, STATE))
    moved = jnp.moveaxis(split, -2, 0)
    picks = (jnp.arange(dest_count, dtype=jnp.int32) // per_dest)[:, None] * span_groups + jnp.arange(
        span_groups, dtype=jnp.int32
    )[None, :]
    taken = jnp.take(moved, picks.reshape(-1), axis=0).reshape((dest_count, span_groups) + lead + (2, STATE))
    return jnp.moveaxis(taken, 1, -2).reshape((dest_count,) + lead + (2 * span_groups * STATE,))


def shards(
    tree_heads,
    tree_gates,
    tree_steps,
    tree_groups,
    new_tree,
    kernel_heads,
    shift_heads,
    kernel_groups,
    shift_groups,
    log_rates,
    step_bias,
    skip_gain,
    norm_gain,
    old_state,
    old_heads,
    old_keys,
    old_steps,
    prior_heads,
    prior_groups,
    old_tree,
    accepted,
    new_owner,
):
    req_count = lax.axis_size("req")
    head_count = lax.axis_size("head")
    req_index = lax.axis_index("req")
    head_index = lax.axis_index("head")
    reqs_dev = new_tree.shape[0]
    local_heads = log_rates.shape[0]
    local_nodes = prior_groups.shape[1]
    per_group = HEADS // GROUPS
    span_heads = min(local_heads, per_group)
    span_groups = local_heads // span_heads
    per_dest = per_group // span_heads
    first_group = head_index * local_heads // per_group
    slot_count = req_count * MOST
    own_width = span_groups * STATE
    highest = lax.Precision.HIGHEST
    owner_table = new_owner.reshape(req_count, reqs_dev)
    target_dev = owner_table // reqs_dev
    local_ids = jnp.arange(reqs_dev, dtype=jnp.int32)
    before = local_ids[None, :, None] > local_ids[None, None, :]
    same_dest = target_dev[:, :, None] == target_dev[:, None, :]
    arrival = jnp.sum((same_dest & before).astype(jnp.int32), axis=-1)
    send_table = target_dev * MOST + arrival
    send_pos = lax.dynamic_index_in_dim(send_table, req_index, 0, keepdims=False)
    wanted_slot = req_index * reqs_dev + local_ids
    all_ids = jnp.arange(new_owner.shape[0], dtype=jnp.int32)
    match = new_owner[None, :] == wanted_slot[:, None]
    anchor = jnp.sum(jnp.where(match, all_ids[None, :], 0), axis=1)
    recv_pos = anchor // reqs_dev * MOST + jnp.take(arrival.reshape(-1), anchor)

    def to_new(payload):
        placed = place_slots(payload, send_pos, slot_count)
        moved = lax.all_to_all(placed, "req", split_axis=0, concat_axis=0, tiled=True)
        return jnp.take(moved, recv_pos, axis=0)

    def to_old(payload):
        placed = place_slots(payload, recv_pos, slot_count)
        moved = lax.all_to_all(placed, "req", split_axis=0, concat_axis=0, tiled=True)
        return jnp.take(moved, send_pos, axis=0)

    decay_rates = -jnp.exp(log_rates)
    node_ids = jnp.arange(NODES, dtype=jnp.int32)
    chosen_hot = node_ids[None, :] == accepted[:, None]
    chosen_row = jnp.sum(jnp.where(chosen_hot[:, :, None], old_tree, 0), axis=1)
    old_depth = jnp.sum(old_tree, axis=-1) - 1
    chosen_depth = jnp.sum(jnp.where(chosen_hot, old_depth, 0), axis=1)
    places = jnp.arange(3, dtype=jnp.int32)
    lineage = chosen_row == 1
    tail_pick = (
        lineage[:, None, :]
        & (old_depth[:, None, :] == chosen_depth[:, None, None] - 2 + places[None, :, None])
    ).astype(jnp.bfloat16)
    tail_heads = jnp.einsum(
        "bij,bjc->bic", tail_pick, prior_heads, preferred_element_type=jnp.float32
    ).astype(jnp.bfloat16)
    old_sums = jnp.einsum(
        "btj,bjh->bth", old_tree.astype(jnp.float32), old_steps * decay_rates, precision=highest
    )
    chosen_sum = jnp.sum(jnp.where(chosen_hot[:, :, None], old_sums, 0.0), axis=1)
    kept_weight = (
        jnp.where(
            lineage[:, :, None],
            jnp.exp(jnp.where(lineage[:, :, None], chosen_sum[:, None, :] - old_sums, 0.0)),
            0.0,
        )
        * old_steps
    )
    weighted = (
        (
            kept_weight[..., None]
            * old_heads.reshape(reqs_dev, NODES, local_heads, HEAD_DIM).astype(jnp.float32)
        )
        .astype(jnp.bfloat16)
        .reshape(reqs_dev, NODES, span_groups, span_heads, HEAD_DIM)
    )
    key_slice = lax.dynamic_slice_in_dim(
        old_keys, first_group * STATE, span_groups * STATE, 2
    ).reshape(reqs_dev, NODES, span_groups, STATE)
    update = jnp.einsum(
        "bjgqp,bjgn->bgqpn", weighted, key_slice, preferred_element_type=jnp.float32
    )
    carry_state = (
        jnp.exp(chosen_sum).reshape(reqs_dev, span_groups, span_heads, 1, 1)
        * old_state.reshape(reqs_dev, span_groups, span_heads, HEAD_DIM, STATE).astype(jnp.float32)
        + update
    ).astype(jnp.bfloat16)
    tree_rows = tree_heads.shape[0]
    head_width = local_heads * HEAD_DIM
    split_heads = jnp.moveaxis(tree_heads.reshape(tree_rows, head_count, head_width), 1, 0)
    split_gates = jnp.moveaxis(tree_gates.reshape(tree_rows, head_count, head_width), 1, 0)
    split_steps = jnp.moveaxis(tree_steps.reshape(tree_rows, head_count, local_heads), 1, 0)
    split_groups = own_columns(tree_groups, span_groups, head_count, per_dest)
    split_prior = own_columns(prior_groups, span_groups, head_count, per_dest).reshape(
        head_count, reqs_dev * local_nodes, 2 * own_width
    )
    widths = [head_width, head_width, local_heads, 2 * own_width, 2 * own_width]
    bundle = jnp.concatenate(
        [split_heads, split_gates, split_steps, split_groups, split_prior.astype(jnp.bfloat16)], axis=-1
    )
    bundle = lax.all_to_all(bundle, "head", split_axis=0, concat_axis=0, tiled=True)
    cuts = [0]
    for width in widths:
        cuts.append(cuts[-1] + width)
    pieces = [bundle[..., cuts[n] : cuts[n + 1]] for n in range(len(widths))]
    head_rows = pieces[0].reshape(reqs_dev, NODES, head_width)
    gate_rows = pieces[1].reshape(reqs_dev, NODES, span_groups, span_heads, HEAD_DIM)
    step_rows = pieces[2].reshape(reqs_dev, NODES, local_heads)
    group_rows = pieces[3].reshape(reqs_dev, NODES, 2 * own_width)
    prior_own = jnp.moveaxis(
        pieces[4].reshape(head_count, reqs_dev, local_nodes, 2 * own_width), 0, 1
    ).reshape(reqs_dev, NODES, 2 * own_width)
    tail_groups = jnp.einsum(
        "bij,bjc->bic", tail_pick, prior_own, preferred_element_type=jnp.float32
    ).astype(jnp.bfloat16)
    new_part = jnp.concatenate([tail_heads, tail_groups], axis=-1).reshape(reqs_dev, -1)
    old_part = jnp.concatenate(
        [group_rows[..., own_width:], new_tree.astype(jnp.bfloat16)], axis=-1
    ).reshape(reqs_dev, -1)
    new_len = new_part.shape[-1]
    exchange = jnp.concatenate(
        [place_slots(new_part, send_pos, slot_count), place_slots(old_part, recv_pos, slot_count)],
        axis=-1,
    )
    exchange = lax.all_to_all(exchange, "req", split_axis=0, concat_axis=0, tiled=True)
    tails_new = jnp.take(exchange[:, :new_len], recv_pos, axis=0).reshape(reqs_dev, 3, -1)
    rows_old = jnp.take(exchange[:, new_len:], send_pos, axis=0).reshape(reqs_dev, NODES, -1)
    tree_old = rows_old[..., own_width:].astype(jnp.int32)
    kernel_own = own_columns(kernel_groups, span_groups, head_count, per_dest)[head_index]
    shift_own = own_columns(shift_groups, span_groups, head_count, per_dest)[head_index]
    query_old = tree_conv(
        rows_old[..., :own_width],
        tail_groups[..., own_width:],
        tree_old,
        kernel_own[:, own_width:],
        shift_own[own_width:],
    ).reshape(reqs_dev, NODES, span_groups, STATE)
    carried_old = jnp.einsum(
        "btgn,bgqpn->btgqp", query_old, carry_state, preferred_element_type=jnp.float32
    ).reshape(reqs_dev, NODES, head_width)
    carried = to_new(carried_old).reshape(reqs_dev, NODES, span_groups, span_heads, HEAD_DIM)
    conv_heads = tree_conv(
        head_rows, tails_new[..., :head_width], new_tree, kernel_heads, shift_heads
    )
    conv_groups = tree_conv(
        group_rows, tails_new[..., head_width:], new_tree, kernel_own, shift_own
    )
    own_keys = conv_groups[..., :own_width]
    own_queries = conv_groups[..., own_width:]
    query_four = own_queries.reshape(reqs_dev, NODES, span_groups, STATE)
    key_four = own_keys.reshape(reqs_dev, NODES, span_groups, STATE)
    step_sizes = jax.nn.softplus(step_rows.astype(jnp.float32) + step_bias)
    decay_sum = jnp.einsum(
        "btj,bjh->bth", new_tree.astype(jnp.float32), step_sizes * decay_rates, precision=highest
    )
    intersection = jnp.einsum(
        "btgn,bjgn->btjg", query_four, key_four, preferred_element_type=jnp.float32
    )
    lineage_new = (new_tree == 1)[:, :, :, None]
    decay_gap = decay_sum[:, :, None, :] - decay_sum[:, None, :, :]
    decays = jnp.where(lineage_new, jnp.exp(jnp.where(lineage_new, decay_gap, 0.0)), 0.0)
    mixing = (
        decays.reshape(reqs_dev, NODES, NODES, span_groups, span_heads)
        * intersection[..., None]
        * step_sizes.reshape(reqs_dev, 1, NODES, span_groups, span_heads)
    ).astype(jnp.bfloat16)
    values = conv_heads.reshape(reqs_dev, NODES, span_groups, span_heads, HEAD_DIM)
    inner_part = jnp.einsum(
        "btjgq,bjgqp->btgqp", mixing, values, preferred_element_type=jnp.float32
    )
    output = (
        inner_part
        + jnp.exp(decay_sum).reshape(reqs_dev, NODES, span_groups, span_heads, 1) * carried
        + skip_gain.reshape(1, 1, span_groups, span_heads, 1) * values.astype(jnp.float32)
    )
    gated_out = output * jax.nn.silu(gate_rows.astype(jnp.float32))
    group_power = jnp.sum(gated_out * gated_out, axis=(3, 4))
    if per_dest == 2:
        partner = [(d, d ^ 1) for d in range(head_count)]
        power_own = group_power + lax.ppermute(group_power, "head", partner)
    else:
        zero_index = jnp.zeros((), jnp.int32)
        power_full = lax.dynamic_update_slice(
            jnp.zeros((reqs_dev, NODES, GROUPS), jnp.float32),
            group_power,
            (zero_index, zero_index, first_group),
        )
        power_total = lax.psum(power_full, "head")
        power_own = lax.dynamic_slice_in_dim(power_total, first_group, span_groups, 2)
    scale_factor = lax.rsqrt(power_own / (per_group * HEAD_DIM) + EPSILON)
    normed = (
        gated_out
        * scale_factor[..., None, None]
        * norm_gain.reshape(1, 1, span_groups, span_heads, HEAD_DIM)
    )
    return normed.reshape(reqs_dev * NODES, local_heads * HEAD_DIM).astype(jnp.bfloat16)


def solution(mesh):
    placed = (
        P(("req", "head"), None),
        P(("req", "head"), None),
        P(("req", "head"), None),
        P(("req", "head"), None),
        P("req", None, None),
        P(None, "head"),
        P("head"),
        P(),
        P(),
        P("head"),
        P("head"),
        P("head"),
        P("head"),
        P("req", "head", None, None),
        P("req", None, "head"),
        P("req", None, None),
        P("req", None, "head"),
        P("req", None, "head"),
        P("req", "head", None),
        P("req", None, None),
        P("req"),
        P(),
    )
    return jax.shard_map(
        shards, mesh=mesh, in_specs=placed, out_specs=P("req", "head"), check_vma=False
    )
```

```python
import jax
import jax.numpy as jnp
from jax import lax
from jax.sharding import PartitionSpec as P

HEADS = 256
HEAD_DIM = 64
STATE = 256
GROUPS = 8
NODES = 32
MOST = 2


EPSILON = 1e-05


def tree_conv(tree_rows, tail_rows, ancestry, weight, offset_bias):
    node_depth = jnp.sum(ancestry, axis=-1) - 1
    places = jnp.arange(3, dtype=jnp.int32)
    summed = weight[3].astype(jnp.float32) * tree_rows.astype(jnp.float32) + offset_bias
    for upward in range(1, 4):
        picked = (
            (ancestry == 1) & (node_depth[:, None, :] == node_depth[:, :, None] - upward)
        ).astype(jnp.bfloat16)
        older_rows = (places[None, None, :] == node_depth[:, :, None] - upward + 3).astype(
            jnp.bfloat16
        )
        shifted = jnp.einsum("btj,bjc->btc", picked, tree_rows, preferred_element_type=jnp.float32)
        shifted = shifted + jnp.einsum(
            "bti,bic->btc", older_rows, tail_rows, preferred_element_type=jnp.float32
        )
        summed = summed + weight[3 - upward].astype(jnp.float32) * shifted
    return jax.nn.silu(summed).astype(jnp.bfloat16)


def place_slots(payload, positions, count):
    wanted = jnp.arange(count, dtype=jnp.int32)
    owners = jnp.arange(positions.shape[0], dtype=jnp.int32)
    hits = positions[None, :] == wanted[:, None]
    chosen = jnp.sum(jnp.where(hits, owners[None, :], 0), axis=1)
    filled = jnp.any(hits, axis=1).reshape((count,) + (1,) * (payload.ndim - 1))
    taken = jnp.take(payload, chosen, axis=0)
    return jnp.where(filled, taken, jnp.zeros_like(taken))


def own_columns(rows, span_groups, dest_count, per_dest):
    lead = rows.shape[:-1]
    split = rows.reshape(lead + (2, GROUPS, STATE))
    moved = jnp.moveaxis(split, -2, 0)
    picks = (jnp.arange(dest_count, dtype=jnp.int32) // per_dest)[:, None] * span_groups + jnp.arange(
        span_groups, dtype=jnp.int32
    )[None, :]
    taken = jnp.take(moved, picks.reshape(-1), axis=0).reshape((dest_count, span_groups) + lead + (2, STATE))
    return jnp.moveaxis(taken, 1, -2).reshape((dest_count,) + lead + (2 * span_groups * STATE,))


def shards(
    tree_heads,
    tree_gates,
    tree_steps,
    tree_groups,
    new_tree,
    kernel_heads,
    shift_heads,
    kernel_groups,
    shift_groups,
    log_rates,
    step_bias,
    skip_gain,
    norm_gain,
    old_state,
    old_heads,
    old_keys,
    old_steps,
    prior_heads,
    prior_groups,
    old_tree,
    accepted,
    new_owner,
):
    req_count = lax.axis_size("req")
    head_count = lax.axis_size("head")
    req_index = lax.axis_index("req")
    head_index = lax.axis_index("head")
    reqs_dev = new_tree.shape[0]
    local_heads = log_rates.shape[0]
    local_nodes = prior_groups.shape[1]
    per_group = HEADS // GROUPS
    span_heads = min(local_heads, per_group)
    span_groups = local_heads // span_heads
    per_dest = per_group // span_heads
    first_group = head_index * local_heads // per_group
    slot_count = req_count * MOST
    own_width = span_groups * STATE
    highest = lax.Precision.HIGHEST
    owner_table = new_owner.reshape(req_count, reqs_dev)
    target_dev = owner_table // reqs_dev
    local_ids = jnp.arange(reqs_dev, dtype=jnp.int32)
    before = local_ids[None, :, None] > local_ids[None, None, :]
    same_dest = target_dev[:, :, None] == target_dev[:, None, :]
    arrival = jnp.sum((same_dest & before).astype(jnp.int32), axis=-1)
    send_table = target_dev * MOST + arrival
    send_pos = lax.dynamic_index_in_dim(send_table, req_index, 0, keepdims=False)
    wanted_slot = req_index * reqs_dev + local_ids
    all_ids = jnp.arange(new_owner.shape[0], dtype=jnp.int32)
    match = new_owner[None, :] == wanted_slot[:, None]
    anchor = jnp.sum(jnp.where(match, all_ids[None, :], 0), axis=1)
    recv_pos = anchor // reqs_dev * MOST + jnp.take(arrival.reshape(-1), anchor)

    def to_new(payload):
        placed = place_slots(payload, send_pos, slot_count)
        moved = lax.all_to_all(placed, "req", split_axis=0, concat_axis=0, tiled=True)
        return jnp.take(moved, recv_pos, axis=0)

    def to_old(payload):
        placed = place_slots(payload, recv_pos, slot_count)
        moved = lax.all_to_all(placed, "req", split_axis=0, concat_axis=0, tiled=True)
        return jnp.take(moved, send_pos, axis=0)

    decay_rates = -jnp.exp(log_rates)
    node_ids = jnp.arange(NODES, dtype=jnp.int32)
    chosen_hot = node_ids[None, :] == accepted[:, None]
    chosen_row = jnp.sum(jnp.where(chosen_hot[:, :, None], old_tree, 0), axis=1)
    old_depth = jnp.sum(old_tree, axis=-1) - 1
    chosen_depth = jnp.sum(jnp.where(chosen_hot, old_depth, 0), axis=1)
    places = jnp.arange(3, dtype=jnp.int32)
    lineage = chosen_row == 1
    tail_pick = (
        lineage[:, None, :]
        & (old_depth[:, None, :] == chosen_depth[:, None, None] - 2 + places[None, :, None])
    ).astype(jnp.bfloat16)
    tail_heads = jnp.einsum(
        "bij,bjc->bic", tail_pick, prior_heads, preferred_element_type=jnp.float32
    ).astype(jnp.bfloat16)
    old_sums = jnp.einsum(
        "btj,bjh->bth", old_tree.astype(jnp.float32), old_steps * decay_rates, precision=highest
    )
    chosen_sum = jnp.sum(jnp.where(chosen_hot[:, :, None], old_sums, 0.0), axis=1)
    kept_weight = (
        jnp.where(
            lineage[:, :, None],
            jnp.exp(jnp.where(lineage[:, :, None], chosen_sum[:, None, :] - old_sums, 0.0)),
            0.0,
        )
        * old_steps
    )
    weighted = (
        (
            kept_weight[..., None]
            * old_heads.reshape(reqs_dev, NODES, local_heads, HEAD_DIM).astype(jnp.float32)
        )
        .astype(jnp.bfloat16)
        .reshape(reqs_dev, NODES, span_groups, span_heads, HEAD_DIM)
    )
    key_slice = lax.dynamic_slice_in_dim(
        old_keys, first_group * STATE, span_groups * STATE, 2
    ).reshape(reqs_dev, NODES, span_groups, STATE)
    update = jnp.einsum(
        "bjgqp,bjgn->bgqpn", weighted, key_slice, preferred_element_type=jnp.float32
    )
    carry_state = (
        jnp.exp(chosen_sum).reshape(reqs_dev, span_groups, span_heads, 1, 1)
        * old_state.reshape(reqs_dev, span_groups, span_heads, HEAD_DIM, STATE).astype(jnp.float32)
        + update
    ).astype(jnp.bfloat16)
    tree_rows = tree_heads.shape[0]
    head_width = local_heads * HEAD_DIM
    split_heads = jnp.moveaxis(tree_heads.reshape(tree_rows, head_count, head_width), 1, 0)
    split_gates = jnp.moveaxis(tree_gates.reshape(tree_rows, head_count, head_width), 1, 0)
    split_steps = jnp.moveaxis(tree_steps.reshape(tree_rows, head_count, local_heads), 1, 0)
    split_groups = own_columns(tree_groups, span_groups, head_count, per_dest)
    split_prior = own_columns(prior_groups, span_groups, head_count, per_dest).reshape(
        head_count, reqs_dev * local_nodes, 2 * own_width
    )
    widths = [head_width, head_width, local_heads, 2 * own_width, 2 * own_width]
    bundle = jnp.concatenate(
        [split_heads, split_gates, split_steps, split_groups, split_prior.astype(jnp.bfloat16)], axis=-1
    )
    bundle = lax.all_to_all(bundle, "head", split_axis=0, concat_axis=0, tiled=True)
    cuts = [0]
    for width in widths:
        cuts.append(cuts[-1] + width)
    pieces = [bundle[..., cuts[n] : cuts[n + 1]] for n in range(len(widths))]
    head_rows = pieces[0].reshape(reqs_dev, NODES, head_width)
    gate_rows = pieces[1].reshape(reqs_dev, NODES, span_groups, span_heads, HEAD_DIM)
    step_rows = pieces[2].reshape(reqs_dev, NODES, local_heads)
    group_rows = pieces[3].reshape(reqs_dev, NODES, 2 * own_width)
    prior_own = jnp.moveaxis(
        pieces[4].reshape(head_count, reqs_dev, local_nodes, 2 * own_width), 0, 1
    ).reshape(reqs_dev, NODES, 2 * own_width)
    tail_groups = jnp.einsum(
        "bij,bjc->bic", tail_pick, prior_own, preferred_element_type=jnp.float32
    ).astype(jnp.bfloat16)
    new_part = jnp.concatenate([tail_heads, tail_groups], axis=-1).reshape(reqs_dev, -1)
    old_part = jnp.concatenate(
        [group_rows[..., own_width:], new_tree.astype(jnp.bfloat16)], axis=-1
    ).reshape(reqs_dev, -1)
    new_len = new_part.shape[-1]
    exchange = jnp.concatenate(
        [place_slots(new_part, send_pos, slot_count), place_slots(old_part, recv_pos, slot_count)],
        axis=-1,
    )
    exchange = lax.all_to_all(exchange, "req", split_axis=0, concat_axis=0, tiled=True)
    tails_new = jnp.take(exchange[:, :new_len], recv_pos, axis=0).reshape(reqs_dev, 3, -1)
    rows_old = jnp.take(exchange[:, new_len:], send_pos, axis=0).reshape(reqs_dev, NODES, -1)
    tree_old = rows_old[..., own_width:].astype(jnp.int32)
    kernel_own = own_columns(kernel_groups, span_groups, head_count, per_dest)[head_index]
    shift_own = own_columns(shift_groups, span_groups, head_count, per_dest)[head_index]
    query_old = tree_conv(
        rows_old[..., :own_width],
        tail_groups[..., own_width:],
        tree_old,
        kernel_own[:, own_width:],
        shift_own[own_width:],
    ).reshape(reqs_dev, NODES, span_groups, STATE)
    carried_old = jnp.einsum(
        "btgn,bgqpn->btgqp", query_old, carry_state, preferred_element_type=jnp.float32
    ).reshape(reqs_dev, NODES, head_width)
    carried = to_new(carried_old.astype(jnp.bfloat16)).astype(jnp.float32).reshape(reqs_dev, NODES, span_groups, span_heads, HEAD_DIM)
    conv_heads = tree_conv(
        head_rows, tails_new[..., :head_width], new_tree, kernel_heads, shift_heads
    )
    conv_groups = tree_conv(
        group_rows, tails_new[..., head_width:], new_tree, kernel_own, shift_own
    )
    own_keys = conv_groups[..., :own_width]
    own_queries = conv_groups[..., own_width:]
    query_four = own_queries.reshape(reqs_dev, NODES, span_groups, STATE)
    key_four = own_keys.reshape(reqs_dev, NODES, span_groups, STATE)
    step_sizes = jax.nn.softplus(step_rows.astype(jnp.float32) + step_bias)
    decay_sum = jnp.einsum(
        "btj,bjh->bth", new_tree.astype(jnp.float32), step_sizes * decay_rates, precision=highest
    )
    intersection = jnp.einsum(
        "btgn,bjgn->btjg", query_four, key_four, preferred_element_type=jnp.float32
    )
    lineage_new = (new_tree == 1)[:, :, :, None]
    decay_gap = decay_sum[:, :, None, :] - decay_sum[:, None, :, :]
    decays = jnp.where(lineage_new, jnp.exp(jnp.where(lineage_new, decay_gap, 0.0)), 0.0)
    mixing = (
        decays.reshape(reqs_dev, NODES, NODES, span_groups, span_heads)
        * intersection[..., None]
        * step_sizes.reshape(reqs_dev, 1, NODES, span_groups, span_heads)
    ).astype(jnp.bfloat16)
    values = conv_heads.reshape(reqs_dev, NODES, span_groups, span_heads, HEAD_DIM)
    inner_part = jnp.einsum(
        "btjgq,bjgqp->btgqp", mixing, values, preferred_element_type=jnp.float32
    )
    output = (
        inner_part
        + jnp.exp(decay_sum).reshape(reqs_dev, NODES, span_groups, span_heads, 1) * carried
        + skip_gain.reshape(1, 1, span_groups, span_heads, 1) * values.astype(jnp.float32)
    )
    gated_out = output * jax.nn.silu(gate_rows.astype(jnp.float32))
    group_power = jnp.sum(gated_out * gated_out, axis=(3, 4))
    if per_dest == 2:
        partner = [(d, d ^ 1) for d in range(head_count)]
        power_own = group_power + lax.ppermute(group_power, "head", partner)
    else:
        zero_index = jnp.zeros((), jnp.int32)
        power_full = lax.dynamic_update_slice(
            jnp.zeros((reqs_dev, NODES, GROUPS), jnp.float32),
            group_power,
            (zero_index, zero_index, first_group),
        )
        power_total = lax.psum(power_full, "head")
        power_own = lax.dynamic_slice_in_dim(power_total, first_group, span_groups, 2)
    scale_factor = lax.rsqrt(power_own / (per_group * HEAD_DIM) + EPSILON)
    normed = (
        gated_out
        * scale_factor[..., None, None]
        * norm_gain.reshape(1, 1, span_groups, span_heads, HEAD_DIM)
    )
    return normed.reshape(reqs_dev * NODES, local_heads * HEAD_DIM).astype(jnp.bfloat16)


def solution(mesh):
    placed = (
        P(("req", "head"), None),
        P(("req", "head"), None),
        P(("req", "head"), None),
        P(("req", "head"), None),
        P("req", None, None),
        P(None, "head"),
        P("head"),
        P(),
        P(),
        P("head"),
        P("head"),
        P("head"),
        P("head"),
        P("req", "head", None, None),
        P("req", None, "head"),
        P("req", None, None),
        P("req", None, "head"),
        P("req", None, "head"),
        P("req", "head", None),
        P("req", None, None),
        P("req"),
        P(),
    )
    return jax.shard_map(
        shards, mesh=mesh, in_specs=placed, out_specs=P("req", "head"), check_vma=False
    )
```

```python
import jax
import jax.numpy as jnp
from jax import lax
from jax.sharding import PartitionSpec as P

HEADS = 256
HEAD_DIM = 64
STATE = 256
GROUPS = 8
NODES = 32
MOST = 2


EPSILON = 1e-05


def tree_conv(tree_rows, tail_rows, ancestry, weight, offset_bias):
    node_depth = jnp.sum(ancestry, axis=-1) - 1
    places = jnp.arange(3, dtype=jnp.int32)
    summed = weight[3].astype(jnp.float32) * tree_rows.astype(jnp.float32) + offset_bias
    for upward in range(1, 4):
        picked = (
            (ancestry == 1) & (node_depth[:, None, :] == node_depth[:, :, None] - upward)
        ).astype(jnp.bfloat16)
        older_rows = (places[None, None, :] == node_depth[:, :, None] - upward + 3).astype(
            jnp.bfloat16
        )
        shifted = jnp.einsum("btj,bjc->btc", picked, tree_rows, preferred_element_type=jnp.float32)
        shifted = shifted + jnp.einsum(
            "bti,bic->btc", older_rows, tail_rows, preferred_element_type=jnp.float32
        )
        summed = summed + weight[3 - upward].astype(jnp.float32) * shifted
    return jax.nn.silu(summed).astype(jnp.bfloat16)


def place_slots(payload, positions, count):
    wanted = jnp.arange(count, dtype=jnp.int32)
    owners = jnp.arange(positions.shape[0], dtype=jnp.int32)
    hits = positions[None, :] == wanted[:, None]
    chosen = jnp.sum(jnp.where(hits, owners[None, :], 0), axis=1)
    filled = jnp.any(hits, axis=1).reshape((count,) + (1,) * (payload.ndim - 1))
    taken = jnp.take(payload, chosen, axis=0)
    return jnp.where(filled, taken, jnp.zeros_like(taken))


def own_columns(rows, span_groups, dest_count, per_dest):
    lead = rows.shape[:-1]
    split = rows.reshape(lead + (2, GROUPS, STATE))
    moved = jnp.moveaxis(split, -2, 0)
    picks = (jnp.arange(dest_count, dtype=jnp.int32) // per_dest)[:, None] * span_groups + jnp.arange(
        span_groups, dtype=jnp.int32
    )[None, :]
    taken = jnp.take(moved, picks.reshape(-1), axis=0).reshape((dest_count, span_groups) + lead + (2, STATE))
    return jnp.moveaxis(taken, 1, -2).reshape((dest_count,) + lead + (2 * span_groups * STATE,))


def shards(
    tree_heads,
    tree_gates,
    tree_steps,
    tree_groups,
    new_tree,
    kernel_heads,
    shift_heads,
    kernel_groups,
    shift_groups,
    log_rates,
    step_bias,
    skip_gain,
    norm_gain,
    old_state,
    old_heads,
    old_keys,
    old_steps,
    prior_heads,
    prior_groups,
    old_tree,
    accepted,
    new_owner,
):
    req_count = lax.axis_size("req")
    head_count = lax.axis_size("head")
    req_index = lax.axis_index("req")
    head_index = lax.axis_index("head")
    reqs_dev = new_tree.shape[0]
    local_heads = log_rates.shape[0]
    local_nodes = prior_groups.shape[1]
    per_group = HEADS // GROUPS
    span_heads = min(local_heads, per_group)
    span_groups = local_heads // span_heads
    per_dest = per_group // span_heads
    assert span_groups == 1
    first_group = head_index * local_heads // per_group
    slot_count = req_count * MOST
    own_width = span_groups * STATE
    highest = lax.Precision.HIGHEST
    owner_table = new_owner.reshape(req_count, reqs_dev)
    target_dev = owner_table // reqs_dev
    local_ids = jnp.arange(reqs_dev, dtype=jnp.int32)
    before = local_ids[None, :, None] > local_ids[None, None, :]
    same_dest = target_dev[:, :, None] == target_dev[:, None, :]
    arrival = jnp.sum((same_dest & before).astype(jnp.int32), axis=-1)
    send_table = target_dev * MOST + arrival
    send_pos = lax.dynamic_index_in_dim(send_table, req_index, 0, keepdims=False)
    wanted_slot = req_index * reqs_dev + local_ids
    all_ids = jnp.arange(new_owner.shape[0], dtype=jnp.int32)
    match = new_owner[None, :] == wanted_slot[:, None]
    anchor = jnp.sum(jnp.where(match, all_ids[None, :], 0), axis=1)
    recv_pos = anchor // reqs_dev * MOST + jnp.take(arrival.reshape(-1), anchor)

    slot_ids = jnp.arange(slot_count, dtype=jnp.int32)
    send_hot = (send_pos[None, :] == slot_ids[:, None]).astype(jnp.bfloat16)
    recv_hot = (recv_pos[None, :] == slot_ids[:, None]).astype(jnp.bfloat16)

    def spread(hot, payload):
        return jnp.einsum(
            "pa,ac->pc", hot, payload, preferred_element_type=jnp.float32
        ).astype(jnp.bfloat16)

    def gather_back(hot, moved):
        return jnp.einsum("pa,pc->ac", hot, moved, preferred_element_type=jnp.float32)

    decay_rates = -jnp.exp(log_rates)
    node_ids = jnp.arange(NODES, dtype=jnp.int32)
    chosen_hot = node_ids[None, :] == accepted[:, None]
    chosen_row = jnp.sum(jnp.where(chosen_hot[:, :, None], old_tree, 0), axis=1)
    old_depth = jnp.sum(old_tree, axis=-1) - 1
    chosen_depth = jnp.sum(jnp.where(chosen_hot, old_depth, 0), axis=1)
    places = jnp.arange(3, dtype=jnp.int32)
    lineage = chosen_row == 1
    tail_pick = (
        lineage[:, None, :]
        & (old_depth[:, None, :] == chosen_depth[:, None, None] - 2 + places[None, :, None])
    ).astype(jnp.bfloat16)
    tail_heads = jnp.einsum(
        "bij,bjc->bic", tail_pick, prior_heads, preferred_element_type=jnp.float32
    ).astype(jnp.bfloat16)
    old_sums = jnp.einsum(
        "btj,bjh->bth", old_tree.astype(jnp.float32), old_steps * decay_rates, precision=highest
    )
    chosen_sum = jnp.sum(jnp.where(chosen_hot[:, :, None], old_sums, 0.0), axis=1)
    kept_weight = (
        jnp.where(
            lineage[:, :, None],
            jnp.exp(jnp.where(lineage[:, :, None], chosen_sum[:, None, :] - old_sums, 0.0)),
            0.0,
        )
        * old_steps
    )
    weighted = (
        (
            kept_weight[..., None]
            * old_heads.reshape(reqs_dev, NODES, local_heads, HEAD_DIM).astype(jnp.float32)
        )
        .astype(jnp.bfloat16)
        .reshape(reqs_dev, NODES, span_groups, span_heads, HEAD_DIM)
    )
    key_slice = lax.dynamic_slice_in_dim(
        old_keys, first_group * STATE, span_groups * STATE, 2
    ).reshape(reqs_dev, NODES, span_groups, STATE)
    update = jnp.einsum(
        "bjgqp,bjgn->bgqpn", weighted, key_slice, preferred_element_type=jnp.float32
    )
    carry_state = (
        jnp.exp(chosen_sum).reshape(reqs_dev, span_groups, span_heads, 1, 1)
        * old_state.reshape(reqs_dev, span_groups, span_heads, HEAD_DIM, STATE).astype(jnp.float32)
        + update
    ).astype(jnp.bfloat16)
    carry_state = lax.optimization_barrier(carry_state)
    tree_rows = tree_heads.shape[0]
    head_width = local_heads * HEAD_DIM
    split_heads = jnp.moveaxis(tree_heads.reshape(tree_rows, head_count, head_width), 1, 0)
    split_gates = jnp.moveaxis(tree_gates.reshape(tree_rows, head_count, head_width), 1, 0)
    split_steps = jnp.moveaxis(tree_steps.reshape(tree_rows, head_count, local_heads), 1, 0)
    split_groups = own_columns(tree_groups, span_groups, head_count, per_dest)
    split_prior = own_columns(prior_groups, span_groups, head_count, per_dest).reshape(
        head_count, reqs_dev * local_nodes, 2 * own_width
    )
    widths = [head_width, head_width, local_heads, 2 * own_width, 2 * own_width]
    bundle = jnp.concatenate(
        [split_heads, split_gates, split_steps, split_groups, split_prior.astype(jnp.bfloat16)], axis=-1
    )
    bundle = lax.all_to_all(bundle, "head", split_axis=0, concat_axis=0, tiled=True)
    cuts = [0]
    for width in widths:
        cuts.append(cuts[-1] + width)
    pieces = [bundle[..., cuts[n] : cuts[n + 1]] for n in range(len(widths))]
    head_rows = pieces[0].reshape(reqs_dev, NODES, head_width)
    gate_rows = pieces[1].reshape(reqs_dev, NODES, span_groups, span_heads, HEAD_DIM)
    step_rows = pieces[2].reshape(reqs_dev, NODES, local_heads)
    group_rows = pieces[3].reshape(reqs_dev, NODES, 2 * own_width)
    prior_own = jnp.moveaxis(
        pieces[4].reshape(head_count, reqs_dev, local_nodes, 2 * own_width), 0, 1
    ).reshape(reqs_dev, NODES, 2 * own_width)
    tail_groups = jnp.einsum(
        "bij,bjc->bic", tail_pick, prior_own, preferred_element_type=jnp.float32
    ).astype(jnp.bfloat16)
    new_part = jnp.concatenate([tail_heads, tail_groups], axis=-1).reshape(reqs_dev, -1)
    old_part = jnp.concatenate(
        [group_rows[..., own_width:], new_tree.astype(jnp.bfloat16)], axis=-1
    ).reshape(reqs_dev, -1)
    new_len = new_part.shape[-1]
    exchange = jnp.concatenate(
        [spread(send_hot, new_part), spread(recv_hot, old_part)],
        axis=-1,
    )
    exchange = lax.all_to_all(exchange, "req", split_axis=0, concat_axis=0, tiled=True)
    tails_new = (
        gather_back(recv_hot, exchange[:, :new_len]).astype(jnp.bfloat16).reshape(reqs_dev, 3, -1)
    )
    rows_old = (
        gather_back(send_hot, exchange[:, new_len:]).astype(jnp.bfloat16).reshape(reqs_dev, NODES, -1)
    )
    tree_old = rows_old[..., own_width:].astype(jnp.int32)
    kernel_own = own_columns(kernel_groups, span_groups, head_count, per_dest)[head_index]
    shift_own = own_columns(shift_groups, span_groups, head_count, per_dest)[head_index]
    query_old = tree_conv(
        rows_old[..., :own_width],
        tail_groups[..., own_width:],
        tree_old,
        kernel_own[:, own_width:],
        shift_own[own_width:],
    ).reshape(reqs_dev, NODES, span_groups, STATE)
    carried_old = jnp.einsum(
        "btn,bmn->btm",
        query_old.reshape(reqs_dev, NODES, STATE),
        carry_state.reshape(reqs_dev, head_width, STATE),
        preferred_element_type=jnp.float32,
    ).reshape(reqs_dev, NODES * head_width)
    carried_moved = lax.all_to_all(
        spread(send_hot, carried_old.astype(jnp.bfloat16)), "req", split_axis=0, concat_axis=0, tiled=True
    )
    carried = gather_back(recv_hot, carried_moved).reshape(reqs_dev, NODES, head_width).reshape(reqs_dev, NODES, span_groups, span_heads, HEAD_DIM)
    conv_heads = tree_conv(
        head_rows, tails_new[..., :head_width], new_tree, kernel_heads, shift_heads
    )
    conv_groups = tree_conv(
        group_rows, tails_new[..., head_width:], new_tree, kernel_own, shift_own
    )
    own_keys = conv_groups[..., :own_width]
    own_queries = conv_groups[..., own_width:]
    query_four = own_queries.reshape(reqs_dev, NODES, span_groups, STATE)
    key_four = own_keys.reshape(reqs_dev, NODES, span_groups, STATE)
    step_sizes = jax.nn.softplus(step_rows.astype(jnp.float32) + step_bias)
    decay_sum = jnp.einsum(
        "btj,bjh->bth", new_tree.astype(jnp.float32), step_sizes * decay_rates, precision=highest
    )
    intersection = jnp.einsum(
        "btgn,bjgn->btjg", query_four, key_four, preferred_element_type=jnp.float32
    )
    lineage_new = (new_tree == 1)[:, :, :, None]
    decay_gap = decay_sum[:, :, None, :] - decay_sum[:, None, :, :]
    decays = jnp.where(lineage_new, jnp.exp(jnp.where(lineage_new, decay_gap, 0.0)), 0.0)
    mixing = (
        decays.reshape(reqs_dev, NODES, NODES, span_groups, span_heads)
        * intersection[..., None]
        * step_sizes.reshape(reqs_dev, 1, NODES, span_groups, span_heads)
    ).astype(jnp.bfloat16)
    values = conv_heads.reshape(reqs_dev, NODES, span_groups, span_heads, HEAD_DIM)
    inner_part = jnp.einsum(
        "btjgq,bjgqp->btgqp", mixing, values, preferred_element_type=jnp.float32
    )
    output = (
        inner_part
        + jnp.exp(decay_sum).reshape(reqs_dev, NODES, span_groups, span_heads, 1) * carried
        + skip_gain.reshape(1, 1, span_groups, span_heads, 1) * values.astype(jnp.float32)
    )
    gated_out = output * jax.nn.silu(gate_rows.astype(jnp.float32))
    group_power = jnp.sum(gated_out * gated_out, axis=(3, 4))
    if per_dest == 2:
        partner = [(d, d ^ 1) for d in range(head_count)]
        power_own = group_power + lax.ppermute(group_power, "head", partner)
    else:
        zero_index = jnp.zeros((), jnp.int32)
        power_full = lax.dynamic_update_slice(
            jnp.zeros((reqs_dev, NODES, GROUPS), jnp.float32),
            group_power,
            (zero_index, zero_index, first_group),
        )
        power_total = lax.psum(power_full, "head")
        power_own = lax.dynamic_slice_in_dim(power_total, first_group, span_groups, 2)
    scale_factor = lax.rsqrt(power_own / (per_group * HEAD_DIM) + EPSILON)
    normed = (
        gated_out
        * scale_factor[..., None, None]
        * norm_gain.reshape(1, 1, span_groups, span_heads, HEAD_DIM)
    )
    return normed.reshape(reqs_dev * NODES, local_heads * HEAD_DIM).astype(jnp.bfloat16)


def solution(mesh):
    placed = (
        P(("req", "head"), None),
        P(("req", "head"), None),
        P(("req", "head"), None),
        P(("req", "head"), None),
        P("req", None, None),
        P(None, "head"),
        P("head"),
        P(),
        P(),
        P("head"),
        P("head"),
        P("head"),
        P("head"),
        P("req", "head", None, None),
        P("req", None, "head"),
        P("req", None, None),
        P("req", None, "head"),
        P("req", None, "head"),
        P("req", "head", None),
        P("req", None, None),
        P("req"),
        P(),
    )
    return jax.shard_map(
        shards, mesh=mesh, in_specs=placed, out_specs=P("req", "head"), check_vma=False
    )
```

```python
import jax
import jax.numpy as jnp
from jax import lax
from jax.sharding import PartitionSpec as P

HEADS = 256
HEAD_DIM = 64
STATE = 256
GROUPS = 8
NODES = 32
MOST = 2


EPSILON = 1e-05


def tree_conv(tree_rows, tail_rows, ancestry, weight, offset_bias):
    node_depth = jnp.sum(ancestry, axis=-1) - 1
    places = jnp.arange(3, dtype=jnp.int32)
    summed = weight[3].astype(jnp.float32) * tree_rows.astype(jnp.float32) + offset_bias
    for upward in range(1, 4):
        picked = (
            (ancestry == 1) & (node_depth[:, None, :] == node_depth[:, :, None] - upward)
        ).astype(jnp.bfloat16)
        older_rows = (places[None, None, :] == node_depth[:, :, None] - upward + 3).astype(
            jnp.bfloat16
        )
        shifted = jnp.einsum("btj,bjc->btc", picked, tree_rows, preferred_element_type=jnp.float32)
        shifted = shifted + jnp.einsum(
            "bti,bic->btc", older_rows, tail_rows, preferred_element_type=jnp.float32
        )
        summed = summed + weight[3 - upward].astype(jnp.float32) * shifted
    return jax.nn.silu(summed).astype(jnp.bfloat16)


def place_slots(payload, positions, count):
    wanted = jnp.arange(count, dtype=jnp.int32)
    owners = jnp.arange(positions.shape[0], dtype=jnp.int32)
    hits = positions[None, :] == wanted[:, None]
    chosen = jnp.sum(jnp.where(hits, owners[None, :], 0), axis=1)
    filled = jnp.any(hits, axis=1).reshape((count,) + (1,) * (payload.ndim - 1))
    taken = jnp.take(payload, chosen, axis=0)
    return jnp.where(filled, taken, jnp.zeros_like(taken))


def own_columns(rows, span_groups, dest_count, per_dest):
    lead = rows.shape[:-1]
    split = rows.reshape(lead + (2, GROUPS, STATE))
    moved = jnp.moveaxis(split, -2, 0)
    picks = (jnp.arange(dest_count, dtype=jnp.int32) // per_dest)[:, None] * span_groups + jnp.arange(
        span_groups, dtype=jnp.int32
    )[None, :]
    taken = jnp.take(moved, picks.reshape(-1), axis=0).reshape((dest_count, span_groups) + lead + (2, STATE))
    return jnp.moveaxis(taken, 1, -2).reshape((dest_count,) + lead + (2 * span_groups * STATE,))


def shards(
    tree_heads,
    tree_gates,
    tree_steps,
    tree_groups,
    new_tree,
    kernel_heads,
    shift_heads,
    kernel_groups,
    shift_groups,
    log_rates,
    step_bias,
    skip_gain,
    norm_gain,
    old_state,
    old_heads,
    old_keys,
    old_steps,
    prior_heads,
    prior_groups,
    old_tree,
    accepted,
    new_owner,
):
    req_count = lax.axis_size("req")
    head_count = lax.axis_size("head")
    req_index = lax.axis_index("req")
    head_index = lax.axis_index("head")
    reqs_dev = new_tree.shape[0]
    local_heads = log_rates.shape[0]
    local_nodes = prior_groups.shape[1]
    per_group = HEADS // GROUPS
    span_heads = min(local_heads, per_group)
    span_groups = local_heads // span_heads
    per_dest = per_group // span_heads
    assert span_groups == 1
    first_group = head_index * local_heads // per_group
    slot_count = req_count * MOST
    own_width = span_groups * STATE
    highest = lax.Precision.HIGHEST
    owner_table = new_owner.reshape(req_count, reqs_dev)
    target_dev = owner_table // reqs_dev
    local_ids = jnp.arange(reqs_dev, dtype=jnp.int32)
    before = local_ids[None, :, None] > local_ids[None, None, :]
    same_dest = target_dev[:, :, None] == target_dev[:, None, :]
    arrival = jnp.sum((same_dest & before).astype(jnp.int32), axis=-1)
    send_table = target_dev * MOST + arrival
    send_pos = lax.dynamic_index_in_dim(send_table, req_index, 0, keepdims=False)
    wanted_slot = req_index * reqs_dev + local_ids
    all_ids = jnp.arange(new_owner.shape[0], dtype=jnp.int32)
    match = new_owner[None, :] == wanted_slot[:, None]
    anchor = jnp.sum(jnp.where(match, all_ids[None, :], 0), axis=1)
    recv_pos = anchor // reqs_dev * MOST + jnp.take(arrival.reshape(-1), anchor)

    slot_ids = jnp.arange(slot_count, dtype=jnp.int32)
    send_hot = (send_pos[None, :] == slot_ids[:, None]).astype(jnp.bfloat16)
    recv_hot = (recv_pos[None, :] == slot_ids[:, None]).astype(jnp.bfloat16)

    def spread(hot, payload):
        return jnp.einsum(
            "pa,a...->p...", hot, payload, preferred_element_type=jnp.float32
        ).astype(jnp.bfloat16)

    def gather_back(hot, moved):
        return jnp.einsum("pa,p...->a...", hot, moved, preferred_element_type=jnp.float32)

    decay_rates = -jnp.exp(log_rates)
    node_ids = jnp.arange(NODES, dtype=jnp.int32)
    chosen_hot = node_ids[None, :] == accepted[:, None]
    chosen_row = jnp.sum(jnp.where(chosen_hot[:, :, None], old_tree, 0), axis=1)
    old_depth = jnp.sum(old_tree, axis=-1) - 1
    chosen_depth = jnp.sum(jnp.where(chosen_hot, old_depth, 0), axis=1)
    places = jnp.arange(3, dtype=jnp.int32)
    lineage = chosen_row == 1
    tail_pick = (
        lineage[:, None, :]
        & (old_depth[:, None, :] == chosen_depth[:, None, None] - 2 + places[None, :, None])
    ).astype(jnp.bfloat16)
    tail_heads = jnp.einsum(
        "bij,bjc->bic", tail_pick, prior_heads, preferred_element_type=jnp.float32
    ).astype(jnp.bfloat16)
    old_sums = jnp.einsum(
        "btj,bjh->bth", old_tree.astype(jnp.float32), old_steps * decay_rates, precision=highest
    )
    chosen_sum = jnp.sum(jnp.where(chosen_hot[:, :, None], old_sums, 0.0), axis=1)
    kept_weight = (
        jnp.where(
            lineage[:, :, None],
            jnp.exp(jnp.where(lineage[:, :, None], chosen_sum[:, None, :] - old_sums, 0.0)),
            0.0,
        )
        * old_steps
    )
    weighted = (
        (
            kept_weight[..., None]
            * old_heads.reshape(reqs_dev, NODES, local_heads, HEAD_DIM).astype(jnp.float32)
        )
        .astype(jnp.bfloat16)
        .reshape(reqs_dev, NODES, span_groups, span_heads, HEAD_DIM)
    )
    key_slice = lax.dynamic_slice_in_dim(
        old_keys, first_group * STATE, span_groups * STATE, 2
    ).reshape(reqs_dev, NODES, span_groups, STATE)
    update = jnp.einsum(
        "bjgqp,bjgn->bgqpn", weighted, key_slice, preferred_element_type=jnp.float32
    )
    carry_state = (
        jnp.exp(chosen_sum).reshape(reqs_dev, span_groups, span_heads, 1, 1)
        * old_state.reshape(reqs_dev, span_groups, span_heads, HEAD_DIM, STATE).astype(jnp.float32)
        + update
    ).astype(jnp.bfloat16)
    carry_state = lax.optimization_barrier(carry_state)
    tree_rows = tree_heads.shape[0]
    head_width = local_heads * HEAD_DIM
    split_heads = jnp.moveaxis(tree_heads.reshape(tree_rows, head_count, head_width), 1, 0)
    split_gates = jnp.moveaxis(tree_gates.reshape(tree_rows, head_count, head_width), 1, 0)
    split_steps = jnp.moveaxis(tree_steps.reshape(tree_rows, head_count, local_heads), 1, 0)
    split_groups = own_columns(tree_groups, span_groups, head_count, per_dest)
    split_prior = own_columns(prior_groups, span_groups, head_count, per_dest).reshape(
        head_count, reqs_dev * local_nodes, 2 * own_width
    )
    widths = [head_width, head_width, local_heads, 2 * own_width, 2 * own_width]
    bundle = jnp.concatenate(
        [split_heads, split_gates, split_steps, split_groups, split_prior.astype(jnp.bfloat16)], axis=-1
    )
    bundle = lax.all_to_all(bundle, "head", split_axis=0, concat_axis=0, tiled=True)
    cuts = [0]
    for width in widths:
        cuts.append(cuts[-1] + width)
    pieces = [bundle[..., cuts[n] : cuts[n + 1]] for n in range(len(widths))]
    head_rows = pieces[0].reshape(reqs_dev, NODES, head_width)
    gate_rows = pieces[1].reshape(reqs_dev, NODES, span_groups, span_heads, HEAD_DIM)
    step_rows = pieces[2].reshape(reqs_dev, NODES, local_heads)
    group_rows = pieces[3].reshape(reqs_dev, NODES, 2 * own_width)
    prior_own = jnp.moveaxis(
        pieces[4].reshape(head_count, reqs_dev, local_nodes, 2 * own_width), 0, 1
    ).reshape(reqs_dev, NODES, 2 * own_width)
    tail_groups = jnp.einsum(
        "bij,bjc->bic", tail_pick, prior_own, preferred_element_type=jnp.float32
    ).astype(jnp.bfloat16)
    new_part = jnp.concatenate([tail_heads, tail_groups], axis=-1).reshape(reqs_dev, NODES, -1)
    old_part = jnp.concatenate(
        [group_rows[..., own_width:], new_tree.astype(jnp.bfloat16)], axis=-1
    )
    new_len = new_part.shape[-1]
    exchange = jnp.concatenate(
        [spread(send_hot, new_part), spread(recv_hot, old_part)],
        axis=-1,
    )
    exchange = lax.all_to_all(exchange, "req", split_axis=0, concat_axis=0, tiled=True)
    tails_new = (
        gather_back(recv_hot, exchange[..., :new_len]).astype(jnp.bfloat16).reshape(reqs_dev, 3, -1)
    )
    rows_old = gather_back(send_hot, exchange[..., new_len:]).astype(jnp.bfloat16)
    tree_old = rows_old[..., own_width:].astype(jnp.int32)
    kernel_own = own_columns(kernel_groups, span_groups, head_count, per_dest)[head_index]
    shift_own = own_columns(shift_groups, span_groups, head_count, per_dest)[head_index]
    query_old = tree_conv(
        rows_old[..., :own_width],
        tail_groups[..., own_width:],
        tree_old,
        kernel_own[:, own_width:],
        shift_own[own_width:],
    ).reshape(reqs_dev, NODES, span_groups, STATE)
    carried_old = jnp.einsum(
        "btn,bmn->btm",
        query_old.reshape(reqs_dev, NODES, STATE),
        carry_state.reshape(reqs_dev, head_width, STATE),
        preferred_element_type=jnp.float32,
    )
    carried_moved = lax.all_to_all(
        spread(send_hot, carried_old.astype(jnp.bfloat16)), "req", split_axis=0, concat_axis=0, tiled=True
    )
    carried = gather_back(recv_hot, carried_moved).reshape(reqs_dev, NODES, span_groups, span_heads, HEAD_DIM)
    conv_heads = tree_conv(
        head_rows, tails_new[..., :head_width], new_tree, kernel_heads, shift_heads
    )
    conv_groups = tree_conv(
        group_rows, tails_new[..., head_width:], new_tree, kernel_own, shift_own
    )
    own_keys = conv_groups[..., :own_width]
    own_queries = conv_groups[..., own_width:]
    query_four = own_queries.reshape(reqs_dev, NODES, span_groups, STATE)
    key_four = own_keys.reshape(reqs_dev, NODES, span_groups, STATE)
    step_sizes = jax.nn.softplus(step_rows.astype(jnp.float32) + step_bias)
    decay_sum = jnp.einsum(
        "btj,bjh->bth", new_tree.astype(jnp.float32), step_sizes * decay_rates, precision=highest
    )
    intersection = jnp.einsum(
        "btgn,bjgn->btjg", query_four, key_four, preferred_element_type=jnp.float32
    )
    lineage_new = (new_tree == 1)[:, :, :, None]
    decay_gap = decay_sum[:, :, None, :] - decay_sum[:, None, :, :]
    decays = jnp.where(lineage_new, jnp.exp(jnp.where(lineage_new, decay_gap, 0.0)), 0.0)
    mixing = (
        decays.reshape(reqs_dev, NODES, NODES, span_groups, span_heads)
        * intersection[..., None]
        * step_sizes.reshape(reqs_dev, 1, NODES, span_groups, span_heads)
    ).astype(jnp.bfloat16)
    values = conv_heads.reshape(reqs_dev, NODES, span_groups, span_heads, HEAD_DIM)
    inner_part = jnp.einsum(
        "btjgq,bjgqp->btgqp", mixing, values, preferred_element_type=jnp.float32
    )
    output = (
        inner_part
        + jnp.exp(decay_sum).reshape(reqs_dev, NODES, span_groups, span_heads, 1) * carried
        + skip_gain.reshape(1, 1, span_groups, span_heads, 1) * values.astype(jnp.float32)
    )
    gated_out = output * jax.nn.silu(gate_rows.astype(jnp.float32))
    group_power = jnp.sum(gated_out * gated_out, axis=(3, 4))
    if per_dest == 2:
        partner = [(d, d ^ 1) for d in range(head_count)]
        power_own = group_power + lax.ppermute(group_power, "head", partner)
    else:
        zero_index = jnp.zeros((), jnp.int32)
        power_full = lax.dynamic_update_slice(
            jnp.zeros((reqs_dev, NODES, GROUPS), jnp.float32),
            group_power,
            (zero_index, zero_index, first_group),
        )
        power_total = lax.psum(power_full, "head")
        power_own = lax.dynamic_slice_in_dim(power_total, first_group, span_groups, 2)
    scale_factor = lax.rsqrt(power_own / (per_group * HEAD_DIM) + EPSILON)
    normed = (
        gated_out
        * scale_factor[..., None, None]
        * norm_gain.reshape(1, 1, span_groups, span_heads, HEAD_DIM)
    )
    return normed.reshape(reqs_dev * NODES, local_heads * HEAD_DIM).astype(jnp.bfloat16)


def solution(mesh):
    placed = (
        P(("req", "head"), None),
        P(("req", "head"), None),
        P(("req", "head"), None),
        P(("req", "head"), None),
        P("req", None, None),
        P(None, "head"),
        P("head"),
        P(),
        P(),
        P("head"),
        P("head"),
        P("head"),
        P("head"),
        P("req", "head", None, None),
        P("req", None, "head"),
        P("req", None, None),
        P("req", None, "head"),
        P("req", None, "head"),
        P("req", "head", None),
        P("req", None, None),
        P("req"),
        P(),
    )
    return jax.shard_map(
        shards, mesh=mesh, in_specs=placed, out_specs=P("req", "head"), check_vma=False
    )
```

```python
import jax
import jax.numpy as jnp
from jax import lax
from jax.sharding import PartitionSpec as P

HEADS = 256
HEAD_DIM = 64
STATE = 256
GROUPS = 8
NODES = 32
MOST = 2


EPSILON = 1e-05


def tree_conv(tree_rows, tail_rows, ancestry, weight, offset_bias):
    node_depth = jnp.sum(ancestry, axis=-1) - 1
    places = jnp.arange(3, dtype=jnp.int32)
    summed = weight[3].astype(jnp.float32) * tree_rows.astype(jnp.float32) + offset_bias
    for upward in range(1, 4):
        picked = (
            (ancestry == 1) & (node_depth[:, None, :] == node_depth[:, :, None] - upward)
        ).astype(jnp.bfloat16)
        older_rows = (places[None, None, :] == node_depth[:, :, None] - upward + 3).astype(
            jnp.bfloat16
        )
        shifted = jnp.einsum("btj,bjc->btc", picked, tree_rows, preferred_element_type=jnp.float32)
        shifted = shifted + jnp.einsum(
            "bti,bic->btc", older_rows, tail_rows, preferred_element_type=jnp.float32
        )
        summed = summed + weight[3 - upward].astype(jnp.float32) * shifted
    return jax.nn.silu(summed).astype(jnp.bfloat16)


def place_slots(payload, positions, count):
    wanted = jnp.arange(count, dtype=jnp.int32)
    owners = jnp.arange(positions.shape[0], dtype=jnp.int32)
    hits = positions[None, :] == wanted[:, None]
    chosen = jnp.sum(jnp.where(hits, owners[None, :], 0), axis=1)
    filled = jnp.any(hits, axis=1).reshape((count,) + (1,) * (payload.ndim - 1))
    taken = jnp.take(payload, chosen, axis=0)
    return jnp.where(filled, taken, jnp.zeros_like(taken))


def own_columns(rows, span_groups, dest_count, per_dest):
    lead = rows.shape[:-1]
    split = rows.reshape(lead + (2, GROUPS, STATE))
    moved = jnp.moveaxis(split, -2, 0)
    picks = (jnp.arange(dest_count, dtype=jnp.int32) // per_dest)[:, None] * span_groups + jnp.arange(
        span_groups, dtype=jnp.int32
    )[None, :]
    taken = jnp.take(moved, picks.reshape(-1), axis=0).reshape((dest_count, span_groups) + lead + (2, STATE))
    return jnp.moveaxis(taken, 1, -2).reshape((dest_count,) + lead + (2 * span_groups * STATE,))


def shards(
    tree_heads,
    tree_gates,
    tree_steps,
    tree_groups,
    new_tree,
    kernel_heads,
    shift_heads,
    kernel_groups,
    shift_groups,
    log_rates,
    step_bias,
    skip_gain,
    norm_gain,
    old_state,
    old_heads,
    old_keys,
    old_steps,
    prior_heads,
    prior_groups,
    old_tree,
    accepted,
    new_owner,
):
    req_count = lax.axis_size("req")
    head_count = lax.axis_size("head")
    req_index = lax.axis_index("req")
    head_index = lax.axis_index("head")
    reqs_dev = new_tree.shape[0]
    local_heads = log_rates.shape[0]
    local_nodes = prior_groups.shape[1]
    per_group = HEADS // GROUPS
    span_heads = min(local_heads, per_group)
    span_groups = local_heads // span_heads
    per_dest = per_group // span_heads
    assert span_groups == 1
    first_group = head_index * local_heads // per_group
    slot_count = req_count * MOST
    own_width = span_groups * STATE
    highest = lax.Precision.HIGHEST
    owner_table = new_owner.reshape(req_count, reqs_dev)
    target_dev = owner_table // reqs_dev
    local_ids = jnp.arange(reqs_dev, dtype=jnp.int32)
    before = local_ids[None, :, None] > local_ids[None, None, :]
    same_dest = target_dev[:, :, None] == target_dev[:, None, :]
    arrival = jnp.sum((same_dest & before).astype(jnp.int32), axis=-1)
    send_table = target_dev * MOST + arrival
    send_pos = lax.dynamic_index_in_dim(send_table, req_index, 0, keepdims=False)
    wanted_slot = req_index * reqs_dev + local_ids
    all_ids = jnp.arange(new_owner.shape[0], dtype=jnp.int32)
    match = new_owner[None, :] == wanted_slot[:, None]
    anchor = jnp.sum(jnp.where(match, all_ids[None, :], 0), axis=1)
    recv_pos = anchor // reqs_dev * MOST + jnp.take(arrival.reshape(-1), anchor)

    slot_ids = jnp.arange(slot_count, dtype=jnp.int32)
    send_hot = (send_pos[None, :] == slot_ids[:, None]).astype(jnp.bfloat16)
    recv_hot = (recv_pos[None, :] == slot_ids[:, None]).astype(jnp.bfloat16)

    def spread(hot, payload):
        return jnp.einsum(
            "pa,a...->p...", hot, payload, preferred_element_type=jnp.float32
        ).astype(jnp.bfloat16)

    def gather_back(hot, moved):
        return jnp.einsum("pa,p...->a...", hot, moved, preferred_element_type=jnp.float32)

    decay_rates = -jnp.exp(log_rates)
    node_ids = jnp.arange(NODES, dtype=jnp.int32)
    chosen_hot = node_ids[None, :] == accepted[:, None]
    chosen_row = jnp.sum(jnp.where(chosen_hot[:, :, None], old_tree, 0), axis=1)
    old_depth = jnp.sum(old_tree, axis=-1) - 1
    chosen_depth = jnp.sum(jnp.where(chosen_hot, old_depth, 0), axis=1)
    places = jnp.arange(3, dtype=jnp.int32)
    lineage = chosen_row == 1
    tail_pick = (
        lineage[:, None, :]
        & (old_depth[:, None, :] == chosen_depth[:, None, None] - 2 + places[None, :, None])
    ).astype(jnp.bfloat16)
    tail_heads = jnp.einsum(
        "bij,bjc->bic", tail_pick, prior_heads, preferred_element_type=jnp.float32
    ).astype(jnp.bfloat16)
    old_sums = jnp.einsum(
        "btj,bjh->bth", old_tree.astype(jnp.float32), old_steps * decay_rates, precision=highest
    )
    chosen_sum = jnp.sum(jnp.where(chosen_hot[:, :, None], old_sums, 0.0), axis=1)
    kept_weight = (
        jnp.where(
            lineage[:, :, None],
            jnp.exp(jnp.where(lineage[:, :, None], chosen_sum[:, None, :] - old_sums, 0.0)),
            0.0,
        )
        * old_steps
    )
    weighted = (
        (
            kept_weight[..., None]
            * old_heads.reshape(reqs_dev, NODES, local_heads, HEAD_DIM).astype(jnp.float32)
        )
        .astype(jnp.bfloat16)
        .reshape(reqs_dev, NODES, span_groups, span_heads, HEAD_DIM)
    )
    key_slice = lax.dynamic_slice_in_dim(
        old_keys, first_group * STATE, span_groups * STATE, 2
    ).reshape(reqs_dev, NODES, span_groups, STATE)
    update = jnp.einsum(
        "bjgqp,bjgn->bgqpn", weighted, key_slice, preferred_element_type=jnp.float32
    )
    carry_state = (
        jnp.exp(chosen_sum).reshape(reqs_dev, span_groups, span_heads, 1, 1)
        * old_state.reshape(reqs_dev, span_groups, span_heads, HEAD_DIM, STATE).astype(jnp.float32)
        + update
    ).astype(jnp.bfloat16)
    carry_state = lax.optimization_barrier(carry_state)
    tree_rows = tree_heads.shape[0]
    head_width = local_heads * HEAD_DIM
    split_heads = jnp.moveaxis(tree_heads.reshape(tree_rows, head_count, head_width), 1, 0)
    split_gates = jnp.moveaxis(tree_gates.reshape(tree_rows, head_count, head_width), 1, 0)
    split_steps = jnp.moveaxis(tree_steps.reshape(tree_rows, head_count, local_heads), 1, 0)
    split_groups = own_columns(tree_groups, span_groups, head_count, per_dest)
    split_prior = own_columns(prior_groups, span_groups, head_count, per_dest).reshape(
        head_count, reqs_dev * local_nodes, 2 * own_width
    )
    widths = [head_width, head_width, local_heads, 2 * own_width, 2 * own_width]
    bundle = jnp.concatenate(
        [split_heads, split_gates, split_steps, split_groups, split_prior.astype(jnp.bfloat16)], axis=-1
    )
    source_ids = jnp.arange(head_count, dtype=jnp.int32)
    rolled = jnp.take(bundle, (head_index + source_ids) % head_count, axis=0)
    arrived = [rolled[0]]
    for shift in range(1, head_count):
        arrived.append(
            lax.ppermute(
                rolled[shift], "head", [(d, (d + shift) % head_count) for d in range(head_count)]
            )
        )
    arrived = jnp.stack(arrived, axis=0)
    bundle = jnp.take(arrived, (head_index - source_ids) % head_count, axis=0)
    cuts = [0]
    for width in widths:
        cuts.append(cuts[-1] + width)
    pieces = [bundle[..., cuts[n] : cuts[n + 1]] for n in range(len(widths))]
    head_rows = pieces[0].reshape(reqs_dev, NODES, head_width)
    gate_rows = pieces[1].reshape(reqs_dev, NODES, span_groups, span_heads, HEAD_DIM)
    step_rows = pieces[2].reshape(reqs_dev, NODES, local_heads)
    group_rows = pieces[3].reshape(reqs_dev, NODES, 2 * own_width)
    prior_own = jnp.moveaxis(
        pieces[4].reshape(head_count, reqs_dev, local_nodes, 2 * own_width), 0, 1
    ).reshape(reqs_dev, NODES, 2 * own_width)
    tail_groups = jnp.einsum(
        "bij,bjc->bic", tail_pick, prior_own, preferred_element_type=jnp.float32
    ).astype(jnp.bfloat16)
    new_part = jnp.concatenate([tail_heads, tail_groups], axis=-1).reshape(reqs_dev, NODES, -1)
    old_part = jnp.concatenate(
        [group_rows[..., own_width:], new_tree.astype(jnp.bfloat16)], axis=-1
    )
    new_len = new_part.shape[-1]
    exchange = jnp.concatenate(
        [spread(send_hot, new_part), spread(recv_hot, old_part)],
        axis=-1,
    )
    exchange = lax.all_to_all(exchange, "req", split_axis=0, concat_axis=0, tiled=True)
    tails_new = (
        gather_back(recv_hot, exchange[..., :new_len]).astype(jnp.bfloat16).reshape(reqs_dev, 3, -1)
    )
    rows_old = gather_back(send_hot, exchange[..., new_len:]).astype(jnp.bfloat16)
    tree_old = rows_old[..., own_width:].astype(jnp.int32)
    kernel_own = own_columns(kernel_groups, span_groups, head_count, per_dest)[head_index]
    shift_own = own_columns(shift_groups, span_groups, head_count, per_dest)[head_index]
    query_old = tree_conv(
        rows_old[..., :own_width],
        tail_groups[..., own_width:],
        tree_old,
        kernel_own[:, own_width:],
        shift_own[own_width:],
    ).reshape(reqs_dev, NODES, span_groups, STATE)
    carried_old = jnp.einsum(
        "btn,bmn->btm",
        query_old.reshape(reqs_dev, NODES, STATE),
        carry_state.reshape(reqs_dev, head_width, STATE),
        preferred_element_type=jnp.float32,
    )
    carried_moved = lax.all_to_all(
        spread(send_hot, carried_old.astype(jnp.bfloat16)), "req", split_axis=0, concat_axis=0, tiled=True
    )
    carried = gather_back(recv_hot, carried_moved).reshape(reqs_dev, NODES, span_groups, span_heads, HEAD_DIM)
    conv_heads = tree_conv(
        head_rows, tails_new[..., :head_width], new_tree, kernel_heads, shift_heads
    )
    conv_groups = tree_conv(
        group_rows, tails_new[..., head_width:], new_tree, kernel_own, shift_own
    )
    own_keys = conv_groups[..., :own_width]
    own_queries = conv_groups[..., own_width:]
    query_four = own_queries.reshape(reqs_dev, NODES, span_groups, STATE)
    key_four = own_keys.reshape(reqs_dev, NODES, span_groups, STATE)
    step_sizes = jax.nn.softplus(step_rows.astype(jnp.float32) + step_bias)
    decay_sum = jnp.einsum(
        "btj,bjh->bth", new_tree.astype(jnp.float32), step_sizes * decay_rates, precision=highest
    )
    intersection = jnp.einsum(
        "btgn,bjgn->btjg", query_four, key_four, preferred_element_type=jnp.float32
    )
    lineage_new = (new_tree == 1)[:, :, :, None]
    decay_gap = decay_sum[:, :, None, :] - decay_sum[:, None, :, :]
    decays = jnp.where(lineage_new, jnp.exp(jnp.where(lineage_new, decay_gap, 0.0)), 0.0)
    mixing = (
        decays.reshape(reqs_dev, NODES, NODES, span_groups, span_heads)
        * intersection[..., None]
        * step_sizes.reshape(reqs_dev, 1, NODES, span_groups, span_heads)
    ).astype(jnp.bfloat16)
    values = conv_heads.reshape(reqs_dev, NODES, span_groups, span_heads, HEAD_DIM)
    inner_part = jnp.einsum(
        "btjgq,bjgqp->btgqp", mixing, values, preferred_element_type=jnp.float32
    )
    output = (
        inner_part
        + jnp.exp(decay_sum).reshape(reqs_dev, NODES, span_groups, span_heads, 1) * carried
        + skip_gain.reshape(1, 1, span_groups, span_heads, 1) * values.astype(jnp.float32)
    )
    gated_out = output * jax.nn.silu(gate_rows.astype(jnp.float32))
    group_power = jnp.sum(gated_out * gated_out, axis=(3, 4))
    if per_dest == 2:
        partner = [(d, d ^ 1) for d in range(head_count)]
        power_own = group_power + lax.ppermute(group_power, "head", partner)
    else:
        zero_index = jnp.zeros((), jnp.int32)
        power_full = lax.dynamic_update_slice(
            jnp.zeros((reqs_dev, NODES, GROUPS), jnp.float32),
            group_power,
            (zero_index, zero_index, first_group),
        )
        power_total = lax.psum(power_full, "head")
        power_own = lax.dynamic_slice_in_dim(power_total, first_group, span_groups, 2)
    scale_factor = lax.rsqrt(power_own / (per_group * HEAD_DIM) + EPSILON)
    normed = (
        gated_out
        * scale_factor[..., None, None]
        * norm_gain.reshape(1, 1, span_groups, span_heads, HEAD_DIM)
    )
    return normed.reshape(reqs_dev * NODES, local_heads * HEAD_DIM).astype(jnp.bfloat16)


def solution(mesh):
    placed = (
        P(("req", "head"), None),
        P(("req", "head"), None),
        P(("req", "head"), None),
        P(("req", "head"), None),
        P("req", None, None),
        P(None, "head"),
        P("head"),
        P(),
        P(),
        P("head"),
        P("head"),
        P("head"),
        P("head"),
        P("req", "head", None, None),
        P("req", None, "head"),
        P("req", None, None),
        P("req", None, "head"),
        P("req", None, "head"),
        P("req", "head", None),
        P("req", None, None),
        P("req"),
        P(),
    )
    return jax.shard_map(
        shards, mesh=mesh, in_specs=placed, out_specs=P("req", "head"), check_vma=False
    )
```

```python
import jax
import jax.numpy as jnp
from jax import lax
from jax.sharding import PartitionSpec as P

HEADS = 256
HEAD_DIM = 64
STATE = 256
GROUPS = 8
NODES = 32
MOST = 2


EPSILON = 1e-05


def tree_conv(tree_rows, tail_rows, ancestry, weight, offset_bias):
    node_depth = jnp.sum(ancestry, axis=-1) - 1
    places = jnp.arange(3, dtype=jnp.int32)
    summed = weight[3].astype(jnp.float32) * tree_rows.astype(jnp.float32) + offset_bias
    for upward in range(1, 4):
        picked = (
            (ancestry == 1) & (node_depth[:, None, :] == node_depth[:, :, None] - upward)
        ).astype(jnp.bfloat16)
        older_rows = (places[None, None, :] == node_depth[:, :, None] - upward + 3).astype(
            jnp.bfloat16
        )
        shifted = jnp.einsum("btj,bjc->btc", picked, tree_rows, preferred_element_type=jnp.float32)
        shifted = shifted + jnp.einsum(
            "bti,bic->btc", older_rows, tail_rows, preferred_element_type=jnp.float32
        )
        summed = summed + weight[3 - upward].astype(jnp.float32) * shifted
    return jax.nn.silu(summed).astype(jnp.bfloat16)


def place_slots(payload, positions, count):
    wanted = jnp.arange(count, dtype=jnp.int32)
    owners = jnp.arange(positions.shape[0], dtype=jnp.int32)
    hits = positions[None, :] == wanted[:, None]
    chosen = jnp.sum(jnp.where(hits, owners[None, :], 0), axis=1)
    filled = jnp.any(hits, axis=1).reshape((count,) + (1,) * (payload.ndim - 1))
    taken = jnp.take(payload, chosen, axis=0)
    return jnp.where(filled, taken, jnp.zeros_like(taken))


def own_columns(rows, span_groups, dest_count, per_dest):
    lead = rows.shape[:-1]
    split = rows.reshape(lead + (2, GROUPS, STATE))
    moved = jnp.moveaxis(split, -2, 0)
    picks = (jnp.arange(dest_count, dtype=jnp.int32) // per_dest)[:, None] * span_groups + jnp.arange(
        span_groups, dtype=jnp.int32
    )[None, :]
    taken = jnp.take(moved, picks.reshape(-1), axis=0).reshape((dest_count, span_groups) + lead + (2, STATE))
    return jnp.moveaxis(taken, 1, -2).reshape((dest_count,) + lead + (2 * span_groups * STATE,))


def shards(
    tree_heads,
    tree_gates,
    tree_steps,
    tree_groups,
    new_tree,
    kernel_heads,
    shift_heads,
    kernel_groups,
    shift_groups,
    log_rates,
    step_bias,
    skip_gain,
    norm_gain,
    old_state,
    old_heads,
    old_keys,
    old_steps,
    prior_heads,
    prior_groups,
    old_tree,
    accepted,
    new_owner,
):
    req_count = lax.axis_size("req")
    head_count = lax.axis_size("head")
    req_index = lax.axis_index("req")
    head_index = lax.axis_index("head")
    reqs_dev = new_tree.shape[0]
    local_heads = log_rates.shape[0]
    local_nodes = prior_groups.shape[1]
    per_group = HEADS // GROUPS
    span_heads = min(local_heads, per_group)
    span_groups = local_heads // span_heads
    per_dest = per_group // span_heads
    assert span_groups == 1
    first_group = head_index * local_heads // per_group
    slot_count = req_count * MOST
    own_width = span_groups * STATE
    highest = lax.Precision.HIGHEST
    owner_table = new_owner.reshape(req_count, reqs_dev)
    target_dev = owner_table // reqs_dev
    local_ids = jnp.arange(reqs_dev, dtype=jnp.int32)
    before = local_ids[None, :, None] > local_ids[None, None, :]
    same_dest = target_dev[:, :, None] == target_dev[:, None, :]
    arrival = jnp.sum((same_dest & before).astype(jnp.int32), axis=-1)
    send_table = target_dev * MOST + arrival
    send_pos = lax.dynamic_index_in_dim(send_table, req_index, 0, keepdims=False)
    wanted_slot = req_index * reqs_dev + local_ids
    all_ids = jnp.arange(new_owner.shape[0], dtype=jnp.int32)
    match = new_owner[None, :] == wanted_slot[:, None]
    anchor = jnp.sum(jnp.where(match, all_ids[None, :], 0), axis=1)
    recv_pos = anchor // reqs_dev * MOST + jnp.take(arrival.reshape(-1), anchor)

    slot_ids = jnp.arange(slot_count, dtype=jnp.int32)
    send_hot = (send_pos[None, :] == slot_ids[:, None]).astype(jnp.bfloat16)
    recv_hot = (recv_pos[None, :] == slot_ids[:, None]).astype(jnp.bfloat16)

    def spread(hot, payload):
        return jnp.einsum(
            "pa,a...->p...", hot, payload, preferred_element_type=jnp.float32
        ).astype(jnp.bfloat16)

    def gather_back(hot, moved):
        return jnp.einsum("pa,p...->a...", hot, moved, preferred_element_type=jnp.float32)

    decay_rates = -jnp.exp(log_rates)
    node_ids = jnp.arange(NODES, dtype=jnp.int32)
    chosen_hot = node_ids[None, :] == accepted[:, None]
    chosen_row = jnp.sum(jnp.where(chosen_hot[:, :, None], old_tree, 0), axis=1)
    old_depth = jnp.sum(old_tree, axis=-1) - 1
    chosen_depth = jnp.sum(jnp.where(chosen_hot, old_depth, 0), axis=1)
    places = jnp.arange(3, dtype=jnp.int32)
    lineage = chosen_row == 1
    tail_pick = (
        lineage[:, None, :]
        & (old_depth[:, None, :] == chosen_depth[:, None, None] - 2 + places[None, :, None])
    ).astype(jnp.bfloat16)
    tail_heads = jnp.einsum(
        "bij,bjc->bic", tail_pick, prior_heads, preferred_element_type=jnp.float32
    ).astype(jnp.bfloat16)
    old_sums = jnp.einsum(
        "btj,bjh->bth", old_tree.astype(jnp.float32), old_steps * decay_rates, precision=highest
    )
    chosen_sum = jnp.sum(jnp.where(chosen_hot[:, :, None], old_sums, 0.0), axis=1)
    kept_weight = (
        jnp.where(
            lineage[:, :, None],
            jnp.exp(jnp.where(lineage[:, :, None], chosen_sum[:, None, :] - old_sums, 0.0)),
            0.0,
        )
        * old_steps
    )
    weighted = (
        (
            kept_weight[..., None]
            * old_heads.reshape(reqs_dev, NODES, local_heads, HEAD_DIM).astype(jnp.float32)
        )
        .astype(jnp.bfloat16)
        .reshape(reqs_dev, NODES, span_groups, span_heads, HEAD_DIM)
    )
    key_slice = lax.dynamic_slice_in_dim(
        old_keys, first_group * STATE, span_groups * STATE, 2
    ).reshape(reqs_dev, NODES, span_groups, STATE)
    update = jnp.einsum(
        "bjgqp,bjgn->bgqpn", weighted, key_slice, preferred_element_type=jnp.float32
    )
    carry_state = (
        jnp.exp(chosen_sum).reshape(reqs_dev, span_groups, span_heads, 1, 1)
        * old_state.reshape(reqs_dev, span_groups, span_heads, HEAD_DIM, STATE).astype(jnp.float32)
        + update
    ).astype(jnp.bfloat16)
    carry_state = lax.optimization_barrier(carry_state)
    tree_rows = tree_heads.shape[0]
    head_width = local_heads * HEAD_DIM
    split_heads = jnp.moveaxis(tree_heads.reshape(tree_rows, head_count, head_width), 1, 0)
    split_gates = jnp.moveaxis(tree_gates.reshape(tree_rows, head_count, head_width), 1, 0)
    split_steps = jnp.moveaxis(tree_steps.reshape(tree_rows, head_count, local_heads), 1, 0)
    split_groups = own_columns(tree_groups, span_groups, head_count, per_dest)
    split_prior = own_columns(prior_groups, span_groups, head_count, per_dest).reshape(
        head_count, reqs_dev * local_nodes, 2 * own_width
    )
    widths = [head_width, head_width, local_heads, 2 * own_width, 2 * own_width]
    bundle = jnp.concatenate(
        [split_heads, split_gates, split_steps, split_groups, split_prior.astype(jnp.bfloat16)], axis=-1
    )
    bundle = lax.all_to_all(bundle, "head", split_axis=0, concat_axis=0, tiled=True)
    cuts = [0]
    for width in widths:
        cuts.append(cuts[-1] + width)
    pieces = [bundle[..., cuts[n] : cuts[n + 1]] for n in range(len(widths))]
    head_rows = pieces[0].reshape(reqs_dev, NODES, head_width)
    gate_rows = pieces[1].reshape(reqs_dev, NODES, span_groups, span_heads, HEAD_DIM)
    step_rows = pieces[2].reshape(reqs_dev, NODES, local_heads)
    group_rows = pieces[3].reshape(reqs_dev, NODES, 2 * own_width)
    prior_own = jnp.moveaxis(
        pieces[4].reshape(head_count, reqs_dev, local_nodes, 2 * own_width), 0, 1
    ).reshape(reqs_dev, NODES, 2 * own_width)
    tail_groups = jnp.einsum(
        "bij,bjc->bic", tail_pick, prior_own, preferred_element_type=jnp.float32
    ).astype(jnp.bfloat16)
    tails_all = lax.all_gather(
        jnp.concatenate([tail_heads, tail_groups], axis=-1), "req", axis=0, tiled=True
    )
    tails_new = jnp.take(tails_all, anchor, axis=0)
    old_part = jnp.concatenate(
        [group_rows[..., own_width:], new_tree.astype(jnp.bfloat16)], axis=-1
    )
    exchange = lax.all_to_all(
        spread(recv_hot, old_part), "req", split_axis=0, concat_axis=0, tiled=True
    )
    rows_old = gather_back(send_hot, exchange).astype(jnp.bfloat16)
    tree_old = rows_old[..., own_width:].astype(jnp.int32)
    kernel_own = own_columns(kernel_groups, span_groups, head_count, per_dest)[head_index]
    shift_own = own_columns(shift_groups, span_groups, head_count, per_dest)[head_index]
    query_old = tree_conv(
        rows_old[..., :own_width],
        tail_groups[..., own_width:],
        tree_old,
        kernel_own[:, own_width:],
        shift_own[own_width:],
    ).reshape(reqs_dev, NODES, span_groups, STATE)
    carried_old = jnp.einsum(
        "btn,bmn->btm",
        query_old.reshape(reqs_dev, NODES, STATE),
        carry_state.reshape(reqs_dev, head_width, STATE),
        preferred_element_type=jnp.float32,
    )
    carried_moved = lax.all_to_all(
        spread(send_hot, carried_old.astype(jnp.bfloat16)), "req", split_axis=0, concat_axis=0, tiled=True
    )
    carried = gather_back(recv_hot, carried_moved).reshape(reqs_dev, NODES, span_groups, span_heads, HEAD_DIM)
    conv_heads = tree_conv(
        head_rows, tails_new[..., :head_width], new_tree, kernel_heads, shift_heads
    )
    conv_groups = tree_conv(
        group_rows, tails_new[..., head_width:], new_tree, kernel_own, shift_own
    )
    own_keys = conv_groups[..., :own_width]
    own_queries = conv_groups[..., own_width:]
    query_four = own_queries.reshape(reqs_dev, NODES, span_groups, STATE)
    key_four = own_keys.reshape(reqs_dev, NODES, span_groups, STATE)
    step_sizes = jax.nn.softplus(step_rows.astype(jnp.float32) + step_bias)
    decay_sum = jnp.einsum(
        "btj,bjh->bth", new_tree.astype(jnp.float32), step_sizes * decay_rates, precision=highest
    )
    intersection = jnp.einsum(
        "btgn,bjgn->btjg", query_four, key_four, preferred_element_type=jnp.float32
    )
    lineage_new = (new_tree == 1)[:, :, :, None]
    decay_gap = decay_sum[:, :, None, :] - decay_sum[:, None, :, :]
    decays = jnp.where(lineage_new, jnp.exp(jnp.where(lineage_new, decay_gap, 0.0)), 0.0)
    mixing = (
        decays.reshape(reqs_dev, NODES, NODES, span_groups, span_heads)
        * intersection[..., None]
        * step_sizes.reshape(reqs_dev, 1, NODES, span_groups, span_heads)
    ).astype(jnp.bfloat16)
    values = conv_heads.reshape(reqs_dev, NODES, span_groups, span_heads, HEAD_DIM)
    inner_part = jnp.einsum(
        "btjgq,bjgqp->btgqp", mixing, values, preferred_element_type=jnp.float32
    )
    output = (
        inner_part
        + jnp.exp(decay_sum).reshape(reqs_dev, NODES, span_groups, span_heads, 1) * carried
        + skip_gain.reshape(1, 1, span_groups, span_heads, 1) * values.astype(jnp.float32)
    )
    gated_out = output * jax.nn.silu(gate_rows.astype(jnp.float32))
    group_power = jnp.sum(gated_out * gated_out, axis=(3, 4))
    if per_dest == 2:
        partner = [(d, d ^ 1) for d in range(head_count)]
        power_own = group_power + lax.ppermute(group_power, "head", partner)
    else:
        zero_index = jnp.zeros((), jnp.int32)
        power_full = lax.dynamic_update_slice(
            jnp.zeros((reqs_dev, NODES, GROUPS), jnp.float32),
            group_power,
            (zero_index, zero_index, first_group),
        )
        power_total = lax.psum(power_full, "head")
        power_own = lax.dynamic_slice_in_dim(power_total, first_group, span_groups, 2)
    scale_factor = lax.rsqrt(power_own / (per_group * HEAD_DIM) + EPSILON)
    normed = (
        gated_out
        * scale_factor[..., None, None]
        * norm_gain.reshape(1, 1, span_groups, span_heads, HEAD_DIM)
    )
    return normed.reshape(reqs_dev * NODES, local_heads * HEAD_DIM).astype(jnp.bfloat16)


def solution(mesh):
    placed = (
        P(("req", "head"), None),
        P(("req", "head"), None),
        P(("req", "head"), None),
        P(("req", "head"), None),
        P("req", None, None),
        P(None, "head"),
        P("head"),
        P(),
        P(),
        P("head"),
        P("head"),
        P("head"),
        P("head"),
        P("req", "head", None, None),
        P("req", None, "head"),
        P("req", None, None),
        P("req", None, "head"),
        P("req", None, "head"),
        P("req", "head", None),
        P("req", None, None),
        P("req"),
        P(),
    )
    return jax.shard_map(
        shards, mesh=mesh, in_specs=placed, out_specs=P("req", "head"), check_vma=False
    )
```

```python
import jax
import jax.numpy as jnp
from jax import lax
from jax.sharding import PartitionSpec as P

HEADS = 256
HEAD_DIM = 64
STATE = 256
GROUPS = 8
NODES = 32
MOST = 2


EPSILON = 1e-05


def tree_conv(tree_rows, tail_rows, ancestry, weight, offset_bias):
    node_depth = jnp.sum(ancestry, axis=-1) - 1
    places = jnp.arange(3, dtype=jnp.int32)
    summed = weight[3].astype(jnp.float32) * tree_rows.astype(jnp.float32) + offset_bias
    for upward in range(1, 4):
        picked = (
            (ancestry == 1) & (node_depth[:, None, :] == node_depth[:, :, None] - upward)
        ).astype(jnp.bfloat16)
        older_rows = (places[None, None, :] == node_depth[:, :, None] - upward + 3).astype(
            jnp.bfloat16
        )
        shifted = jnp.einsum("btj,bjc->btc", picked, tree_rows, preferred_element_type=jnp.float32)
        shifted = shifted + jnp.einsum(
            "bti,bic->btc", older_rows, tail_rows, preferred_element_type=jnp.float32
        )
        summed = summed + weight[3 - upward].astype(jnp.float32) * shifted
    return jax.nn.silu(summed).astype(jnp.bfloat16)


def place_slots(payload, positions, count):
    wanted = jnp.arange(count, dtype=jnp.int32)
    owners = jnp.arange(positions.shape[0], dtype=jnp.int32)
    hits = positions[None, :] == wanted[:, None]
    chosen = jnp.sum(jnp.where(hits, owners[None, :], 0), axis=1)
    filled = jnp.any(hits, axis=1).reshape((count,) + (1,) * (payload.ndim - 1))
    taken = jnp.take(payload, chosen, axis=0)
    return jnp.where(filled, taken, jnp.zeros_like(taken))


def own_columns(rows, span_groups, dest_count, per_dest):
    lead = rows.shape[:-1]
    split = rows.reshape(lead + (2, GROUPS, STATE))
    moved = jnp.moveaxis(split, -2, 0)
    picks = (jnp.arange(dest_count, dtype=jnp.int32) // per_dest)[:, None] * span_groups + jnp.arange(
        span_groups, dtype=jnp.int32
    )[None, :]
    taken = jnp.take(moved, picks.reshape(-1), axis=0).reshape((dest_count, span_groups) + lead + (2, STATE))
    return jnp.moveaxis(taken, 1, -2).reshape((dest_count,) + lead + (2 * span_groups * STATE,))


def shards(
    tree_heads,
    tree_gates,
    tree_steps,
    tree_groups,
    new_tree,
    kernel_heads,
    shift_heads,
    kernel_groups,
    shift_groups,
    log_rates,
    step_bias,
    skip_gain,
    norm_gain,
    old_state,
    old_heads,
    old_keys,
    old_steps,
    prior_heads,
    prior_groups,
    old_tree,
    accepted,
    new_owner,
):
    req_count = lax.axis_size("req")
    head_count = lax.axis_size("head")
    req_index = lax.axis_index("req")
    head_index = lax.axis_index("head")
    reqs_dev = new_tree.shape[0]
    local_heads = log_rates.shape[0]
    local_nodes = prior_groups.shape[1]
    per_group = HEADS // GROUPS
    span_heads = min(local_heads, per_group)
    span_groups = local_heads // span_heads
    per_dest = per_group // span_heads
    assert span_groups == 1
    first_group = head_index * local_heads // per_group
    slot_count = req_count * MOST
    own_width = span_groups * STATE
    highest = lax.Precision.HIGHEST
    owner_table = new_owner.reshape(req_count, reqs_dev)
    target_dev = owner_table // reqs_dev
    local_ids = jnp.arange(reqs_dev, dtype=jnp.int32)
    before = local_ids[None, :, None] > local_ids[None, None, :]
    same_dest = target_dev[:, :, None] == target_dev[:, None, :]
    arrival = jnp.sum((same_dest & before).astype(jnp.int32), axis=-1)
    send_table = target_dev * MOST + arrival
    send_pos = lax.dynamic_index_in_dim(send_table, req_index, 0, keepdims=False)
    wanted_slot = req_index * reqs_dev + local_ids
    all_ids = jnp.arange(new_owner.shape[0], dtype=jnp.int32)
    match = new_owner[None, :] == wanted_slot[:, None]
    anchor = jnp.sum(jnp.where(match, all_ids[None, :], 0), axis=1)
    recv_pos = anchor // reqs_dev * MOST + jnp.take(arrival.reshape(-1), anchor)

    slot_ids = jnp.arange(slot_count, dtype=jnp.int32)
    send_hot = (send_pos[None, :] == slot_ids[:, None]).astype(jnp.bfloat16)
    recv_hot = (recv_pos[None, :] == slot_ids[:, None]).astype(jnp.bfloat16)

    def spread(hot, payload):
        return jnp.einsum(
            "pa,a...->p...", hot, payload, preferred_element_type=jnp.float32
        ).astype(jnp.bfloat16)

    def gather_back(hot, moved):
        return jnp.einsum("pa,p...->a...", hot, moved, preferred_element_type=jnp.float32)

    decay_rates = -jnp.exp(log_rates)
    node_ids = jnp.arange(NODES, dtype=jnp.int32)
    chosen_hot = node_ids[None, :] == accepted[:, None]
    chosen_row = jnp.sum(jnp.where(chosen_hot[:, :, None], old_tree, 0), axis=1)
    old_depth = jnp.sum(old_tree, axis=-1) - 1
    chosen_depth = jnp.sum(jnp.where(chosen_hot, old_depth, 0), axis=1)
    places = jnp.arange(3, dtype=jnp.int32)
    lineage = chosen_row == 1
    tail_pick = (
        lineage[:, None, :]
        & (old_depth[:, None, :] == chosen_depth[:, None, None] - 2 + places[None, :, None])
    ).astype(jnp.bfloat16)
    tail_heads = jnp.einsum(
        "bij,bjc->bic", tail_pick, prior_heads, preferred_element_type=jnp.float32
    ).astype(jnp.bfloat16)
    old_sums = jnp.einsum(
        "btj,bjh->bth", old_tree.astype(jnp.float32), old_steps * decay_rates, precision=highest
    )
    chosen_sum = jnp.sum(jnp.where(chosen_hot[:, :, None], old_sums, 0.0), axis=1)
    kept_weight = (
        jnp.where(
            lineage[:, :, None],
            jnp.exp(jnp.where(lineage[:, :, None], chosen_sum[:, None, :] - old_sums, 0.0)),
            0.0,
        )
        * old_steps
    )
    weighted = (
        (
            kept_weight[..., None]
            * old_heads.reshape(reqs_dev, NODES, local_heads, HEAD_DIM).astype(jnp.float32)
        )
        .astype(jnp.bfloat16)
        .reshape(reqs_dev, NODES, span_groups, span_heads, HEAD_DIM)
    )
    key_slice = lax.dynamic_slice_in_dim(
        old_keys, first_group * STATE, span_groups * STATE, 2
    ).reshape(reqs_dev, NODES, span_groups, STATE)
    update = jnp.einsum(
        "bjgqp,bjgn->bgqpn", weighted, key_slice, preferred_element_type=jnp.float32
    )
    carry_state = (
        jnp.exp(chosen_sum).reshape(reqs_dev, span_groups, span_heads, 1, 1)
        * old_state.reshape(reqs_dev, span_groups, span_heads, HEAD_DIM, STATE).astype(jnp.float32)
        + update
    ).astype(jnp.bfloat16)
    carry_state = lax.optimization_barrier(carry_state)
    tree_rows = tree_heads.shape[0]
    head_width = local_heads * HEAD_DIM
    split_heads = jnp.moveaxis(tree_heads.reshape(tree_rows, head_count, head_width), 1, 0)
    split_gates = jnp.moveaxis(tree_gates.reshape(tree_rows, head_count, head_width), 1, 0)
    split_steps = jnp.moveaxis(tree_steps.reshape(tree_rows, head_count, local_heads), 1, 0)
    split_groups = own_columns(tree_groups, span_groups, head_count, per_dest)
    split_prior = own_columns(prior_groups, span_groups, head_count, per_dest).reshape(
        head_count, reqs_dev * local_nodes, 2 * own_width
    )
    widths = [2 * own_width, 2 * own_width, head_width, head_width, local_heads]
    bundle = jnp.concatenate(
        [split_groups, split_prior.astype(jnp.bfloat16), split_heads, split_gates, split_steps], axis=-1
    )
    bundle = lax.all_to_all(bundle, "head", split_axis=0, concat_axis=0, tiled=True)
    cuts = [0]
    for width in widths:
        cuts.append(cuts[-1] + width)
    pieces = [bundle[..., cuts[n] : cuts[n + 1]] for n in range(len(widths))]
    group_rows = pieces[0].reshape(reqs_dev, NODES, 2 * own_width)
    prior_flat = pieces[1].reshape(head_count * reqs_dev * local_nodes, 2 * own_width)
    head_rows = pieces[2].reshape(reqs_dev, NODES, head_width)
    gate_rows = pieces[3].reshape(reqs_dev, NODES, span_groups, span_heads, HEAD_DIM)
    step_rows = pieces[4].reshape(reqs_dev, NODES, local_heads)
    pick_split = tail_pick.reshape(reqs_dev, 3, head_count, local_nodes)
    same_slot = (local_ids[:, None] == local_ids[None, :]).astype(jnp.bfloat16)
    pick_rows = (
        pick_split[:, :, :, None, :] * same_slot[:, None, None, :, None]
    ).reshape(reqs_dev * 3, head_count * reqs_dev * local_nodes)
    tail_groups = (
        jnp.dot(pick_rows, prior_flat, preferred_element_type=jnp.float32)
        .astype(jnp.bfloat16)
        .reshape(reqs_dev, 3, 2 * own_width)
    )
    new_part = jnp.concatenate([tail_heads, tail_groups], axis=-1).reshape(reqs_dev, NODES, -1)
    old_part = jnp.concatenate(
        [group_rows[..., own_width:], new_tree.astype(jnp.bfloat16)], axis=-1
    )
    new_len = new_part.shape[-1]
    exchange = jnp.concatenate(
        [spread(send_hot, new_part), spread(recv_hot, old_part)],
        axis=-1,
    )
    exchange = lax.all_to_all(exchange, "req", split_axis=0, concat_axis=0, tiled=True)
    tails_new = (
        gather_back(recv_hot, exchange[..., :new_len]).astype(jnp.bfloat16).reshape(reqs_dev, 3, -1)
    )
    rows_old = gather_back(send_hot, exchange[..., new_len:]).astype(jnp.bfloat16)
    tree_old = rows_old[..., own_width:].astype(jnp.int32)
    kernel_own = own_columns(kernel_groups, span_groups, head_count, per_dest)[head_index]
    shift_own = own_columns(shift_groups, span_groups, head_count, per_dest)[head_index]
    query_old = tree_conv(
        rows_old[..., :own_width],
        tail_groups[..., own_width:],
        tree_old,
        kernel_own[:, own_width:],
        shift_own[own_width:],
    ).reshape(reqs_dev, NODES, span_groups, STATE)
    carried_old = jnp.einsum(
        "btn,bmn->btm",
        query_old.reshape(reqs_dev, NODES, STATE),
        carry_state.reshape(reqs_dev, head_width, STATE),
        preferred_element_type=jnp.float32,
    )
    carried_moved = lax.all_to_all(
        spread(send_hot, carried_old.astype(jnp.bfloat16)), "req", split_axis=0, concat_axis=0, tiled=True
    )
    carried = gather_back(recv_hot, carried_moved).reshape(reqs_dev, NODES, span_groups, span_heads, HEAD_DIM)
    conv_heads = tree_conv(
        head_rows, tails_new[..., :head_width], new_tree, kernel_heads, shift_heads
    )
    conv_groups = tree_conv(
        group_rows, tails_new[..., head_width:], new_tree, kernel_own, shift_own
    )
    own_keys = conv_groups[..., :own_width]
    own_queries = conv_groups[..., own_width:]
    query_four = own_queries.reshape(reqs_dev, NODES, span_groups, STATE)
    key_four = own_keys.reshape(reqs_dev, NODES, span_groups, STATE)
    step_sizes = jax.nn.softplus(step_rows.astype(jnp.float32) + step_bias)
    decay_sum = jnp.einsum(
        "btj,bjh->bth", new_tree.astype(jnp.float32), step_sizes * decay_rates, precision=highest
    )
    intersection = jnp.einsum(
        "btgn,bjgn->btjg", query_four, key_four, preferred_element_type=jnp.float32
    )
    lineage_new = (new_tree == 1)[:, :, :, None]
    decay_gap = decay_sum[:, :, None, :] - decay_sum[:, None, :, :]
    decays = jnp.where(lineage_new, jnp.exp(jnp.where(lineage_new, decay_gap, 0.0)), 0.0)
    mixing = (
        decays.reshape(reqs_dev, NODES, NODES, span_groups, span_heads)
        * intersection[..., None]
        * step_sizes.reshape(reqs_dev, 1, NODES, span_groups, span_heads)
    ).astype(jnp.bfloat16)
    values = conv_heads.reshape(reqs_dev, NODES, span_groups, span_heads, HEAD_DIM)
    inner_part = jnp.einsum(
        "btjgq,bjgqp->btgqp", mixing, values, preferred_element_type=jnp.float32
    )
    output = (
        inner_part
        + jnp.exp(decay_sum).reshape(reqs_dev, NODES, span_groups, span_heads, 1) * carried
        + skip_gain.reshape(1, 1, span_groups, span_heads, 1) * values.astype(jnp.float32)
    )
    gated_out = output * jax.nn.silu(gate_rows.astype(jnp.float32))
    group_power = jnp.sum(gated_out * gated_out, axis=(3, 4))
    if per_dest == 2:
        partner = [(d, d ^ 1) for d in range(head_count)]
        power_own = group_power + lax.ppermute(group_power, "head", partner)
    else:
        zero_index = jnp.zeros((), jnp.int32)
        power_full = lax.dynamic_update_slice(
            jnp.zeros((reqs_dev, NODES, GROUPS), jnp.float32),
            group_power,
            (zero_index, zero_index, first_group),
        )
        power_total = lax.psum(power_full, "head")
        power_own = lax.dynamic_slice_in_dim(power_total, first_group, span_groups, 2)
    scale_factor = lax.rsqrt(power_own / (per_group * HEAD_DIM) + EPSILON)
    normed = (
        gated_out
        * scale_factor[..., None, None]
        * norm_gain.reshape(1, 1, span_groups, span_heads, HEAD_DIM)
    )
    return normed.reshape(reqs_dev * NODES, local_heads * HEAD_DIM).astype(jnp.bfloat16)


def solution(mesh):
    placed = (
        P(("req", "head"), None),
        P(("req", "head"), None),
        P(("req", "head"), None),
        P(("req", "head"), None),
        P("req", None, None),
        P(None, "head"),
        P("head"),
        P(),
        P(),
        P("head"),
        P("head"),
        P("head"),
        P("head"),
        P("req", "head", None, None),
        P("req", None, "head"),
        P("req", None, None),
        P("req", None, "head"),
        P("req", None, "head"),
        P("req", "head", None),
        P("req", None, None),
        P("req"),
        P(),
    )
    return jax.shard_map(
        shards, mesh=mesh, in_specs=placed, out_specs=P("req", "head"), check_vma=False
    )
```

```python
import jax
import jax.numpy as jnp
from jax import lax
from jax.sharding import PartitionSpec as P

HEADS = 256
HEAD_DIM = 64
STATE = 256
GROUPS = 8
NODES = 32
MOST = 2


EPSILON = 1e-05


def tree_conv(tree_rows, tail_rows, ancestry, weight, offset_bias):
    node_depth = jnp.sum(ancestry, axis=-1) - 1
    places = jnp.arange(3, dtype=jnp.int32)
    summed = weight[3].astype(jnp.float32) * tree_rows.astype(jnp.float32) + offset_bias
    for upward in range(1, 4):
        picked = (
            (ancestry == 1) & (node_depth[:, None, :] == node_depth[:, :, None] - upward)
        ).astype(jnp.bfloat16)
        older_rows = (places[None, None, :] == node_depth[:, :, None] - upward + 3).astype(
            jnp.bfloat16
        )
        shifted = jnp.einsum("btj,bjc->btc", picked, tree_rows, preferred_element_type=jnp.float32)
        shifted = shifted + jnp.einsum(
            "bti,bic->btc", older_rows, tail_rows, preferred_element_type=jnp.float32
        )
        summed = summed + weight[3 - upward].astype(jnp.float32) * shifted
    return jax.nn.silu(summed).astype(jnp.bfloat16)


def place_slots(payload, positions, count):
    wanted = jnp.arange(count, dtype=jnp.int32)
    owners = jnp.arange(positions.shape[0], dtype=jnp.int32)
    hits = positions[None, :] == wanted[:, None]
    chosen = jnp.sum(jnp.where(hits, owners[None, :], 0), axis=1)
    filled = jnp.any(hits, axis=1).reshape((count,) + (1,) * (payload.ndim - 1))
    taken = jnp.take(payload, chosen, axis=0)
    return jnp.where(filled, taken, jnp.zeros_like(taken))


def own_columns(rows, span_groups, dest_count, per_dest):
    lead = rows.shape[:-1]
    split = rows.reshape(lead + (2, GROUPS, STATE))
    moved = jnp.moveaxis(split, -2, 0)
    picks = (jnp.arange(dest_count, dtype=jnp.int32) // per_dest)[:, None] * span_groups + jnp.arange(
        span_groups, dtype=jnp.int32
    )[None, :]
    taken = jnp.take(moved, picks.reshape(-1), axis=0).reshape((dest_count, span_groups) + lead + (2, STATE))
    return jnp.moveaxis(taken, 1, -2).reshape((dest_count,) + lead + (2 * span_groups * STATE,))


def columns_by_dest(rows, span_groups, dest_count, per_dest):
    count = rows.shape[0]
    split = rows.reshape(count, 2, GROUPS, STATE)
    picks = (jnp.arange(dest_count, dtype=jnp.int32) // per_dest)[:, None] * span_groups + jnp.arange(
        span_groups, dtype=jnp.int32
    )[None, :]
    taken = jnp.take(split, picks.reshape(-1), axis=2).reshape(count, 2, dest_count, span_groups, STATE)
    return jnp.moveaxis(taken, 2, 1).reshape(count, dest_count, 2 * span_groups * STATE)


def shards(
    tree_heads,
    tree_gates,
    tree_steps,
    tree_groups,
    new_tree,
    kernel_heads,
    shift_heads,
    kernel_groups,
    shift_groups,
    log_rates,
    step_bias,
    skip_gain,
    norm_gain,
    old_state,
    old_heads,
    old_keys,
    old_steps,
    prior_heads,
    prior_groups,
    old_tree,
    accepted,
    new_owner,
):
    req_count = lax.axis_size("req")
    head_count = lax.axis_size("head")
    req_index = lax.axis_index("req")
    head_index = lax.axis_index("head")
    reqs_dev = new_tree.shape[0]
    local_heads = log_rates.shape[0]
    local_nodes = prior_groups.shape[1]
    per_group = HEADS // GROUPS
    span_heads = min(local_heads, per_group)
    span_groups = local_heads // span_heads
    per_dest = per_group // span_heads
    assert span_groups == 1
    first_group = head_index * local_heads // per_group
    slot_count = req_count * MOST
    own_width = span_groups * STATE
    highest = lax.Precision.HIGHEST
    owner_table = new_owner.reshape(req_count, reqs_dev)
    target_dev = owner_table // reqs_dev
    local_ids = jnp.arange(reqs_dev, dtype=jnp.int32)
    before = local_ids[None, :, None] > local_ids[None, None, :]
    same_dest = target_dev[:, :, None] == target_dev[:, None, :]
    arrival = jnp.sum((same_dest & before).astype(jnp.int32), axis=-1)
    send_table = target_dev * MOST + arrival
    send_pos = lax.dynamic_index_in_dim(send_table, req_index, 0, keepdims=False)
    wanted_slot = req_index * reqs_dev + local_ids
    all_ids = jnp.arange(new_owner.shape[0], dtype=jnp.int32)
    match = new_owner[None, :] == wanted_slot[:, None]
    anchor = jnp.sum(jnp.where(match, all_ids[None, :], 0), axis=1)
    recv_pos = anchor // reqs_dev * MOST + jnp.take(arrival.reshape(-1), anchor)

    slot_ids = jnp.arange(slot_count, dtype=jnp.int32)
    send_hot = (send_pos[None, :] == slot_ids[:, None]).astype(jnp.bfloat16)
    recv_hot = (recv_pos[None, :] == slot_ids[:, None]).astype(jnp.bfloat16)

    def spread(hot, payload):
        return jnp.einsum(
            "pa,a...->p...", hot, payload, preferred_element_type=jnp.float32
        ).astype(jnp.bfloat16)

    def gather_back(hot, moved):
        return jnp.einsum("pa,p...->a...", hot, moved, preferred_element_type=jnp.float32)

    decay_rates = -jnp.exp(log_rates)
    node_ids = jnp.arange(NODES, dtype=jnp.int32)
    chosen_hot = node_ids[None, :] == accepted[:, None]
    chosen_row = jnp.sum(jnp.where(chosen_hot[:, :, None], old_tree, 0), axis=1)
    old_depth = jnp.sum(old_tree, axis=-1) - 1
    chosen_depth = jnp.sum(jnp.where(chosen_hot, old_depth, 0), axis=1)
    places = jnp.arange(3, dtype=jnp.int32)
    lineage = chosen_row == 1
    tail_pick = (
        lineage[:, None, :]
        & (old_depth[:, None, :] == chosen_depth[:, None, None] - 2 + places[None, :, None])
    ).astype(jnp.bfloat16)
    tail_heads = jnp.einsum(
        "bij,bjc->bic", tail_pick, prior_heads, preferred_element_type=jnp.float32
    ).astype(jnp.bfloat16)
    old_sums = jnp.einsum(
        "btj,bjh->bth", old_tree.astype(jnp.float32), old_steps * decay_rates, precision=highest
    )
    chosen_sum = jnp.sum(jnp.where(chosen_hot[:, :, None], old_sums, 0.0), axis=1)
    kept_weight = (
        jnp.where(
            lineage[:, :, None],
            jnp.exp(jnp.where(lineage[:, :, None], chosen_sum[:, None, :] - old_sums, 0.0)),
            0.0,
        )
        * old_steps
    )
    weighted = (
        (
            kept_weight[..., None]
            * old_heads.reshape(reqs_dev, NODES, local_heads, HEAD_DIM).astype(jnp.float32)
        )
        .astype(jnp.bfloat16)
        .reshape(reqs_dev, NODES, span_groups, span_heads, HEAD_DIM)
    )
    key_slice = lax.dynamic_slice_in_dim(
        old_keys, first_group * STATE, span_groups * STATE, 2
    ).reshape(reqs_dev, NODES, span_groups, STATE)
    update = jnp.einsum(
        "bjgqp,bjgn->bgqpn", weighted, key_slice, preferred_element_type=jnp.float32
    )
    carry_state = (
        jnp.exp(chosen_sum).reshape(reqs_dev, span_groups, span_heads, 1, 1)
        * old_state.reshape(reqs_dev, span_groups, span_heads, HEAD_DIM, STATE).astype(jnp.float32)
        + update
    ).astype(jnp.bfloat16)
    carry_state = lax.optimization_barrier(carry_state)
    tree_rows = tree_heads.shape[0]
    head_width = local_heads * HEAD_DIM
    widths = [2 * own_width, 2 * own_width, head_width, head_width, local_heads]
    bundle = jnp.concatenate(
        [
            columns_by_dest(tree_groups, span_groups, head_count, per_dest),
            columns_by_dest(
                prior_groups.reshape(reqs_dev * local_nodes, -1), span_groups, head_count, per_dest
            ),
            tree_heads.reshape(tree_rows, head_count, head_width),
            tree_gates.reshape(tree_rows, head_count, head_width),
            tree_steps.reshape(tree_rows, head_count, local_heads),
        ],
        axis=-1,
    )
    bundle = lax.all_to_all(bundle, "head", split_axis=1, concat_axis=0, tiled=True)
    bundle = bundle.reshape(head_count * tree_rows, -1)
    cuts = [0]
    for width in widths:
        cuts.append(cuts[-1] + width)
    pieces = [bundle[..., cuts[n] : cuts[n + 1]] for n in range(len(widths))]
    group_rows = pieces[0].reshape(reqs_dev, NODES, 2 * own_width)
    prior_flat = pieces[1]
    head_rows = pieces[2].reshape(reqs_dev, NODES, head_width)
    gate_rows = pieces[3].reshape(reqs_dev, NODES, span_groups, span_heads, HEAD_DIM)
    step_rows = pieces[4].reshape(reqs_dev, NODES, local_heads)
    pick_split = tail_pick.reshape(reqs_dev, 3, head_count, local_nodes)
    same_slot = (local_ids[:, None] == local_ids[None, :]).astype(jnp.bfloat16)
    pick_rows = (
        pick_split[:, :, :, None, :] * same_slot[:, None, None, :, None]
    ).reshape(reqs_dev * 3, head_count * reqs_dev * local_nodes)
    tail_groups = (
        jnp.dot(pick_rows, prior_flat, preferred_element_type=jnp.float32)
        .astype(jnp.bfloat16)
        .reshape(reqs_dev, 3, 2 * own_width)
    )
    new_part = jnp.concatenate([tail_heads, tail_groups], axis=-1).reshape(reqs_dev, NODES, -1)
    old_part = jnp.concatenate(
        [group_rows[..., own_width:], new_tree.astype(jnp.bfloat16)], axis=-1
    )
    new_len = new_part.shape[-1]
    exchange = jnp.concatenate(
        [spread(send_hot, new_part), spread(recv_hot, old_part)],
        axis=-1,
    )
    exchange = lax.all_to_all(exchange, "req", split_axis=0, concat_axis=0, tiled=True)
    tails_new = (
        gather_back(recv_hot, exchange[..., :new_len]).astype(jnp.bfloat16).reshape(reqs_dev, 3, -1)
    )
    rows_old = gather_back(send_hot, exchange[..., new_len:]).astype(jnp.bfloat16)
    tree_old = rows_old[..., own_width:].astype(jnp.int32)
    kernel_own = own_columns(kernel_groups, span_groups, head_count, per_dest)[head_index]
    shift_own = own_columns(shift_groups, span_groups, head_count, per_dest)[head_index]
    query_old = tree_conv(
        rows_old[..., :own_width],
        tail_groups[..., own_width:],
        tree_old,
        kernel_own[:, own_width:],
        shift_own[own_width:],
    ).reshape(reqs_dev, NODES, span_groups, STATE)
    carried_old = jnp.einsum(
        "btn,bmn->btm",
        query_old.reshape(reqs_dev, NODES, STATE),
        carry_state.reshape(reqs_dev, head_width, STATE),
        preferred_element_type=jnp.float32,
    )
    carried_moved = lax.all_to_all(
        spread(send_hot, carried_old.astype(jnp.bfloat16)), "req", split_axis=0, concat_axis=0, tiled=True
    )
    carried = gather_back(recv_hot, carried_moved).reshape(reqs_dev, NODES, span_groups, span_heads, HEAD_DIM)
    conv_heads = tree_conv(
        head_rows, tails_new[..., :head_width], new_tree, kernel_heads, shift_heads
    )
    conv_groups = tree_conv(
        group_rows, tails_new[..., head_width:], new_tree, kernel_own, shift_own
    )
    own_keys = conv_groups[..., :own_width]
    own_queries = conv_groups[..., own_width:]
    query_four = own_queries.reshape(reqs_dev, NODES, span_groups, STATE)
    key_four = own_keys.reshape(reqs_dev, NODES, span_groups, STATE)
    step_sizes = jax.nn.softplus(step_rows.astype(jnp.float32) + step_bias)
    decay_sum = jnp.einsum(
        "btj,bjh->bth", new_tree.astype(jnp.float32), step_sizes * decay_rates, precision=highest
    )
    intersection = jnp.einsum(
        "btgn,bjgn->btjg", query_four, key_four, preferred_element_type=jnp.float32
    )
    lineage_new = (new_tree == 1)[:, :, :, None]
    decay_gap = decay_sum[:, :, None, :] - decay_sum[:, None, :, :]
    decays = jnp.where(lineage_new, jnp.exp(jnp.where(lineage_new, decay_gap, 0.0)), 0.0)
    mixing = (
        decays.reshape(reqs_dev, NODES, NODES, span_groups, span_heads)
        * intersection[..., None]
        * step_sizes.reshape(reqs_dev, 1, NODES, span_groups, span_heads)
    ).astype(jnp.bfloat16)
    values = conv_heads.reshape(reqs_dev, NODES, span_groups, span_heads, HEAD_DIM)
    inner_part = jnp.einsum(
        "btjgq,bjgqp->btgqp", mixing, values, preferred_element_type=jnp.float32
    )
    output = (
        inner_part
        + jnp.exp(decay_sum).reshape(reqs_dev, NODES, span_groups, span_heads, 1) * carried
        + skip_gain.reshape(1, 1, span_groups, span_heads, 1) * values.astype(jnp.float32)
    )
    gated_out = output * jax.nn.silu(gate_rows.astype(jnp.float32))
    group_power = jnp.sum(gated_out * gated_out, axis=(3, 4))
    if per_dest == 2:
        partner = [(d, d ^ 1) for d in range(head_count)]
        power_own = group_power + lax.ppermute(group_power, "head", partner)
    else:
        zero_index = jnp.zeros((), jnp.int32)
        power_full = lax.dynamic_update_slice(
            jnp.zeros((reqs_dev, NODES, GROUPS), jnp.float32),
            group_power,
            (zero_index, zero_index, first_group),
        )
        power_total = lax.psum(power_full, "head")
        power_own = lax.dynamic_slice_in_dim(power_total, first_group, span_groups, 2)
    scale_factor = lax.rsqrt(power_own / (per_group * HEAD_DIM) + EPSILON)
    normed = (
        gated_out
        * scale_factor[..., None, None]
        * norm_gain.reshape(1, 1, span_groups, span_heads, HEAD_DIM)
    )
    return normed.reshape(reqs_dev * NODES, local_heads * HEAD_DIM).astype(jnp.bfloat16)


def solution(mesh):
    placed = (
        P(("req", "head"), None),
        P(("req", "head"), None),
        P(("req", "head"), None),
        P(("req", "head"), None),
        P("req", None, None),
        P(None, "head"),
        P("head"),
        P(),
        P(),
        P("head"),
        P("head"),
        P("head"),
        P("head"),
        P("req", "head", None, None),
        P("req", None, "head"),
        P("req", None, None),
        P("req", None, "head"),
        P("req", None, "head"),
        P("req", "head", None),
        P("req", None, None),
        P("req"),
        P(),
    )
    return jax.shard_map(
        shards, mesh=mesh, in_specs=placed, out_specs=P("req", "head"), check_vma=False
    )
```

```python
import jax
import jax.numpy as jnp
from jax import lax
from jax.sharding import PartitionSpec as P

HEADS = 256
HEAD_DIM = 64
STATE = 256
GROUPS = 8
NODES = 32
MOST = 2


EPSILON = 1e-05


def tree_conv(tree_rows, tail_rows, ancestry, weight, offset_bias):
    node_depth = jnp.sum(ancestry, axis=-1) - 1
    places = jnp.arange(3, dtype=jnp.int32)
    summed = weight[3].astype(jnp.float32) * tree_rows.astype(jnp.float32) + offset_bias
    for upward in range(1, 4):
        picked = (
            (ancestry == 1) & (node_depth[:, None, :] == node_depth[:, :, None] - upward)
        ).astype(jnp.bfloat16)
        older_rows = (places[None, None, :] == node_depth[:, :, None] - upward + 3).astype(
            jnp.bfloat16
        )
        shifted = jnp.einsum("btj,bjc->btc", picked, tree_rows, preferred_element_type=jnp.float32)
        shifted = shifted + jnp.einsum(
            "bti,bic->btc", older_rows, tail_rows, preferred_element_type=jnp.float32
        )
        summed = summed + weight[3 - upward].astype(jnp.float32) * shifted
    return jax.nn.silu(summed).astype(jnp.bfloat16)


def place_slots(payload, positions, count):
    wanted = jnp.arange(count, dtype=jnp.int32)
    owners = jnp.arange(positions.shape[0], dtype=jnp.int32)
    hits = positions[None, :] == wanted[:, None]
    chosen = jnp.sum(jnp.where(hits, owners[None, :], 0), axis=1)
    filled = jnp.any(hits, axis=1).reshape((count,) + (1,) * (payload.ndim - 1))
    taken = jnp.take(payload, chosen, axis=0)
    return jnp.where(filled, taken, jnp.zeros_like(taken))


def own_columns(rows, span_groups, dest_count, per_dest):
    lead = rows.shape[:-1]
    split = rows.reshape(lead + (2, GROUPS, STATE))
    moved = jnp.moveaxis(split, -2, 0)
    picks = (jnp.arange(dest_count, dtype=jnp.int32) // per_dest)[:, None] * span_groups + jnp.arange(
        span_groups, dtype=jnp.int32
    )[None, :]
    taken = jnp.take(moved, picks.reshape(-1), axis=0).reshape((dest_count, span_groups) + lead + (2, STATE))
    return jnp.moveaxis(taken, 1, -2).reshape((dest_count,) + lead + (2 * span_groups * STATE,))


def columns_by_dest(rows, span_groups, dest_count, per_dest):
    count = rows.shape[0]
    split = rows.reshape(count, 2, GROUPS, STATE)
    picks = (jnp.arange(dest_count, dtype=jnp.int32) // per_dest)[:, None] * span_groups + jnp.arange(
        span_groups, dtype=jnp.int32
    )[None, :]
    taken = jnp.take(split, picks.reshape(-1), axis=2).reshape(count, 2, dest_count, span_groups, STATE)
    return jnp.moveaxis(taken, 2, 1).reshape(count, dest_count, 2 * span_groups * STATE)


def shards(
    tree_heads,
    tree_gates,
    tree_steps,
    tree_groups,
    new_tree,
    kernel_heads,
    shift_heads,
    kernel_groups,
    shift_groups,
    log_rates,
    step_bias,
    skip_gain,
    norm_gain,
    old_state,
    old_heads,
    old_keys,
    old_steps,
    prior_heads,
    prior_groups,
    old_tree,
    accepted,
    new_owner,
):
    req_count = lax.axis_size("req")
    head_count = lax.axis_size("head")
    req_index = lax.axis_index("req")
    head_index = lax.axis_index("head")
    reqs_dev = new_tree.shape[0]
    local_heads = log_rates.shape[0]
    local_nodes = prior_groups.shape[1]
    per_group = HEADS // GROUPS
    span_heads = min(local_heads, per_group)
    span_groups = local_heads // span_heads
    per_dest = per_group // span_heads
    assert span_groups == 1
    first_group = head_index * local_heads // per_group
    slot_count = req_count * MOST
    own_width = span_groups * STATE
    highest = lax.Precision.HIGHEST
    owner_table = new_owner.reshape(req_count, reqs_dev)
    target_dev = owner_table // reqs_dev
    local_ids = jnp.arange(reqs_dev, dtype=jnp.int32)
    before = local_ids[None, :, None] > local_ids[None, None, :]
    same_dest = target_dev[:, :, None] == target_dev[:, None, :]
    arrival = jnp.sum((same_dest & before).astype(jnp.int32), axis=-1)
    send_table = target_dev * MOST + arrival
    send_pos = lax.dynamic_index_in_dim(send_table, req_index, 0, keepdims=False)
    wanted_slot = req_index * reqs_dev + local_ids
    all_ids = jnp.arange(new_owner.shape[0], dtype=jnp.int32)
    match = new_owner[None, :] == wanted_slot[:, None]
    anchor = jnp.sum(jnp.where(match, all_ids[None, :], 0), axis=1)
    recv_pos = anchor // reqs_dev * MOST + jnp.take(arrival.reshape(-1), anchor)

    slot_ids = jnp.arange(slot_count, dtype=jnp.int32)
    send_hot = (send_pos[None, :] == slot_ids[:, None]).astype(jnp.bfloat16)
    recv_hot = (recv_pos[None, :] == slot_ids[:, None]).astype(jnp.bfloat16)

    def spread(hot, payload):
        return jnp.einsum(
            "pa,a...->p...", hot, payload, preferred_element_type=jnp.float32
        ).astype(jnp.bfloat16)

    def gather_back(hot, moved):
        return jnp.einsum("pa,p...->a...", hot, moved, preferred_element_type=jnp.float32)

    decay_rates = -jnp.exp(log_rates)
    node_ids = jnp.arange(NODES, dtype=jnp.int32)
    chosen_hot = node_ids[None, :] == accepted[:, None]
    chosen_row = jnp.sum(jnp.where(chosen_hot[:, :, None], old_tree, 0), axis=1)
    old_depth = jnp.sum(old_tree, axis=-1) - 1
    chosen_depth = jnp.sum(jnp.where(chosen_hot, old_depth, 0), axis=1)
    places = jnp.arange(3, dtype=jnp.int32)
    lineage = chosen_row == 1
    tail_pick = (
        lineage[:, None, :]
        & (old_depth[:, None, :] == chosen_depth[:, None, None] - 2 + places[None, :, None])
    ).astype(jnp.bfloat16)
    tail_heads = jnp.einsum(
        "bij,bjc->bic", tail_pick, prior_heads, preferred_element_type=jnp.float32
    ).astype(jnp.bfloat16)
    old_sums = jnp.einsum(
        "btj,bjh->bth", old_tree.astype(jnp.float32), old_steps * decay_rates, precision=highest
    )
    chosen_sum = jnp.sum(jnp.where(chosen_hot[:, :, None], old_sums, 0.0), axis=1)
    kept_weight = (
        jnp.where(
            lineage[:, :, None],
            jnp.exp(jnp.where(lineage[:, :, None], chosen_sum[:, None, :] - old_sums, 0.0)),
            0.0,
        )
        * old_steps
    )
    weighted = (
        (
            kept_weight[..., None]
            * old_heads.reshape(reqs_dev, NODES, local_heads, HEAD_DIM).astype(jnp.float32)
        )
        .astype(jnp.bfloat16)
        .reshape(reqs_dev, NODES, span_groups, span_heads, HEAD_DIM)
    )
    key_slice = lax.dynamic_slice_in_dim(
        old_keys, first_group * STATE, span_groups * STATE, 2
    ).reshape(reqs_dev, NODES, span_groups, STATE)
    update = jnp.einsum(
        "bjgqp,bjgn->bgqpn", weighted, key_slice, preferred_element_type=jnp.float32
    )
    carry_state = (
        jnp.exp(chosen_sum).reshape(reqs_dev, span_groups, span_heads, 1, 1)
        * old_state.reshape(reqs_dev, span_groups, span_heads, HEAD_DIM, STATE).astype(jnp.float32)
        + update
    ).astype(jnp.bfloat16)
    carry_state = lax.optimization_barrier(carry_state)
    tree_rows = tree_heads.shape[0]
    head_width = local_heads * HEAD_DIM
    widths = [2 * own_width, 2 * own_width, head_width, head_width, local_heads]
    bundle = jnp.concatenate(
        [
            columns_by_dest(tree_groups, span_groups, head_count, per_dest),
            columns_by_dest(
                prior_groups.reshape(reqs_dev * local_nodes, -1), span_groups, head_count, per_dest
            ),
            tree_heads.reshape(tree_rows, head_count, head_width),
            tree_gates.reshape(tree_rows, head_count, head_width),
            tree_steps.reshape(tree_rows, head_count, local_heads),
        ],
        axis=-1,
    )
    bundle = lax.all_to_all(bundle, "head", split_axis=1, concat_axis=0, tiled=True)
    bundle = bundle.reshape(head_count * tree_rows, -1)
    cuts = [0]
    for width in widths:
        cuts.append(cuts[-1] + width)
    pieces = [bundle[..., cuts[n] : cuts[n + 1]] for n in range(len(widths))]
    group_rows = pieces[0].reshape(reqs_dev, NODES, 2 * own_width)
    prior_flat = pieces[1]
    head_rows = pieces[2].reshape(reqs_dev, NODES, head_width)
    gate_rows = pieces[3].reshape(reqs_dev, NODES, span_groups, span_heads, HEAD_DIM)
    step_rows = pieces[4].reshape(reqs_dev, NODES, local_heads)
    pick_split = tail_pick.reshape(reqs_dev, 3, head_count, local_nodes)
    same_slot = (local_ids[:, None] == local_ids[None, :]).astype(jnp.bfloat16)
    pick_rows = (
        pick_split[:, :, :, None, :] * same_slot[:, None, None, :, None]
    ).reshape(reqs_dev * 3, head_count * reqs_dev * local_nodes)
    tail_groups = (
        jnp.dot(pick_rows, prior_flat, preferred_element_type=jnp.float32)
        .astype(jnp.bfloat16)
        .reshape(reqs_dev, 3, 2 * own_width)
    )
    new_part = jnp.concatenate([tail_heads, tail_groups], axis=-1).reshape(reqs_dev, NODES, -1)
    old_part = jnp.concatenate(
        [group_rows[..., own_width:], new_tree.astype(jnp.bfloat16)], axis=-1
    )
    new_len = new_part.shape[-1]
    exchange = jnp.concatenate(
        [spread(send_hot, new_part), spread(recv_hot, old_part)],
        axis=-1,
    )
    exchange = lax.all_to_all(exchange, "req", split_axis=0, concat_axis=0, tiled=True)
    tails_new = (
        gather_back(recv_hot, exchange[..., :new_len]).astype(jnp.bfloat16).reshape(reqs_dev, 3, -1)
    )
    rows_old = gather_back(send_hot, exchange[..., new_len:]).astype(jnp.bfloat16)
    tree_old = rows_old[..., own_width:].astype(jnp.int32)
    kernel_own = own_columns(kernel_groups, span_groups, head_count, per_dest)[head_index]
    shift_own = own_columns(shift_groups, span_groups, head_count, per_dest)[head_index]
    query_old = tree_conv(
        rows_old[..., :own_width],
        tail_groups[..., own_width:],
        tree_old,
        kernel_own[:, own_width:],
        shift_own[own_width:],
    ).reshape(reqs_dev, NODES, span_groups, STATE)
    carried_old = jnp.einsum(
        "btn,bmn->btm",
        query_old.reshape(reqs_dev, NODES, STATE),
        carry_state.reshape(reqs_dev, head_width, STATE),
        preferred_element_type=jnp.float32,
    )
    carried_moved = lax.all_to_all(
        spread(send_hot, carried_old.astype(jnp.bfloat16)), "req", split_axis=0, concat_axis=0, tiled=True
    )
    carried = gather_back(recv_hot, carried_moved).reshape(reqs_dev, NODES, span_groups, span_heads, HEAD_DIM)
    conv_heads = tree_conv(
        head_rows, tails_new[..., :head_width], new_tree, kernel_heads, shift_heads
    )
    conv_groups = tree_conv(
        group_rows, tails_new[..., head_width:], new_tree, kernel_own, shift_own
    )
    own_keys = conv_groups[..., :own_width]
    own_queries = conv_groups[..., own_width:]
    query_four = own_queries.reshape(reqs_dev, NODES, span_groups, STATE)
    key_four = own_keys.reshape(reqs_dev, NODES, span_groups, STATE)
    step_sizes = jax.nn.softplus(step_rows.astype(jnp.float32) + step_bias)
    decay_sum = jnp.einsum(
        "btj,bjh->bth", new_tree.astype(jnp.float32), step_sizes * decay_rates, precision=highest
    )
    intersection = jnp.einsum(
        "btgn,bjgn->btjg", query_four, key_four, preferred_element_type=jnp.float32
    )
    lineage_new = (new_tree == 1)[:, :, :, None]
    decay_gap = decay_sum[:, :, None, :] - decay_sum[:, None, :, :]
    decays = jnp.where(lineage_new, jnp.exp(jnp.where(lineage_new, decay_gap, 0.0)), 0.0)
    mixing = (
        decays.reshape(reqs_dev, NODES, NODES, span_groups, span_heads)
        * intersection[..., None]
        * step_sizes.reshape(reqs_dev, 1, NODES, span_groups, span_heads)
    ).astype(jnp.bfloat16)
    values = conv_heads.reshape(reqs_dev, NODES, span_groups, span_heads, HEAD_DIM)
    inner_part = jnp.einsum(
        "btjgq,bjgqp->btgqp", mixing, values, preferred_element_type=jnp.float32
    )
    inner_part = lax.optimization_barrier(inner_part)
    output = (
        inner_part
        + jnp.exp(decay_sum).reshape(reqs_dev, NODES, span_groups, span_heads, 1) * carried
        + skip_gain.reshape(1, 1, span_groups, span_heads, 1) * values.astype(jnp.float32)
    )
    gated_out = output * jax.nn.silu(gate_rows.astype(jnp.float32))
    group_power = jnp.sum(gated_out * gated_out, axis=(3, 4))
    if per_dest == 2:
        partner = [(d, d ^ 1) for d in range(head_count)]
        power_own = group_power + lax.ppermute(group_power, "head", partner)
    else:
        zero_index = jnp.zeros((), jnp.int32)
        power_full = lax.dynamic_update_slice(
            jnp.zeros((reqs_dev, NODES, GROUPS), jnp.float32),
            group_power,
            (zero_index, zero_index, first_group),
        )
        power_total = lax.psum(power_full, "head")
        power_own = lax.dynamic_slice_in_dim(power_total, first_group, span_groups, 2)
    scale_factor = lax.rsqrt(power_own / (per_group * HEAD_DIM) + EPSILON)
    normed = (
        gated_out
        * scale_factor[..., None, None]
        * norm_gain.reshape(1, 1, span_groups, span_heads, HEAD_DIM)
    )
    return normed.reshape(reqs_dev * NODES, local_heads * HEAD_DIM).astype(jnp.bfloat16)


def solution(mesh):
    placed = (
        P(("req", "head"), None),
        P(("req", "head"), None),
        P(("req", "head"), None),
        P(("req", "head"), None),
        P("req", None, None),
        P(None, "head"),
        P("head"),
        P(),
        P(),
        P("head"),
        P("head"),
        P("head"),
        P("head"),
        P("req", "head", None, None),
        P("req", None, "head"),
        P("req", None, None),
        P("req", None, "head"),
        P("req", None, "head"),
        P("req", "head", None),
        P("req", None, None),
        P("req"),
        P(),
    )
    return jax.shard_map(
        shards, mesh=mesh, in_specs=placed, out_specs=P("req", "head"), check_vma=False
    )
```

```python
import jax
import jax.numpy as jnp
from jax import lax
from jax.sharding import PartitionSpec as P

HEADS = 256
HEAD_DIM = 64
STATE = 256
GROUPS = 8
NODES = 32
MOST = 2


EPSILON = 1e-05


def tree_conv(tree_rows, tail_rows, ancestry, weight, offset_bias):
    node_depth = jnp.sum(ancestry, axis=-1) - 1
    places = jnp.arange(3, dtype=jnp.int32)
    summed = weight[3].astype(jnp.float32) * tree_rows.astype(jnp.float32) + offset_bias
    for upward in range(1, 4):
        picked = (
            (ancestry == 1) & (node_depth[:, None, :] == node_depth[:, :, None] - upward)
        ).astype(jnp.bfloat16)
        older_rows = (places[None, None, :] == node_depth[:, :, None] - upward + 3).astype(
            jnp.bfloat16
        )
        shifted = jnp.einsum("btj,bjc->btc", picked, tree_rows, preferred_element_type=jnp.float32)
        shifted = shifted + jnp.einsum(
            "bti,bic->btc", older_rows, tail_rows, preferred_element_type=jnp.float32
        )
        summed = summed + weight[3 - upward].astype(jnp.float32) * shifted
    return jax.nn.silu(summed).astype(jnp.bfloat16)


def place_slots(payload, positions, count):
    wanted = jnp.arange(count, dtype=jnp.int32)
    owners = jnp.arange(positions.shape[0], dtype=jnp.int32)
    hits = positions[None, :] == wanted[:, None]
    chosen = jnp.sum(jnp.where(hits, owners[None, :], 0), axis=1)
    filled = jnp.any(hits, axis=1).reshape((count,) + (1,) * (payload.ndim - 1))
    taken = jnp.take(payload, chosen, axis=0)
    return jnp.where(filled, taken, jnp.zeros_like(taken))


def own_columns(rows, span_groups, dest_count, per_dest):
    lead = rows.shape[:-1]
    split = rows.reshape(lead + (2, GROUPS, STATE))
    moved = jnp.moveaxis(split, -2, 0)
    picks = (jnp.arange(dest_count, dtype=jnp.int32) // per_dest)[:, None] * span_groups + jnp.arange(
        span_groups, dtype=jnp.int32
    )[None, :]
    taken = jnp.take(moved, picks.reshape(-1), axis=0).reshape((dest_count, span_groups) + lead + (2, STATE))
    return jnp.moveaxis(taken, 1, -2).reshape((dest_count,) + lead + (2 * span_groups * STATE,))


def columns_by_dest(rows, span_groups, dest_count, per_dest):
    count = rows.shape[0]
    split = rows.reshape(count, 2, GROUPS, STATE)
    picks = (jnp.arange(dest_count, dtype=jnp.int32) // per_dest)[:, None] * span_groups + jnp.arange(
        span_groups, dtype=jnp.int32
    )[None, :]
    taken = jnp.take(split, picks.reshape(-1), axis=2).reshape(count, 2, dest_count, span_groups, STATE)
    return jnp.moveaxis(taken, 2, 1).reshape(count, dest_count, 2 * span_groups * STATE)


def shards(
    tree_heads,
    tree_gates,
    tree_steps,
    tree_groups,
    new_tree,
    kernel_heads,
    shift_heads,
    kernel_groups,
    shift_groups,
    log_rates,
    step_bias,
    skip_gain,
    norm_gain,
    old_state,
    old_heads,
    old_keys,
    old_steps,
    prior_heads,
    prior_groups,
    old_tree,
    accepted,
    new_owner,
):
    req_count = lax.axis_size("req")
    head_count = lax.axis_size("head")
    req_index = lax.axis_index("req")
    head_index = lax.axis_index("head")
    reqs_dev = new_tree.shape[0]
    local_heads = log_rates.shape[0]
    local_nodes = prior_groups.shape[1]
    per_group = HEADS // GROUPS
    span_heads = min(local_heads, per_group)
    span_groups = local_heads // span_heads
    per_dest = per_group // span_heads
    assert span_groups == 1 and per_dest == 2
    first_group = head_index * local_heads // per_group
    slot_count = req_count * MOST
    own_width = span_groups * STATE
    highest = lax.Precision.HIGHEST
    owner_table = new_owner.reshape(req_count, reqs_dev)
    target_dev = owner_table // reqs_dev
    local_ids = jnp.arange(reqs_dev, dtype=jnp.int32)
    before = local_ids[None, :, None] > local_ids[None, None, :]
    same_dest = target_dev[:, :, None] == target_dev[:, None, :]
    arrival = jnp.sum((same_dest & before).astype(jnp.int32), axis=-1)
    send_table = target_dev * MOST + arrival
    send_pos = lax.dynamic_index_in_dim(send_table, req_index, 0, keepdims=False)
    wanted_slot = req_index * reqs_dev + local_ids
    all_ids = jnp.arange(new_owner.shape[0], dtype=jnp.int32)
    match = new_owner[None, :] == wanted_slot[:, None]
    anchor = jnp.sum(jnp.where(match, all_ids[None, :], 0), axis=1)
    recv_pos = anchor // reqs_dev * MOST + jnp.take(arrival.reshape(-1), anchor)

    slot_ids = jnp.arange(slot_count, dtype=jnp.int32)
    send_hot = (send_pos[None, :] == slot_ids[:, None]).astype(jnp.bfloat16)
    recv_hot = (recv_pos[None, :] == slot_ids[:, None]).astype(jnp.bfloat16)

    def spread(hot, payload):
        return jnp.einsum(
            "pa,a...->p...", hot, payload, preferred_element_type=jnp.float32
        ).astype(jnp.bfloat16)

    def gather_back(hot, moved):
        return jnp.einsum("pa,p...->a...", hot, moved, preferred_element_type=jnp.float32)

    decay_rates = -jnp.exp(log_rates)
    node_ids = jnp.arange(NODES, dtype=jnp.int32)
    chosen_hot = node_ids[None, :] == accepted[:, None]
    chosen_row = jnp.sum(jnp.where(chosen_hot[:, :, None], old_tree, 0), axis=1)
    old_depth = jnp.sum(old_tree, axis=-1) - 1
    chosen_depth = jnp.sum(jnp.where(chosen_hot, old_depth, 0), axis=1)
    places = jnp.arange(3, dtype=jnp.int32)
    lineage = chosen_row == 1
    tail_pick = (
        lineage[:, None, :]
        & (old_depth[:, None, :] == chosen_depth[:, None, None] - 2 + places[None, :, None])
    ).astype(jnp.bfloat16)
    tail_heads = jnp.einsum(
        "bij,bjc->bic", tail_pick, prior_heads, preferred_element_type=jnp.float32
    ).astype(jnp.bfloat16)
    old_sums = jnp.einsum(
        "btj,bjh->bth", old_tree.astype(jnp.float32), old_steps * decay_rates, precision=highest
    )
    chosen_sum = jnp.sum(jnp.where(chosen_hot[:, :, None], old_sums, 0.0), axis=1)
    kept_weight = (
        jnp.where(
            lineage[:, :, None],
            jnp.exp(jnp.where(lineage[:, :, None], chosen_sum[:, None, :] - old_sums, 0.0)),
            0.0,
        )
        * old_steps
    )
    weighted = (
        (
            kept_weight[..., None]
            * old_heads.reshape(reqs_dev, NODES, local_heads, HEAD_DIM).astype(jnp.float32)
        )
        .astype(jnp.bfloat16)
        .reshape(reqs_dev, NODES, span_groups, span_heads, HEAD_DIM)
    )
    key_slice = lax.dynamic_slice_in_dim(
        old_keys, first_group * STATE, span_groups * STATE, 2
    ).reshape(reqs_dev, NODES, span_groups, STATE)
    update = jnp.einsum(
        "bjgqp,bjgn->bgqpn", weighted, key_slice, preferred_element_type=jnp.float32
    )
    carry_state = (
        jnp.exp(chosen_sum).reshape(reqs_dev, span_groups, span_heads, 1, 1)
        * old_state.reshape(reqs_dev, span_groups, span_heads, HEAD_DIM, STATE).astype(jnp.float32)
        + update
    ).astype(jnp.bfloat16)
    carry_state = lax.optimization_barrier(carry_state)
    tree_rows = tree_heads.shape[0]
    head_width = local_heads * HEAD_DIM
    widths = [2 * own_width, 2 * own_width, head_width, head_width, local_heads]
    bundle = jnp.concatenate(
        [
            columns_by_dest(tree_groups, span_groups, head_count, per_dest),
            columns_by_dest(
                prior_groups.reshape(reqs_dev * local_nodes, -1), span_groups, head_count, per_dest
            ),
            tree_heads.reshape(tree_rows, head_count, head_width),
            tree_gates.reshape(tree_rows, head_count, head_width),
            tree_steps.reshape(tree_rows, head_count, local_heads),
        ],
        axis=-1,
    )
    bundle = lax.all_to_all(bundle, "head", split_axis=1, concat_axis=0, tiled=True)
    bundle = bundle.reshape(head_count * tree_rows, -1)
    cuts = [0]
    for width in widths:
        cuts.append(cuts[-1] + width)
    pieces = [bundle[..., cuts[n] : cuts[n + 1]] for n in range(len(widths))]
    group_rows = pieces[0].reshape(reqs_dev, NODES, 2 * own_width)
    prior_flat = pieces[1]
    head_rows = pieces[2].reshape(reqs_dev, NODES, head_width)
    gate_rows = pieces[3].reshape(reqs_dev, NODES, span_groups, span_heads, HEAD_DIM)
    step_rows = pieces[4].reshape(reqs_dev, NODES, local_heads)
    pick_split = tail_pick.reshape(reqs_dev, 3, head_count, local_nodes)
    same_slot = (local_ids[:, None] == local_ids[None, :]).astype(jnp.bfloat16)
    pick_rows = (
        pick_split[:, :, :, None, :] * same_slot[:, None, None, :, None]
    ).reshape(reqs_dev * 3, head_count * reqs_dev * local_nodes)
    tail_groups = (
        jnp.dot(pick_rows, prior_flat, preferred_element_type=jnp.float32)
        .astype(jnp.bfloat16)
        .reshape(reqs_dev, 3, 2 * own_width)
    )
    new_part = jnp.concatenate([tail_heads, tail_groups], axis=-1).reshape(reqs_dev, NODES, -1)
    old_part = jnp.concatenate(
        [group_rows[..., own_width:], new_tree.astype(jnp.bfloat16)], axis=-1
    )
    new_len = new_part.shape[-1]
    exchange = jnp.concatenate(
        [spread(send_hot, new_part), spread(recv_hot, old_part)],
        axis=-1,
    )
    exchange = lax.all_to_all(exchange, "req", split_axis=0, concat_axis=0, tiled=True)
    tails_new = (
        gather_back(recv_hot, exchange[..., :new_len]).astype(jnp.bfloat16).reshape(reqs_dev, 3, -1)
    )
    rows_old = gather_back(send_hot, exchange[..., new_len:]).astype(jnp.bfloat16)
    tree_old = rows_old[..., own_width:].astype(jnp.int32)
    kernel_own = own_columns(kernel_groups, span_groups, head_count, per_dest)[head_index]
    shift_own = own_columns(shift_groups, span_groups, head_count, per_dest)[head_index]
    query_old = tree_conv(
        rows_old[..., :own_width],
        tail_groups[..., own_width:],
        tree_old,
        kernel_own[:, own_width:],
        shift_own[own_width:],
    ).reshape(reqs_dev, NODES, span_groups, STATE)
    carried_old = jnp.einsum(
        "btn,bmn->btm",
        query_old.reshape(reqs_dev, NODES, STATE),
        carry_state.reshape(reqs_dev, head_width, STATE),
        preferred_element_type=jnp.float32,
    )
    carried_moved = lax.all_to_all(
        spread(send_hot, carried_old.astype(jnp.bfloat16)), "req", split_axis=0, concat_axis=0, tiled=True
    )
    carried = gather_back(recv_hot, carried_moved)
    conv_heads = tree_conv(
        head_rows, tails_new[..., :head_width], new_tree, kernel_heads, shift_heads
    )
    conv_groups = tree_conv(
        group_rows, tails_new[..., head_width:], new_tree, kernel_own, shift_own
    )
    own_keys = conv_groups[..., :own_width]
    own_queries = conv_groups[..., own_width:]
    query_four = own_queries.reshape(reqs_dev, NODES, span_groups, STATE)
    key_four = own_keys.reshape(reqs_dev, NODES, span_groups, STATE)
    step_sizes = jax.nn.softplus(step_rows.astype(jnp.float32) + step_bias)
    decay_sum = jnp.einsum(
        "btj,bjh->bth", new_tree.astype(jnp.float32), step_sizes * decay_rates, precision=highest
    )
    intersection = jnp.einsum(
        "btgn,bjgn->btjg", query_four, key_four, preferred_element_type=jnp.float32
    )
    lineage_new = (new_tree == 1)[:, :, :, None]
    decay_gap = decay_sum[:, :, None, :] - decay_sum[:, None, :, :]
    decays = jnp.where(lineage_new, jnp.exp(jnp.where(lineage_new, decay_gap, 0.0)), 0.0)
    mixing = (
        decays.reshape(reqs_dev, NODES, NODES, span_groups, span_heads)
        * intersection[..., None]
        * step_sizes.reshape(reqs_dev, 1, NODES, span_groups, span_heads)
    ).astype(jnp.bfloat16)
    values = conv_heads.reshape(reqs_dev, NODES, span_groups, span_heads, HEAD_DIM)
    inner_part = jnp.einsum(
        "btjgq,bjgqp->btgqp", mixing, values, preferred_element_type=jnp.float32
    )
    flat_width = local_heads * HEAD_DIM
    inner_flat = inner_part.reshape(reqs_dev, NODES, flat_width)
    decay_flat = jnp.repeat(jnp.exp(decay_sum), HEAD_DIM, axis=-1)
    skip_flat = jnp.repeat(skip_gain, HEAD_DIM)
    output = (
        inner_flat
        + decay_flat * carried
        + skip_flat * conv_heads.astype(jnp.float32)
    )
    gated_out = output * jax.nn.silu(gate_rows.reshape(reqs_dev, NODES, flat_width).astype(jnp.float32))
    group_power = jnp.sum(gated_out * gated_out, axis=-1)
    partner = [(d, d ^ 1) for d in range(head_count)]
    power_own = group_power + lax.ppermute(group_power, "head", partner)
    scale_factor = lax.rsqrt(power_own / (per_group * HEAD_DIM) + EPSILON)
    normed = gated_out * scale_factor[..., None] * norm_gain
    return normed.reshape(reqs_dev * NODES, flat_width).astype(jnp.bfloat16)


def solution(mesh):
    placed = (
        P(("req", "head"), None),
        P(("req", "head"), None),
        P(("req", "head"), None),
        P(("req", "head"), None),
        P("req", None, None),
        P(None, "head"),
        P("head"),
        P(),
        P(),
        P("head"),
        P("head"),
        P("head"),
        P("head"),
        P("req", "head", None, None),
        P("req", None, "head"),
        P("req", None, None),
        P("req", None, "head"),
        P("req", None, "head"),
        P("req", "head", None),
        P("req", None, None),
        P("req"),
        P(),
    )
    return jax.shard_map(
        shards, mesh=mesh, in_specs=placed, out_specs=P("req", "head"), check_vma=False
    )
```

```python
import jax
import jax.numpy as jnp
from jax import lax
from jax.sharding import PartitionSpec as P

HEADS = 256
HEAD_DIM = 64
STATE = 256
GROUPS = 8
NODES = 32
MOST = 2


EPSILON = 1e-05


def tree_conv(tree_rows, tail_rows, ancestry, weight, offset_bias):
    node_depth = jnp.sum(ancestry, axis=-1) - 1
    places = jnp.arange(3, dtype=jnp.int32)
    summed = weight[3].astype(jnp.float32) * tree_rows.astype(jnp.float32) + offset_bias
    for upward in range(1, 4):
        picked = (
            (ancestry == 1) & (node_depth[:, None, :] == node_depth[:, :, None] - upward)
        ).astype(jnp.bfloat16)
        older_rows = (places[None, None, :] == node_depth[:, :, None] - upward + 3).astype(
            jnp.bfloat16
        )
        shifted = jnp.einsum("btj,bjc->btc", picked, tree_rows, preferred_element_type=jnp.float32)
        shifted = shifted + jnp.einsum(
            "bti,bic->btc", older_rows, tail_rows, preferred_element_type=jnp.float32
        )
        summed = summed + weight[3 - upward].astype(jnp.float32) * shifted
    return jax.nn.silu(summed).astype(jnp.bfloat16)


def place_slots(payload, positions, count):
    wanted = jnp.arange(count, dtype=jnp.int32)
    owners = jnp.arange(positions.shape[0], dtype=jnp.int32)
    hits = positions[None, :] == wanted[:, None]
    chosen = jnp.sum(jnp.where(hits, owners[None, :], 0), axis=1)
    filled = jnp.any(hits, axis=1).reshape((count,) + (1,) * (payload.ndim - 1))
    taken = jnp.take(payload, chosen, axis=0)
    return jnp.where(filled, taken, jnp.zeros_like(taken))


def own_columns(rows, span_groups, dest_count, per_dest):
    lead = rows.shape[:-1]
    split = rows.reshape(lead + (2, GROUPS, STATE))
    moved = jnp.moveaxis(split, -2, 0)
    picks = (jnp.arange(dest_count, dtype=jnp.int32) // per_dest)[:, None] * span_groups + jnp.arange(
        span_groups, dtype=jnp.int32
    )[None, :]
    taken = jnp.take(moved, picks.reshape(-1), axis=0).reshape((dest_count, span_groups) + lead + (2, STATE))
    return jnp.moveaxis(taken, 1, -2).reshape((dest_count,) + lead + (2 * span_groups * STATE,))


def columns_by_dest(rows, span_groups, dest_count, per_dest):
    count = rows.shape[0]
    split = rows.reshape(count, 2, GROUPS, STATE)
    picks = (jnp.arange(dest_count, dtype=jnp.int32) // per_dest)[:, None] * span_groups + jnp.arange(
        span_groups, dtype=jnp.int32
    )[None, :]
    taken = jnp.take(split, picks.reshape(-1), axis=2).reshape(count, 2, dest_count, span_groups, STATE)
    return jnp.moveaxis(taken, 2, 1).reshape(count, dest_count, 2 * span_groups * STATE)


def shards(
    tree_heads,
    tree_gates,
    tree_steps,
    tree_groups,
    new_tree,
    kernel_heads,
    shift_heads,
    kernel_groups,
    shift_groups,
    log_rates,
    step_bias,
    skip_gain,
    norm_gain,
    old_state,
    old_heads,
    old_keys,
    old_steps,
    prior_heads,
    prior_groups,
    old_tree,
    accepted,
    new_owner,
):
    req_count = lax.axis_size("req")
    head_count = lax.axis_size("head")
    req_index = lax.axis_index("req")
    head_index = lax.axis_index("head")
    reqs_dev = new_tree.shape[0]
    local_heads = log_rates.shape[0]
    local_nodes = prior_groups.shape[1]
    per_group = HEADS // GROUPS
    span_heads = min(local_heads, per_group)
    span_groups = local_heads // span_heads
    per_dest = per_group // span_heads
    assert span_groups == 1 and per_dest == 2
    first_group = head_index * local_heads // per_group
    slot_count = req_count * MOST
    own_width = span_groups * STATE
    highest = lax.Precision.HIGHEST
    owner_table = new_owner.reshape(req_count, reqs_dev)
    target_dev = owner_table // reqs_dev
    local_ids = jnp.arange(reqs_dev, dtype=jnp.int32)
    before = local_ids[None, :, None] > local_ids[None, None, :]
    same_dest = target_dev[:, :, None] == target_dev[:, None, :]
    arrival = jnp.sum((same_dest & before).astype(jnp.int32), axis=-1)
    send_table = target_dev * MOST + arrival
    send_pos = lax.dynamic_index_in_dim(send_table, req_index, 0, keepdims=False)
    wanted_slot = req_index * reqs_dev + local_ids
    all_ids = jnp.arange(new_owner.shape[0], dtype=jnp.int32)
    match = new_owner[None, :] == wanted_slot[:, None]
    anchor = jnp.sum(jnp.where(match, all_ids[None, :], 0), axis=1)
    recv_pos = anchor // reqs_dev * MOST + jnp.take(arrival.reshape(-1), anchor)

    slot_ids = jnp.arange(slot_count, dtype=jnp.int32)
    send_hot = (send_pos[None, :] == slot_ids[:, None]).astype(jnp.bfloat16)
    recv_hot = (recv_pos[None, :] == slot_ids[:, None]).astype(jnp.bfloat16)

    def spread(hot, payload):
        return jnp.einsum(
            "pa,a...->p...", hot, payload, preferred_element_type=jnp.float32
        ).astype(jnp.bfloat16)

    def gather_back(hot, moved):
        return jnp.einsum("pa,p...->a...", hot, moved, preferred_element_type=jnp.float32)

    decay_rates = -jnp.exp(log_rates)
    node_ids = jnp.arange(NODES, dtype=jnp.int32)
    chosen_hot = node_ids[None, :] == accepted[:, None]
    chosen_row = jnp.sum(jnp.where(chosen_hot[:, :, None], old_tree, 0), axis=1)
    old_depth = jnp.sum(old_tree, axis=-1) - 1
    chosen_depth = jnp.sum(jnp.where(chosen_hot, old_depth, 0), axis=1)
    places = jnp.arange(3, dtype=jnp.int32)
    lineage = chosen_row == 1
    tail_pick = (
        lineage[:, None, :]
        & (old_depth[:, None, :] == chosen_depth[:, None, None] - 2 + places[None, :, None])
    ).astype(jnp.bfloat16)
    tail_heads = jnp.einsum(
        "bij,bjc->bic", tail_pick, prior_heads, preferred_element_type=jnp.float32
    ).astype(jnp.bfloat16)
    old_sums = jnp.einsum(
        "btj,bjh->bth", old_tree.astype(jnp.float32), old_steps * decay_rates, precision=highest
    )
    chosen_sum = jnp.sum(jnp.where(chosen_hot[:, :, None], old_sums, 0.0), axis=1)
    kept_weight = (
        jnp.where(
            lineage[:, :, None],
            jnp.exp(jnp.where(lineage[:, :, None], chosen_sum[:, None, :] - old_sums, 0.0)),
            0.0,
        )
        * old_steps
    )
    weighted = (
        (
            kept_weight[..., None]
            * old_heads.reshape(reqs_dev, NODES, local_heads, HEAD_DIM).astype(jnp.float32)
        )
        .astype(jnp.bfloat16)
        .reshape(reqs_dev, NODES, span_groups, span_heads, HEAD_DIM)
    )
    key_slice = lax.dynamic_slice_in_dim(
        old_keys, first_group * STATE, span_groups * STATE, 2
    ).reshape(reqs_dev, NODES, span_groups, STATE)
    update = jnp.einsum(
        "bjgqp,bjgn->bgqpn", weighted, key_slice, preferred_element_type=jnp.float32
    )
    carry_state = (
        jnp.exp(chosen_sum).reshape(reqs_dev, span_groups, span_heads, 1, 1)
        * old_state.reshape(reqs_dev, span_groups, span_heads, HEAD_DIM, STATE).astype(jnp.float32)
        + update
    ).astype(jnp.bfloat16)
    carry_state = lax.optimization_barrier(carry_state)
    tree_rows = tree_heads.shape[0]
    head_width = local_heads * HEAD_DIM
    widths = [2 * own_width, 2 * own_width, head_width, head_width, local_heads]
    bundle = jnp.concatenate(
        [
            columns_by_dest(tree_groups, span_groups, head_count, per_dest),
            columns_by_dest(
                prior_groups.reshape(reqs_dev * local_nodes, -1), span_groups, head_count, per_dest
            ),
            tree_heads.reshape(tree_rows, head_count, head_width),
            tree_gates.reshape(tree_rows, head_count, head_width),
            tree_steps.reshape(tree_rows, head_count, local_heads),
        ],
        axis=-1,
    )
    bundle = lax.all_to_all(bundle, "head", split_axis=1, concat_axis=0, tiled=True)
    bundle = bundle.reshape(head_count * tree_rows, -1)
    cuts = [0]
    for width in widths:
        cuts.append(cuts[-1] + width)
    pieces = [bundle[..., cuts[n] : cuts[n + 1]] for n in range(len(widths))]
    group_rows = pieces[0].reshape(reqs_dev, NODES, 2 * own_width)
    prior_flat = pieces[1]
    head_rows = pieces[2].reshape(reqs_dev, NODES, head_width)
    gate_rows = pieces[3].reshape(reqs_dev, NODES, span_groups, span_heads, HEAD_DIM)
    step_rows = pieces[4].reshape(reqs_dev, NODES, local_heads)
    pick_split = tail_pick.reshape(reqs_dev, 3, head_count, local_nodes)
    same_slot = (local_ids[:, None] == local_ids[None, :]).astype(jnp.bfloat16)
    pick_rows = (
        pick_split[:, :, :, None, :] * same_slot[:, None, None, :, None]
    ).reshape(reqs_dev * 3, head_count * reqs_dev * local_nodes)
    tail_groups = (
        jnp.dot(pick_rows, prior_flat, preferred_element_type=jnp.float32)
        .astype(jnp.bfloat16)
        .reshape(reqs_dev, 3, 2 * own_width)
    )
    new_part = jnp.concatenate([tail_heads, tail_groups], axis=-1).reshape(reqs_dev, NODES, -1)
    old_part = jnp.concatenate(
        [group_rows[..., own_width:], new_tree.astype(jnp.bfloat16)], axis=-1
    )
    new_len = new_part.shape[-1]
    old_len = old_part.shape[-1]
    exchange = jnp.concatenate(
        [spread(recv_hot, old_part), spread(send_hot, new_part)],
        axis=-1,
    )
    exchange = lax.all_to_all(exchange, "req", split_axis=0, concat_axis=0, tiled=True)
    tails_new = (
        gather_back(recv_hot, exchange[..., old_len:]).astype(jnp.bfloat16).reshape(reqs_dev, 3, -1)
    )
    rows_old = gather_back(send_hot, exchange[..., :old_len]).astype(jnp.bfloat16)
    tree_old = rows_old[..., own_width:].astype(jnp.int32)
    kernel_own = own_columns(kernel_groups, span_groups, head_count, per_dest)[head_index]
    shift_own = own_columns(shift_groups, span_groups, head_count, per_dest)[head_index]
    query_old = tree_conv(
        rows_old[..., :own_width],
        tail_groups[..., own_width:],
        tree_old,
        kernel_own[:, own_width:],
        shift_own[own_width:],
    ).reshape(reqs_dev, NODES, span_groups, STATE)
    carried_old = jnp.einsum(
        "btn,bmn->btm",
        query_old.reshape(reqs_dev, NODES, STATE),
        carry_state.reshape(reqs_dev, head_width, STATE),
        preferred_element_type=jnp.float32,
    )
    carried_moved = lax.all_to_all(
        spread(send_hot, carried_old.astype(jnp.bfloat16)), "req", split_axis=0, concat_axis=0, tiled=True
    )
    carried = jnp.einsum(
        "pa,p...->a...", recv_hot, carried_moved, preferred_element_type=jnp.bfloat16
    ).astype(jnp.float32)
    conv_heads = tree_conv(
        head_rows, tails_new[..., :head_width], new_tree, kernel_heads, shift_heads
    )
    conv_groups = tree_conv(
        group_rows, tails_new[..., head_width:], new_tree, kernel_own, shift_own
    )
    own_keys = conv_groups[..., :own_width]
    own_queries = conv_groups[..., own_width:]
    query_four = own_queries.reshape(reqs_dev, NODES, span_groups, STATE)
    key_four = own_keys.reshape(reqs_dev, NODES, span_groups, STATE)
    step_sizes = jax.nn.softplus(step_rows.astype(jnp.float32) + step_bias)
    decay_sum = jnp.einsum(
        "btj,bjh->bth", new_tree.astype(jnp.float32), step_sizes * decay_rates, precision=highest
    )
    intersection = jnp.einsum(
        "btgn,bjgn->btjg", query_four, key_four, preferred_element_type=jnp.float32
    )
    lineage_new = (new_tree == 1)[:, :, :, None]
    decay_gap = decay_sum[:, :, None, :] - decay_sum[:, None, :, :]
    decays = jnp.where(lineage_new, jnp.exp(jnp.where(lineage_new, decay_gap, 0.0)), 0.0)
    mixing = (
        decays.reshape(reqs_dev, NODES, NODES, span_groups, span_heads)
        * intersection[..., None]
        * step_sizes.reshape(reqs_dev, 1, NODES, span_groups, span_heads)
    ).astype(jnp.bfloat16)
    values = conv_heads.reshape(reqs_dev, NODES, span_groups, span_heads, HEAD_DIM)
    inner_part = jnp.einsum(
        "btjgq,bjgqp->btgqp", mixing, values, preferred_element_type=jnp.float32
    )
    flat_width = local_heads * HEAD_DIM
    inner_flat = inner_part.reshape(reqs_dev, NODES, flat_width)
    decay_flat = jnp.repeat(jnp.exp(decay_sum), HEAD_DIM, axis=-1)
    skip_flat = jnp.repeat(skip_gain, HEAD_DIM)
    output = (
        inner_flat
        + decay_flat * carried
        + skip_flat * conv_heads.astype(jnp.float32)
    )
    gated_out = output * jax.nn.silu(gate_rows.reshape(reqs_dev, NODES, flat_width).astype(jnp.float32))
    group_power = jnp.sum(gated_out * gated_out, axis=-1)
    partner = [(d, d ^ 1) for d in range(head_count)]
    power_own = group_power + lax.ppermute(group_power, "head", partner)
    scale_factor = lax.rsqrt(power_own / (per_group * HEAD_DIM) + EPSILON)
    normed = gated_out * scale_factor[..., None] * norm_gain
    return normed.reshape(reqs_dev * NODES, flat_width).astype(jnp.bfloat16)


def solution(mesh):
    placed = (
        P(("req", "head"), None),
        P(("req", "head"), None),
        P(("req", "head"), None),
        P(("req", "head"), None),
        P("req", None, None),
        P(None, "head"),
        P("head"),
        P(),
        P(),
        P("head"),
        P("head"),
        P("head"),
        P("head"),
        P("req", "head", None, None),
        P("req", None, "head"),
        P("req", None, None),
        P("req", None, "head"),
        P("req", None, "head"),
        P("req", "head", None),
        P("req", None, None),
        P("req"),
        P(),
    )
    return jax.shard_map(
        shards, mesh=mesh, in_specs=placed, out_specs=P("req", "head"), check_vma=False
    )
```

```python
import jax
import jax.numpy as jnp
from jax import lax
from jax.sharding import PartitionSpec as P

HEADS = 256
HEAD_DIM = 64
STATE = 256
GROUPS = 8
NODES = 32
MOST = 2


EPSILON = 1e-05


def tree_conv(tree_rows, tail_rows, ancestry, weight, offset_bias):
    node_depth = jnp.sum(ancestry, axis=-1) - 1
    places = jnp.arange(3, dtype=jnp.int32)
    summed = weight[3].astype(jnp.float32) * tree_rows.astype(jnp.float32) + offset_bias
    for upward in range(1, 4):
        picked = (
            (ancestry == 1) & (node_depth[:, None, :] == node_depth[:, :, None] - upward)
        ).astype(jnp.bfloat16)
        older_rows = (places[None, None, :] == node_depth[:, :, None] - upward + 3).astype(
            jnp.bfloat16
        )
        shifted = jnp.einsum("btj,bjc->btc", picked, tree_rows, preferred_element_type=jnp.float32)
        shifted = shifted + jnp.einsum(
            "bti,bic->btc", older_rows, tail_rows, preferred_element_type=jnp.float32
        )
        summed = summed + weight[3 - upward].astype(jnp.float32) * shifted
    return jax.nn.silu(summed).astype(jnp.bfloat16)


def place_slots(payload, positions, count):
    wanted = jnp.arange(count, dtype=jnp.int32)
    owners = jnp.arange(positions.shape[0], dtype=jnp.int32)
    hits = positions[None, :] == wanted[:, None]
    chosen = jnp.sum(jnp.where(hits, owners[None, :], 0), axis=1)
    filled = jnp.any(hits, axis=1).reshape((count,) + (1,) * (payload.ndim - 1))
    taken = jnp.take(payload, chosen, axis=0)
    return jnp.where(filled, taken, jnp.zeros_like(taken))


def own_columns(rows, span_groups, dest_count, per_dest):
    lead = rows.shape[:-1]
    split = rows.reshape(lead + (2, GROUPS, STATE))
    moved = jnp.moveaxis(split, -2, 0)
    picks = (jnp.arange(dest_count, dtype=jnp.int32) // per_dest)[:, None] * span_groups + jnp.arange(
        span_groups, dtype=jnp.int32
    )[None, :]
    taken = jnp.take(moved, picks.reshape(-1), axis=0).reshape((dest_count, span_groups) + lead + (2, STATE))
    return jnp.moveaxis(taken, 1, -2).reshape((dest_count,) + lead + (2 * span_groups * STATE,))


def columns_by_dest(rows, span_groups, dest_count, per_dest):
    count = rows.shape[0]
    split = rows.reshape(count, 2, GROUPS, STATE)
    picks = (jnp.arange(dest_count, dtype=jnp.int32) // per_dest)[:, None] * span_groups + jnp.arange(
        span_groups, dtype=jnp.int32
    )[None, :]
    taken = jnp.take(split, picks.reshape(-1), axis=2).reshape(count, 2, dest_count, span_groups, STATE)
    return jnp.moveaxis(taken, 2, 1).reshape(count, dest_count, 2 * span_groups * STATE)


def shards(
    tree_heads,
    tree_gates,
    tree_steps,
    tree_groups,
    new_tree,
    kernel_heads,
    shift_heads,
    kernel_groups,
    shift_groups,
    log_rates,
    step_bias,
    skip_gain,
    norm_gain,
    old_state,
    old_heads,
    old_keys,
    old_steps,
    prior_heads,
    prior_groups,
    old_tree,
    accepted,
    new_owner,
):
    req_count = lax.axis_size("req")
    head_count = lax.axis_size("head")
    req_index = lax.axis_index("req")
    head_index = lax.axis_index("head")
    reqs_dev = new_tree.shape[0]
    local_heads = log_rates.shape[0]
    local_nodes = prior_groups.shape[1]
    per_group = HEADS // GROUPS
    span_heads = min(local_heads, per_group)
    span_groups = local_heads // span_heads
    per_dest = per_group // span_heads
    assert span_groups == 1 and per_dest == 2
    first_group = head_index * local_heads // per_group
    slot_count = req_count * MOST
    own_width = span_groups * STATE
    highest = lax.Precision.HIGHEST
    owner_table = new_owner.reshape(req_count, reqs_dev)
    target_dev = owner_table // reqs_dev
    local_ids = jnp.arange(reqs_dev, dtype=jnp.int32)
    before = local_ids[None, :, None] > local_ids[None, None, :]
    same_dest = target_dev[:, :, None] == target_dev[:, None, :]
    arrival = jnp.sum((same_dest & before).astype(jnp.int32), axis=-1)
    send_table = target_dev * MOST + arrival
    send_pos = lax.dynamic_index_in_dim(send_table, req_index, 0, keepdims=False)
    wanted_slot = req_index * reqs_dev + local_ids
    all_ids = jnp.arange(new_owner.shape[0], dtype=jnp.int32)
    match = new_owner[None, :] == wanted_slot[:, None]
    anchor = jnp.sum(jnp.where(match, all_ids[None, :], 0), axis=1)
    recv_pos = anchor // reqs_dev * MOST + jnp.take(arrival.reshape(-1), anchor)

    slot_ids = jnp.arange(slot_count, dtype=jnp.int32)
    send_hot = (send_pos[None, :] == slot_ids[:, None]).astype(jnp.bfloat16)
    recv_hot = (recv_pos[None, :] == slot_ids[:, None]).astype(jnp.bfloat16)

    def spread(hot, payload):
        return jnp.einsum(
            "pa,a...->p...", hot, payload, preferred_element_type=jnp.float32
        ).astype(jnp.bfloat16)

    def gather_back(hot, moved):
        return jnp.einsum("pa,p...->a...", hot, moved, preferred_element_type=jnp.float32)

    decay_rates = -jnp.exp(log_rates)
    node_ids = jnp.arange(NODES, dtype=jnp.int32)
    chosen_hot = node_ids[None, :] == accepted[:, None]
    chosen_row = jnp.sum(jnp.where(chosen_hot[:, :, None], old_tree, 0), axis=1)
    old_depth = jnp.sum(old_tree, axis=-1) - 1
    chosen_depth = jnp.sum(jnp.where(chosen_hot, old_depth, 0), axis=1)
    places = jnp.arange(3, dtype=jnp.int32)
    lineage = chosen_row == 1
    tail_pick = (
        lineage[:, None, :]
        & (old_depth[:, None, :] == chosen_depth[:, None, None] - 2 + places[None, :, None])
    ).astype(jnp.bfloat16)
    tail_heads = jnp.einsum(
        "bij,bjc->bic", tail_pick, prior_heads, preferred_element_type=jnp.float32
    ).astype(jnp.bfloat16)
    old_sums = jnp.einsum(
        "btj,bjh->bth", old_tree.astype(jnp.float32), old_steps * decay_rates, precision=highest
    )
    chosen_sum = jnp.sum(jnp.where(chosen_hot[:, :, None], old_sums, 0.0), axis=1)
    kept_weight = (
        jnp.where(
            lineage[:, :, None],
            jnp.exp(jnp.where(lineage[:, :, None], chosen_sum[:, None, :] - old_sums, 0.0)),
            0.0,
        )
        * old_steps
    )
    weighted = (
        (
            kept_weight[..., None]
            * old_heads.reshape(reqs_dev, NODES, local_heads, HEAD_DIM).astype(jnp.float32)
        )
        .astype(jnp.bfloat16)
        .reshape(reqs_dev, NODES, span_groups, span_heads, HEAD_DIM)
    )
    key_slice = lax.dynamic_slice_in_dim(
        old_keys, first_group * STATE, span_groups * STATE, 2
    ).reshape(reqs_dev, NODES, span_groups, STATE)
    update = jnp.einsum(
        "bjgqp,bjgn->bgqpn", weighted, key_slice, preferred_element_type=jnp.float32
    )
    carry_state = (
        jnp.exp(chosen_sum).reshape(reqs_dev, span_groups, span_heads, 1, 1)
        * old_state.reshape(reqs_dev, span_groups, span_heads, HEAD_DIM, STATE).astype(jnp.float32)
        + update
    ).astype(jnp.bfloat16)
    carry_state = lax.optimization_barrier(carry_state)
    tree_rows = tree_heads.shape[0]
    head_width = local_heads * HEAD_DIM
    widths = [2 * own_width, 2 * own_width, head_width, head_width, local_heads]
    bundle = jnp.concatenate(
        [
            columns_by_dest(tree_groups, span_groups, head_count, per_dest),
            columns_by_dest(
                prior_groups.reshape(reqs_dev * local_nodes, -1), span_groups, head_count, per_dest
            ),
            tree_heads.reshape(tree_rows, head_count, head_width),
            tree_gates.reshape(tree_rows, head_count, head_width),
            tree_steps.reshape(tree_rows, head_count, local_heads),
        ],
        axis=-1,
    )
    bundle = lax.all_to_all(bundle, "head", split_axis=1, concat_axis=0, tiled=True)
    bundle = bundle.reshape(head_count * tree_rows, -1)
    cuts = [0]
    for width in widths:
        cuts.append(cuts[-1] + width)
    pieces = [bundle[..., cuts[n] : cuts[n + 1]] for n in range(len(widths))]
    group_rows = pieces[0].reshape(reqs_dev, NODES, 2 * own_width)
    prior_flat = pieces[1]
    head_rows = pieces[2].reshape(reqs_dev, NODES, head_width)
    gate_rows = pieces[3].reshape(reqs_dev, NODES, span_groups, span_heads, HEAD_DIM)
    step_rows = pieces[4].reshape(reqs_dev, NODES, local_heads)
    pick_split = tail_pick.reshape(reqs_dev, 3, head_count, local_nodes)
    same_slot = (local_ids[:, None] == local_ids[None, :]).astype(jnp.bfloat16)
    pick_rows = (
        pick_split[:, :, :, None, :] * same_slot[:, None, None, :, None]
    ).reshape(reqs_dev * 3, head_count * reqs_dev * local_nodes)
    tail_groups = (
        jnp.dot(pick_rows, prior_flat, preferred_element_type=jnp.float32)
        .astype(jnp.bfloat16)
        .reshape(reqs_dev, 3, 2 * own_width)
    )
    new_part = jnp.concatenate([tail_heads, tail_groups], axis=-1).reshape(reqs_dev, NODES, -1)
    old_part = jnp.concatenate(
        [group_rows[..., own_width:], new_tree.astype(jnp.bfloat16)], axis=-1
    )
    new_len = new_part.shape[-1]
    exchange = jnp.concatenate(
        [spread(send_hot, new_part), spread(recv_hot, old_part)],
        axis=-1,
    )
    exchange = lax.all_to_all(exchange, "req", split_axis=0, concat_axis=0, tiled=True)
    tails_new = (
        gather_back(recv_hot, exchange[..., :new_len]).astype(jnp.bfloat16).reshape(reqs_dev, 3, -1)
    )
    rows_old = gather_back(send_hot, exchange[..., new_len:]).astype(jnp.bfloat16)
    tree_old = rows_old[..., own_width:].astype(jnp.int32)
    kernel_own = own_columns(kernel_groups, span_groups, head_count, per_dest)[head_index]
    shift_own = own_columns(shift_groups, span_groups, head_count, per_dest)[head_index]
    query_old = tree_conv(
        rows_old[..., :own_width],
        tail_groups[..., own_width:],
        tree_old,
        kernel_own[:, own_width:],
        shift_own[own_width:],
    ).reshape(reqs_dev, NODES, span_groups, STATE)
    carried_old = jnp.einsum(
        "btn,bmn->btm",
        query_old.reshape(reqs_dev, NODES, STATE),
        carry_state.reshape(reqs_dev, head_width, STATE),
        preferred_element_type=jnp.float32,
    )
    carried_placed = jnp.sum(
        send_hot[:, :, None, None] * carried_old.astype(jnp.bfloat16)[None], axis=1
    )
    carried_moved = lax.all_to_all(carried_placed, "req", split_axis=0, concat_axis=0, tiled=True)
    carried = gather_back(recv_hot, carried_moved)
    conv_heads = tree_conv(
        head_rows, tails_new[..., :head_width], new_tree, kernel_heads, shift_heads
    )
    conv_groups = tree_conv(
        group_rows, tails_new[..., head_width:], new_tree, kernel_own, shift_own
    )
    own_keys = conv_groups[..., :own_width]
    own_queries = conv_groups[..., own_width:]
    query_four = own_queries.reshape(reqs_dev, NODES, span_groups, STATE)
    key_four = own_keys.reshape(reqs_dev, NODES, span_groups, STATE)
    step_sizes = jax.nn.softplus(step_rows.astype(jnp.float32) + step_bias)
    decay_sum = jnp.einsum(
        "btj,bjh->bth", new_tree.astype(jnp.float32), step_sizes * decay_rates, precision=highest
    )
    intersection = jnp.einsum(
        "btgn,bjgn->btjg", query_four, key_four, preferred_element_type=jnp.float32
    )
    lineage_new = (new_tree == 1)[:, :, :, None]
    decay_gap = decay_sum[:, :, None, :] - decay_sum[:, None, :, :]
    decays = jnp.where(lineage_new, jnp.exp(jnp.where(lineage_new, decay_gap, 0.0)), 0.0)
    mixing = (
        decays.reshape(reqs_dev, NODES, NODES, span_groups, span_heads)
        * intersection[..., None]
        * step_sizes.reshape(reqs_dev, 1, NODES, span_groups, span_heads)
    ).astype(jnp.bfloat16)
    values = conv_heads.reshape(reqs_dev, NODES, span_groups, span_heads, HEAD_DIM)
    inner_part = jnp.einsum(
        "btjgq,bjgqp->btgqp", mixing, values, preferred_element_type=jnp.float32
    )
    flat_width = local_heads * HEAD_DIM
    inner_flat = inner_part.reshape(reqs_dev, NODES, flat_width)
    decay_flat = jnp.repeat(jnp.exp(decay_sum), HEAD_DIM, axis=-1)
    skip_flat = jnp.repeat(skip_gain, HEAD_DIM)
    output = (
        inner_flat
        + decay_flat * carried
        + skip_flat * conv_heads.astype(jnp.float32)
    )
    gated_out = output * jax.nn.silu(gate_rows.reshape(reqs_dev, NODES, flat_width).astype(jnp.float32))
    group_power = jnp.sum(gated_out * gated_out, axis=-1)
    partner = [(d, d ^ 1) for d in range(head_count)]
    power_own = group_power + lax.ppermute(group_power, "head", partner)
    scale_factor = lax.rsqrt(power_own / (per_group * HEAD_DIM) + EPSILON)
    normed = gated_out * scale_factor[..., None] * norm_gain
    return normed.reshape(reqs_dev * NODES, flat_width).astype(jnp.bfloat16)


def solution(mesh):
    placed = (
        P(("req", "head"), None),
        P(("req", "head"), None),
        P(("req", "head"), None),
        P(("req", "head"), None),
        P("req", None, None),
        P(None, "head"),
        P("head"),
        P(),
        P(),
        P("head"),
        P("head"),
        P("head"),
        P("head"),
        P("req", "head", None, None),
        P("req", None, "head"),
        P("req", None, None),
        P("req", None, "head"),
        P("req", None, "head"),
        P("req", "head", None),
        P("req", None, None),
        P("req"),
        P(),
    )
    return jax.shard_map(
        shards, mesh=mesh, in_specs=placed, out_specs=P("req", "head"), check_vma=False
    )
```

```python
import jax
import jax.numpy as jnp
from jax import lax
from jax.sharding import PartitionSpec as P

HEADS = 256
HEAD_DIM = 64
STATE = 256
GROUPS = 8
NODES = 32
MOST = 2


EPSILON = 1e-05


def tree_conv(tree_rows, tail_rows, ancestry, weight, offset_bias):
    node_depth = jnp.sum(ancestry, axis=-1) - 1
    places = jnp.arange(3, dtype=jnp.int32)
    summed = weight[3].astype(jnp.float32) * tree_rows.astype(jnp.float32) + offset_bias
    for upward in range(1, 4):
        picked = (
            (ancestry == 1) & (node_depth[:, None, :] == node_depth[:, :, None] - upward)
        ).astype(jnp.bfloat16)
        older_rows = (places[None, None, :] == node_depth[:, :, None] - upward + 3).astype(
            jnp.bfloat16
        )
        shifted = jnp.einsum("btj,bjc->btc", picked, tree_rows, preferred_element_type=jnp.float32)
        shifted = shifted + jnp.einsum(
            "bti,bic->btc", older_rows, tail_rows, preferred_element_type=jnp.float32
        )
        summed = summed + weight[3 - upward].astype(jnp.float32) * shifted
    return jax.nn.silu(summed).astype(jnp.bfloat16)


def place_slots(payload, positions, count):
    wanted = jnp.arange(count, dtype=jnp.int32)
    owners = jnp.arange(positions.shape[0], dtype=jnp.int32)
    hits = positions[None, :] == wanted[:, None]
    chosen = jnp.sum(jnp.where(hits, owners[None, :], 0), axis=1)
    filled = jnp.any(hits, axis=1).reshape((count,) + (1,) * (payload.ndim - 1))
    taken = jnp.take(payload, chosen, axis=0)
    return jnp.where(filled, taken, jnp.zeros_like(taken))


def own_columns(rows, span_groups, dest_count, per_dest):
    lead = rows.shape[:-1]
    split = rows.reshape(lead + (2, GROUPS, STATE))
    moved = jnp.moveaxis(split, -2, 0)
    picks = (jnp.arange(dest_count, dtype=jnp.int32) // per_dest)[:, None] * span_groups + jnp.arange(
        span_groups, dtype=jnp.int32
    )[None, :]
    taken = jnp.take(moved, picks.reshape(-1), axis=0).reshape((dest_count, span_groups) + lead + (2, STATE))
    return jnp.moveaxis(taken, 1, -2).reshape((dest_count,) + lead + (2 * span_groups * STATE,))


def columns_by_dest(rows, span_groups, dest_count, per_dest):
    count = rows.shape[0]
    split = rows.reshape(count, 2, GROUPS, STATE)
    picks = (jnp.arange(dest_count, dtype=jnp.int32) // per_dest)[:, None] * span_groups + jnp.arange(
        span_groups, dtype=jnp.int32
    )[None, :]
    taken = jnp.take(split, picks.reshape(-1), axis=2).reshape(count, 2, dest_count, span_groups, STATE)
    return jnp.moveaxis(taken, 2, 1).reshape(count, dest_count, 2 * span_groups * STATE)


def shards(
    tree_heads,
    tree_gates,
    tree_steps,
    tree_groups,
    new_tree,
    kernel_heads,
    shift_heads,
    kernel_groups,
    shift_groups,
    log_rates,
    step_bias,
    skip_gain,
    norm_gain,
    old_state,
    old_heads,
    old_keys,
    old_steps,
    prior_heads,
    prior_groups,
    old_tree,
    accepted,
    new_owner,
):
    req_count = lax.axis_size("req")
    head_count = lax.axis_size("head")
    req_index = lax.axis_index("req")
    head_index = lax.axis_index("head")
    reqs_dev = new_tree.shape[0]
    local_heads = log_rates.shape[0]
    local_nodes = prior_groups.shape[1]
    per_group = HEADS // GROUPS
    span_heads = min(local_heads, per_group)
    span_groups = local_heads // span_heads
    per_dest = per_group // span_heads
    assert span_groups == 1 and per_dest == 2
    first_group = head_index * local_heads // per_group
    slot_count = req_count * MOST
    own_width = span_groups * STATE
    highest = lax.Precision.HIGHEST
    owner_table = new_owner.reshape(req_count, reqs_dev)
    target_dev = owner_table // reqs_dev
    local_ids = jnp.arange(reqs_dev, dtype=jnp.int32)
    before = local_ids[None, :, None] > local_ids[None, None, :]
    same_dest = target_dev[:, :, None] == target_dev[:, None, :]
    arrival = jnp.sum((same_dest & before).astype(jnp.int32), axis=-1)
    send_table = target_dev * MOST + arrival
    send_pos = lax.dynamic_index_in_dim(send_table, req_index, 0, keepdims=False)
    wanted_slot = req_index * reqs_dev + local_ids
    all_ids = jnp.arange(new_owner.shape[0], dtype=jnp.int32)
    match = new_owner[None, :] == wanted_slot[:, None]
    anchor = jnp.sum(jnp.where(match, all_ids[None, :], 0), axis=1)
    recv_pos = anchor // reqs_dev * MOST + jnp.take(arrival.reshape(-1), anchor)

    slot_ids = jnp.arange(slot_count, dtype=jnp.int32)
    send_hot = (send_pos[None, :] == slot_ids[:, None]).astype(jnp.bfloat16)
    recv_hot = (recv_pos[None, :] == slot_ids[:, None]).astype(jnp.bfloat16)

    def spread(hot, payload):
        return jnp.einsum(
            "pa,a...->p...", hot, payload, preferred_element_type=jnp.float32
        ).astype(jnp.bfloat16)

    def gather_back(hot, moved):
        return jnp.einsum("pa,p...->a...", hot, moved, preferred_element_type=jnp.float32)

    decay_rates = -jnp.exp(log_rates)
    node_ids = jnp.arange(NODES, dtype=jnp.int32)
    chosen_hot = node_ids[None, :] == accepted[:, None]
    chosen_row = jnp.sum(jnp.where(chosen_hot[:, :, None], old_tree, 0), axis=1)
    old_depth = jnp.sum(old_tree, axis=-1) - 1
    chosen_depth = jnp.sum(jnp.where(chosen_hot, old_depth, 0), axis=1)
    places = jnp.arange(3, dtype=jnp.int32)
    lineage = chosen_row == 1
    tail_pick = (
        lineage[:, None, :]
        & (old_depth[:, None, :] == chosen_depth[:, None, None] - 2 + places[None, :, None])
    ).astype(jnp.bfloat16)
    tail_heads = jnp.einsum(
        "bij,bjc->bic", tail_pick, prior_heads, preferred_element_type=jnp.float32
    ).astype(jnp.bfloat16)
    old_sums = jnp.einsum(
        "btj,bjh->bth", old_tree.astype(jnp.float32), old_steps * decay_rates, precision=highest
    )
    chosen_sum = jnp.sum(jnp.where(chosen_hot[:, :, None], old_sums, 0.0), axis=1)
    kept_weight = (
        jnp.where(
            lineage[:, :, None],
            jnp.exp(jnp.where(lineage[:, :, None], chosen_sum[:, None, :] - old_sums, 0.0)),
            0.0,
        )
        * old_steps
    )
    weighted = (
        (
            kept_weight[..., None]
            * old_heads.reshape(reqs_dev, NODES, local_heads, HEAD_DIM).astype(jnp.float32)
        )
        .astype(jnp.bfloat16)
        .reshape(reqs_dev, NODES, span_groups, span_heads, HEAD_DIM)
    )
    key_slice = lax.dynamic_slice_in_dim(
        old_keys, first_group * STATE, span_groups * STATE, 2
    ).reshape(reqs_dev, NODES, span_groups, STATE)
    update = jnp.einsum(
        "bjgqp,bjgn->bgqpn", weighted, key_slice, preferred_element_type=jnp.float32
    )
    carry_state = (
        jnp.exp(chosen_sum).reshape(reqs_dev, span_groups, span_heads, 1, 1)
        * old_state.reshape(reqs_dev, span_groups, span_heads, HEAD_DIM, STATE).astype(jnp.float32)
        + update
    ).astype(jnp.bfloat16)
    carry_state = lax.optimization_barrier(carry_state)
    tree_rows = tree_heads.shape[0]
    head_width = local_heads * HEAD_DIM
    widths = [2 * own_width, 2 * own_width, head_width, head_width, local_heads]
    bundle = jnp.concatenate(
        [
            columns_by_dest(tree_groups, span_groups, head_count, per_dest),
            columns_by_dest(
                prior_groups.reshape(reqs_dev * local_nodes, -1), span_groups, head_count, per_dest
            ),
            tree_heads.reshape(tree_rows, head_count, head_width),
            tree_gates.reshape(tree_rows, head_count, head_width),
            tree_steps.reshape(tree_rows, head_count, local_heads),
        ],
        axis=-1,
    )
    bundle = lax.all_to_all(bundle, "head", split_axis=1, concat_axis=0, tiled=True)
    bundle = bundle.reshape(head_count * tree_rows, -1)
    cuts = [0]
    for width in widths:
        cuts.append(cuts[-1] + width)
    pieces = [bundle[..., cuts[n] : cuts[n + 1]] for n in range(len(widths))]
    group_rows = pieces[0].reshape(reqs_dev, NODES, 2 * own_width)
    prior_flat = pieces[1]
    head_rows = pieces[2].reshape(reqs_dev, NODES, head_width)
    gate_rows = pieces[3].reshape(reqs_dev, NODES, span_groups, span_heads, HEAD_DIM)
    step_rows = pieces[4].reshape(reqs_dev, NODES, local_heads)
    pick_split = tail_pick.reshape(reqs_dev, 3, head_count, local_nodes)
    same_slot = (local_ids[:, None] == local_ids[None, :]).astype(jnp.bfloat16)
    pick_rows = (
        pick_split[:, :, :, None, :] * same_slot[:, None, None, :, None]
    ).reshape(reqs_dev * 3, head_count * reqs_dev * local_nodes)
    tail_groups = (
        jnp.dot(pick_rows, prior_flat, preferred_element_type=jnp.float32)
        .astype(jnp.bfloat16)
        .reshape(reqs_dev, 3, 2 * own_width)
    )
    new_part = jnp.concatenate([tail_heads, tail_groups], axis=-1).reshape(reqs_dev, NODES, -1)
    old_part = jnp.concatenate(
        [group_rows[..., own_width:], new_tree.astype(jnp.bfloat16)], axis=-1
    )
    new_len = new_part.shape[-1]
    half = NODES // 2
    old_len = old_part.shape[-1]
    exchange = jnp.concatenate(
        [
            spread(recv_hot, old_part.reshape(reqs_dev, half, 2 * old_len)),
            spread(send_hot, new_part.reshape(reqs_dev, half, 2 * new_len)),
        ],
        axis=-1,
    )
    exchange = lax.all_to_all(exchange, "req", split_axis=0, concat_axis=0, tiled=True)
    tails_new = (
        gather_back(recv_hot, exchange[..., 2 * old_len :]).astype(jnp.bfloat16).reshape(reqs_dev, 3, -1)
    )
    rows_old = (
        gather_back(send_hot, exchange[..., : 2 * old_len])
        .astype(jnp.bfloat16)
        .reshape(reqs_dev, NODES, old_len)
    )
    tree_old = rows_old[..., own_width:].astype(jnp.int32)
    kernel_own = own_columns(kernel_groups, span_groups, head_count, per_dest)[head_index]
    shift_own = own_columns(shift_groups, span_groups, head_count, per_dest)[head_index]
    query_old = tree_conv(
        rows_old[..., :own_width],
        tail_groups[..., own_width:],
        tree_old,
        kernel_own[:, own_width:],
        shift_own[own_width:],
    ).reshape(reqs_dev, NODES, span_groups, STATE)
    carried_old = jnp.einsum(
        "btn,bmn->btm",
        query_old.reshape(reqs_dev, NODES, STATE),
        carry_state.reshape(reqs_dev, head_width, STATE),
        preferred_element_type=jnp.float32,
    )
    carried_moved = lax.all_to_all(
        spread(send_hot, carried_old.astype(jnp.bfloat16)), "req", split_axis=0, concat_axis=0, tiled=True
    )
    carried = gather_back(recv_hot, carried_moved)
    conv_heads = tree_conv(
        head_rows, tails_new[..., :head_width], new_tree, kernel_heads, shift_heads
    )
    conv_groups = tree_conv(
        group_rows, tails_new[..., head_width:], new_tree, kernel_own, shift_own
    )
    own_keys = conv_groups[..., :own_width]
    own_queries = conv_groups[..., own_width:]
    query_four = own_queries.reshape(reqs_dev, NODES, span_groups, STATE)
    key_four = own_keys.reshape(reqs_dev, NODES, span_groups, STATE)
    step_sizes = jax.nn.softplus(step_rows.astype(jnp.float32) + step_bias)
    decay_sum = jnp.einsum(
        "btj,bjh->bth", new_tree.astype(jnp.float32), step_sizes * decay_rates, precision=highest
    )
    intersection = jnp.einsum(
        "btgn,bjgn->btjg", query_four, key_four, preferred_element_type=jnp.float32
    )
    lineage_new = (new_tree == 1)[:, :, :, None]
    decay_gap = decay_sum[:, :, None, :] - decay_sum[:, None, :, :]
    decays = jnp.where(lineage_new, jnp.exp(jnp.where(lineage_new, decay_gap, 0.0)), 0.0)
    mixing = (
        decays.reshape(reqs_dev, NODES, NODES, span_groups, span_heads)
        * intersection[..., None]
        * step_sizes.reshape(reqs_dev, 1, NODES, span_groups, span_heads)
    ).astype(jnp.bfloat16)
    values = conv_heads.reshape(reqs_dev, NODES, span_groups, span_heads, HEAD_DIM)
    inner_part = jnp.einsum(
        "btjgq,bjgqp->btgqp", mixing, values, preferred_element_type=jnp.float32
    )
    flat_width = local_heads * HEAD_DIM
    inner_flat = inner_part.reshape(reqs_dev, NODES, flat_width)
    decay_flat = jnp.repeat(jnp.exp(decay_sum), HEAD_DIM, axis=-1)
    skip_flat = jnp.repeat(skip_gain, HEAD_DIM)
    output = (
        inner_flat
        + decay_flat * carried
        + skip_flat * conv_heads.astype(jnp.float32)
    )
    gated_out = output * jax.nn.silu(gate_rows.reshape(reqs_dev, NODES, flat_width).astype(jnp.float32))
    group_power = jnp.sum(gated_out * gated_out, axis=-1)
    partner = [(d, d ^ 1) for d in range(head_count)]
    power_own = group_power + lax.ppermute(group_power, "head", partner)
    scale_factor = lax.rsqrt(power_own / (per_group * HEAD_DIM) + EPSILON)
    normed = gated_out * scale_factor[..., None] * norm_gain
    return normed.reshape(reqs_dev * NODES, flat_width).astype(jnp.bfloat16)


def solution(mesh):
    placed = (
        P(("req", "head"), None),
        P(("req", "head"), None),
        P(("req", "head"), None),
        P(("req", "head"), None),
        P("req", None, None),
        P(None, "head"),
        P("head"),
        P(),
        P(),
        P("head"),
        P("head"),
        P("head"),
        P("head"),
        P("req", "head", None, None),
        P("req", None, "head"),
        P("req", None, None),
        P("req", None, "head"),
        P("req", None, "head"),
        P("req", "head", None),
        P("req", None, None),
        P("req"),
        P(),
    )
    return jax.shard_map(
        shards, mesh=mesh, in_specs=placed, out_specs=P("req", "head"), check_vma=False
    )
```
